32 devices in a mesh: dp: 8 (over z, core), mp: 4 (over y, x).
Axes of the slice: x: 2, y: 2, z: 4, core: 2. Of those that a mesh axis runs over, the one named last changes fastest.
Arguments:
- tokens: bfloat16 [16, 640, 2048], P('dp', 'mp'), may hold values from -6 to 6
- lengths: int32 [16], P('dp'), may hold values from 320 to 640, as said below
- w_query: bfloat16 [2048, 2048], P(None, 'mp'), may hold values from -0.125 to 0.125
- w_key: bfloat16 [2048, 2048], P(None, 'mp'), may hold values from -0.125 to 0.125
- w_value: bfloat16 [2048, 2048], P(None, 'mp'), may hold values from -0.125 to 0.125
- b_query: float32 [16, 128], P('mp'), may hold values from -3 to 3
- b_value: float32 [16, 128], P('mp'), may hold values from -2 to 2
- w_out: bfloat16 [2048, 2048], P('mp'), may hold values from -1 to 1
- b_out: float32 [2048], replicated, may hold values from -2 to 2
- w_up: bfloat16 [2048, 8192], P(None, 'mp'), may hold values from -0.125 to 0.125
- b_up: float32 [64, 128], P('mp'), may hold values from -2 to 2
- w_down: bfloat16 [8192, 2048], P('mp'), may hold values from -0.0625 to 0.0625
- b_down: float32 [2048], replicated, may hold values from -2 to 2
- norm1_gain: float32 [2048], replicated, may hold values from 0.5 to 1.5
- norm1_shift: float32 [2048], replicated, may hold values from -1.5 to 1.5
- norm2_gain: float32 [2048], replicated, may hold values from 0.5 to 1.5
- norm2_shift: float32 [2048], replicated, may hold values from -1.5 to 1.5
- cotangent: bfloat16 [16, 640, 2048], P('dp', 'mp'), may hold values from -6 to 6
Outputs:
- output: bfloat16 [16, 640, 2048], P('dp', 'mp')
- grad_tokens: bfloat16 [16, 640, 2048], P('dp', 'mp')
- grad_w_query: float32 [2048, 2048], P('dp', 'mp')
- grad_w_key: float32 [2048, 2048], P('dp', 'mp')
- grad_w_value: float32 [2048, 2048], P('dp', 'mp')
- grad_b_query: float32 [16, 128], P('mp', 'dp')
- grad_b_value: float32 [16, 128], P('mp', 'dp')
- grad_w_out: float32 [2048, 2048], P('mp', 'dp')
- grad_b_out: float32 [2048], P(('dp', 'mp'))
- grad_w_up: float32 [2048, 8192], P('dp', 'mp')
- grad_b_up: float32 [64, 128], P('mp', 'dp')
- grad_w_down: float32 [8192, 2048], P('mp', 'dp')
- grad_b_down: float32 [2048], P(('dp', 'mp'))
- grad_norm1_gain: float32 [2048], P(('dp', 'mp'))
- grad_norm1_shift: float32 [2048], P(('dp', 'mp'))
- grad_norm2_gain: float32 [2048], P(('dp', 'mp'))
- grad_norm2_shift: float32 [2048], P(('dp', 'mp'))
The draws below stay inside these ranges and needn't reach their ends.
Inputs may be any that keep to these rules, and one draw needn't show every extreme that they name: `lengths`: each item has 320 to 640 valid slots, the first ones; some item is full.
All inputs are finite; a program needn't handle non-finite values.
Results may differ from the reference program's by a relative error of at most 0.02.
Values may be sent and summed in bfloat16 or wider, within the bound.
No kernel may reach another device: no remote copies, remote signals or barrier semaphores. Data moves between devices by JAX's collectives and lax.ppermute only.
A program may use at most 256 MiB of HBM per device.

```python
import jax
import jax.numpy as jnp
from jax import lax

D = 2048
HEADS = 16
HEAD_DIM = 128
FF = 8192
SEQ = 640
HD = 2048
ITEMS = 16


def draw_lengths(key, part):
    key_lengths, key_pick = jax.random.split(key)
    drawn = jax.random.randint(key_lengths, (ITEMS,), SEQ // 2, SEQ + 1)
    chosen = jax.random.randint(key_pick, (), 0, ITEMS)
    return jnp.where(jnp.arange(ITEMS) == chosen, SEQ, drawn).astype(jnp.int32)


def block_levels(own_key, dims, pieces, low, largest):
    def one(position, parts):
        steps = jax.random.uniform(jax.random.fold_in(jax.random.fold_in(own_key, 6), position), (parts,), jnp.float32, low / len(pieces), largest / len(pieces))
        return jnp.repeat(jnp.exp(steps), dims[position] // parts).reshape((-1,) + (1,) * (len(dims) - position - 1))

    loudness = one(*pieces[0])
    for cut in pieces[1:]:
        loudness = loudness * one(*cut)
    return loudness


def noise(key, extent, scale, bound, pieces=(), kind=jnp.bfloat16):
    level = block_levels(key, extent, pieces, -0.22, 0.18) if pieces else 1.0
    values = jax.random.normal(key, extent, jnp.float32) * scale * level
    return jnp.minimum(jnp.maximum(values, -bound), bound).astype(kind)


def setup_inputs(seed: int = 0) -> dict:
    seeds = jax.random.split(jax.random.key(seed), 19)
    return {
        "tokens": noise(seeds[0], (ITEMS, SEQ, D), 1.0, 6.0, ((0, 8), (1, 4))),
        "lengths": draw_lengths(jax.random.fold_in(seeds[18], 71), 0),
        "w_query": noise(seeds[2], (D, HD), D ** -0.5, 0.125, ((1, 4),)),
        "w_key": noise(seeds[3], (D, HD), D ** -0.5, 0.125, ((1, 4),)),
        "w_value": noise(seeds[4], (D, HD), D ** -0.5, 0.125, ((1, 4),)),
        "b_query": noise(seeds[5], (HEADS, HEAD_DIM), 0.5, 3.0, ((0, 4),), jnp.float32),
        "b_value": noise(seeds[6], (HEADS, HEAD_DIM), 0.3, 2.0, ((0, 4),), jnp.float32),
        "w_out": noise(seeds[7], (HD, D), (HD // 64) ** -0.5, 1.0, ((0, 4),)),
        "b_out": noise(seeds[8], (D,), 0.3, 2.0, (), jnp.float32),
        "w_up": noise(seeds[9], (D, FF), D ** -0.5, 0.125, ((1, 4),)),
        "b_up": noise(seeds[10], (FF // 128, 128), 0.3, 2.0, ((0, 4),), jnp.float32),
        "w_down": noise(seeds[11], (FF, D), FF ** -0.5, 0.0625, ((0, 4),)),
        "b_down": noise(seeds[12], (D,), 0.3, 2.0, (), jnp.float32),
        "norm1_gain": jnp.clip(1.0 + 0.1 * jax.random.normal(seeds[13], (D,), jnp.float32), 0.5, 1.5),
        "norm1_shift": noise(seeds[14], (D,), 0.2, 1.5, (), jnp.float32),
        "norm2_gain": jnp.clip(1.0 + 0.1 * jax.random.normal(seeds[15], (D,), jnp.float32), 0.5, 1.5),
        "norm2_shift": noise(seeds[16], (D,), 0.2, 1.5, (), jnp.float32),
        "cotangent": noise(seeds[17], (ITEMS, SEQ, D), 1.0, 6.0, ((0, 8), (1, 4))),
    }


@jax.custom_vjp
def low(v):
    return lax.optimization_barrier(v.astype(jnp.bfloat16)).astype(jnp.float32)

@jax.custom_vjp
def low_back(v):
    return v

def low_keep(v):
    return (low(v), None)

def low_pass(kept, grad):
    return (grad,)

def back_keep(v):
    return (v, None)

def back_low(kept, grad):
    return (low(grad),)
low.defvjp(low_keep, low_pass)
low_back.defvjp(back_keep, back_low)

def matmul(left, right):
    return jnp.dot(left, right, precision=lax.Precision.HIGHEST)

def layer_norm(values, gain, shift):
    centre = values - lax.optimization_barrier(jnp.mean(values, axis=-1, keepdims=True))
    spread = lax.optimization_barrier(jnp.mean(centre * centre, axis=-1, keepdims=True))
    return centre * lax.rsqrt(spread + 1e-05) * gain + shift

def block_forward(inputs, weights, length):
    w_query, w_key, w_value, b_query, b_value, w_out, b_out, w_up, b_up, w_down, b_down, gain_one, shift_one, gain_two, shift_two = weights
    seq_len = inputs.shape[0]
    normed = low(layer_norm(inputs, gain_one, shift_one))
    queries = low(low_back(matmul(normed, w_query) + b_query.reshape(-1)))
    keys_all = low(low_back(matmul(normed, w_key)))
    values_all = low(low_back(matmul(normed, w_value) + b_value.reshape(-1)))
    split = (seq_len, HEADS, HEAD_DIM)
    scores = jnp.einsum('qhd,khd->hqk', queries.reshape(split), keys_all.reshape(split), precision=lax.Precision.HIGHEST) * HEAD_DIM ** (-0.5)
    scores = low_back(scores)
    places = jnp.arange(seq_len)
    allowed = (places[None, :] <= places[:, None]) & (places[None, :] < length)
    scores = jnp.where(allowed[None], scores, -1e+30)
    probs = low(jax.nn.softmax(scores, axis=-1))
    mixed = jnp.einsum('hqk,khd->qhd', probs, values_all.reshape(split), precision=lax.Precision.HIGHEST).reshape(seq_len, HEADS * HEAD_DIM)
    mixed = low(low_back(mixed))
    middle = inputs + low_back(matmul(mixed, w_out)) + b_out
    normed_two = low(layer_norm(middle, gain_two, shift_two))
    hidden_pre = low_back(matmul(normed_two, w_up) + b_up.reshape(-1))
    hidden = low(jax.nn.gelu(hidden_pre, approximate=False))
    return middle + low_back(matmul(hidden, w_down)) + b_down

def reference(tokens, lengths, w_query, w_key, w_value, b_query, b_value, w_out, b_out, w_up, b_up, w_down, b_down, norm1_gain, norm1_shift, norm2_gain, norm2_shift, cotangent):
    weights = tuple((weight_arg.astype(jnp.float32) for weight_arg in (w_query, w_key, w_value, b_query, b_value, w_out, b_out, w_up, b_up, w_down, b_down, norm1_gain, norm1_shift, norm2_gain, norm2_shift)))

    def one_item(summed, packed):
        item_rows, item_grad, length = packed

        def forward(rows, *params):
            return block_forward(rows, params, length)
        result, backward = jax.vjp(forward, item_rows.astype(jnp.float32), *weights)
        grads = backward(item_grad.astype(jnp.float32))
        summed = tuple((before + update for before, update in zip(summed, grads[1:])))
        return (summed, (result.astype(jnp.bfloat16), grads[0].astype(jnp.bfloat16)))
    zeros = tuple((jnp.zeros_like(weight_arg) for weight_arg in weights))
    totals, (outputs, input_grads) = lax.scan(one_item, zeros, (tokens, cotangent, lengths))
    return (outputs, input_grads, totals[0], totals[1], totals[2], totals[3], totals[4], totals[5], totals[6], totals[7], totals[8], totals[9], totals[10], totals[11], totals[12], totals[13], totals[14])
```

```python
from functools import partial

import jax
import jax.numpy as jnp
from jax import lax
from jax.sharding import PartitionSpec as P

HEAD_DIM = 128


def _pairs(n, flip):
    return [(m, m ^ flip) for m in range(n)]


def gather_rows(x, axis=1):
    n = lax.axis_size("mp")
    if n != 4:
        return lax.all_gather(x, "mp", axis=axis, tiled=True)
    me = lax.axis_index("mp")
    rows = x.shape[axis]
    half = rows // 2
    from_x = lax.ppermute(x, "mp", _pairs(n, 1))
    from_y = lax.ppermute(x, "mp", _pairs(n, 2))
    diag_a = lax.ppermute(lax.slice_in_dim(from_y, 0, half, axis=axis), "mp", _pairs(n, 1))
    diag_b = lax.ppermute(lax.slice_in_dim(from_x, half, rows, axis=axis), "mp", _pairs(n, 2))
    diag = jnp.concatenate([diag_a, diag_b], axis=axis)
    shape = list(x.shape)
    shape[axis] = rows * n
    full = jnp.zeros(shape, x.dtype)
    for flip, piece in ((0, x), (1, from_x), (2, from_y), (3, diag)):
        start = [0] * x.ndim
        start[axis] = (me ^ flip) * rows
        full = lax.dynamic_update_slice(full, piece, start)
    return full


def scatter_rows(y, axis=1):
    n = lax.axis_size("mp")
    if n != 4:
        return lax.psum_scatter(
            y.astype(jnp.bfloat16), "mp", scatter_dimension=axis, tiled=True
        ).astype(jnp.float32)
    me = lax.axis_index("mp")
    rows = y.shape[axis] // n
    half = rows // 2

    def part(flip, lo, hi):
        return lax.dynamic_slice_in_dim(y, (me ^ flip) * rows + lo, hi - lo, axis=axis)

    bf16 = jnp.bfloat16
    send_x = jnp.stack([part(1, 0, half), part(3, 0, half)]).astype(bf16)
    send_y = jnp.stack([part(2, half, rows), part(3, half, rows)]).astype(bf16)
    got_x = lax.ppermute(send_x, "mp", _pairs(n, 1))
    got_y = lax.ppermute(send_y, "mp", _pairs(n, 2))
    fwd_y = (got_x[1].astype(jnp.float32) + part(2, 0, half)).astype(bf16)
    fwd_x = (got_y[1].astype(jnp.float32) + part(1, half, rows)).astype(bf16)
    last_y = lax.ppermute(fwd_y, "mp", _pairs(n, 2))
    last_x = lax.ppermute(fwd_x, "mp", _pairs(n, 1))
    low = part(0, 0, half) + got_x[0].astype(jnp.float32) + last_y.astype(jnp.float32)
    high = part(0, half, rows) + got_y[0].astype(jnp.float32) + last_x.astype(jnp.float32)
    return jnp.concatenate([low, high], axis=axis)


def layer_norm(values, gain, shift):
    centre = values - jnp.mean(values, axis=-1, keepdims=True)
    spread = jnp.mean(centre * centre, axis=-1, keepdims=True)
    return centre * lax.rsqrt(spread + 1e-05) * gain + shift


def allowed_keys(lengths, seq_len):
    places = jnp.arange(seq_len)
    causal = places[None, :] <= places[:, None]
    inside = places[None, None, :] < lengths[:, None, None]
    return (causal[None] & inside)[:, None]


def head_scores(query_heads, key_heads, allowed):
    scores = jnp.einsum(
        "iqhd,ikhd->ihqk", query_heads, key_heads, preferred_element_type=jnp.float32
    ) * HEAD_DIM ** (-0.5)
    return jnp.where(allowed, scores, -1e30)


def body(
    tokens,
    lengths,
    w_query,
    w_key,
    w_value,
    b_query,
    b_value,
    w_out,
    b_out,
    w_up,
    b_up,
    w_down,
    b_down,
    norm1_gain,
    norm1_shift,
    norm2_gain,
    norm2_shift,
    cotangent,
):
    f32 = jnp.float32
    bf16 = jnp.bfloat16
    rows_in = tokens.astype(f32)
    normed_one = layer_norm(rows_in, norm1_gain, norm1_shift).astype(bf16)
    full_one = gather_rows(normed_one)
    items, seq_len = (full_one.shape[0], full_one.shape[1])
    heads_here = w_query.shape[1] // HEAD_DIM
    split = (items, seq_len, heads_here, HEAD_DIM)

    def project(weight):
        return jnp.einsum("isd,de->ise", full_one, weight, preferred_element_type=f32)

    queries = (project(w_query) + b_query.reshape(-1)).astype(bf16)
    keys_all = project(w_key).astype(bf16)
    values_all = (project(w_value) + b_value.reshape(-1)).astype(bf16)
    query_heads = queries.reshape(split)
    key_heads = keys_all.reshape(split)
    value_heads = values_all.reshape(split)
    allowed = allowed_keys(lengths, seq_len)
    scores = head_scores(query_heads, key_heads, allowed)
    row_max = jnp.max(scores, axis=-1, keepdims=True)
    raw_weights = jnp.exp(scores - row_max)
    row_total = jnp.sum(raw_weights, axis=-1, keepdims=True)
    probs = (raw_weights / row_total).astype(bf16)
    mixed = (
        jnp.einsum("ihqk,ikhd->iqhd", probs, value_heads, preferred_element_type=f32)
        .reshape(items, seq_len, -1)
        .astype(bf16)
    )
    attn_terms = jnp.einsum("ise,ed->isd", mixed, w_out, preferred_element_type=f32)
    attn_rows = scatter_rows(attn_terms)
    middle = rows_in + attn_rows + b_out
    normed_two = layer_norm(middle, norm2_gain, norm2_shift).astype(bf16)
    full_two = gather_rows(normed_two)
    hidden_pre = jnp.einsum(
        "isd,df->isf", full_two, w_up, preferred_element_type=f32
    ) + b_up.reshape(-1)
    hidden = jax.nn.gelu(hidden_pre, approximate=False).astype(bf16)
    ffn_terms = jnp.einsum("isf,fd->isd", hidden, w_down, preferred_element_type=f32)
    ffn_rows = scatter_rows(ffn_terms)
    result = (middle + ffn_rows + b_down).astype(bf16)
    grad_out = cotangent.astype(f32)
    grad_full = gather_rows(cotangent)
    grad_w_down = jnp.einsum("isf,isd->fd", hidden, grad_full, preferred_element_type=f32)
    grad_b_down = jnp.sum(grad_out, axis=(0, 1))
    grad_hidden = jnp.einsum("isd,fd->isf", grad_full, w_down, preferred_element_type=f32)
    _, gelu_back = jax.vjp(partial(jax.nn.gelu, approximate=False), hidden_pre)
    grad_pre = gelu_back(grad_hidden)[0].astype(bf16)
    grad_w_up = jnp.einsum("isd,isf->df", full_two, grad_pre, preferred_element_type=f32)
    grad_b_up = jnp.sum(grad_pre, axis=(0, 1), dtype=f32).reshape(b_up.shape)
    back_terms = jnp.einsum("isf,df->isd", grad_pre, w_up, preferred_element_type=f32)
    back_rows = scatter_rows(back_terms)
    _, second_back = jax.vjp(layer_norm, middle, norm2_gain, norm2_shift)
    grad_mid_norm, grad_gain_two, grad_shift_two = second_back(back_rows)
    grad_middle = grad_out + grad_mid_norm
    grad_b_out = jnp.sum(grad_middle, axis=(0, 1))
    middle_full = gather_rows(grad_middle.astype(bf16))
    grad_w_out = jnp.einsum("ise,isd->ed", mixed, middle_full, preferred_element_type=f32)
    grad_mixed = (
        jnp.einsum("isd,ed->ise", middle_full, w_out, preferred_element_type=f32)
        .astype(bf16)
        .reshape(split)
    )
    again = head_scores(query_heads, key_heads, allowed)
    probs_full = jnp.exp(again - row_max) / row_total
    probs_low = probs_full.astype(bf16)
    grad_value = (
        jnp.einsum("ihqk,iqhd->ikhd", probs_low, grad_mixed, preferred_element_type=f32)
        .astype(bf16)
        .reshape(items, seq_len, -1)
    )
    grad_probs = jnp.einsum("iqhd,ikhd->ihqk", grad_mixed, value_heads, preferred_element_type=f32)
    inner = jnp.sum(probs_full * grad_probs, axis=-1, keepdims=True)
    grad_scores = (probs_full * (grad_probs - inner)).astype(bf16)
    grad_query = (
        (
            jnp.einsum("ihqk,ikhd->iqhd", grad_scores, key_heads, preferred_element_type=f32)
            * HEAD_DIM ** (-0.5)
        )
        .astype(bf16)
        .reshape(items, seq_len, -1)
    )
    grad_key = (
        (
            jnp.einsum("ihqk,iqhd->ikhd", grad_scores, query_heads, preferred_element_type=f32)
            * HEAD_DIM ** (-0.5)
        )
        .astype(bf16)
        .reshape(items, seq_len, -1)
    )

    def weight_grad(grad_cols):
        return jnp.einsum("isd,ise->de", full_one, grad_cols, preferred_element_type=f32)

    grad_w_query = weight_grad(grad_query)
    grad_w_key = weight_grad(grad_key)
    grad_w_value = weight_grad(grad_value)
    grad_b_query = jnp.sum(grad_query, axis=(0, 1), dtype=f32).reshape(b_query.shape)
    grad_b_value = jnp.sum(grad_value, axis=(0, 1), dtype=f32).reshape(b_value.shape)
    back_one = (
        jnp.einsum("ise,de->isd", grad_query, w_query, preferred_element_type=f32)
        + jnp.einsum("ise,de->isd", grad_key, w_key, preferred_element_type=f32)
        + jnp.einsum("ise,de->isd", grad_value, w_value, preferred_element_type=f32)
    )
    rows_one = scatter_rows(back_one)
    _, first_back = jax.vjp(layer_norm, rows_in, norm1_gain, norm1_shift)
    grad_in_norm, grad_gain_one, grad_shift_one = first_back(rows_one)
    grad_inputs = (grad_middle + grad_in_norm).astype(bf16)
    every_sum = (
        lax.psum_scatter(
            grad_w_query.astype(jnp.bfloat16), "dp", scatter_dimension=0, tiled=True
        ).astype(jnp.float32),
        lax.psum_scatter(
            grad_w_key.astype(jnp.bfloat16), "dp", scatter_dimension=0, tiled=True
        ).astype(jnp.float32),
        lax.psum_scatter(
            grad_w_value.astype(jnp.bfloat16), "dp", scatter_dimension=0, tiled=True
        ).astype(jnp.float32),
        lax.psum_scatter(
            grad_b_query.astype(jnp.bfloat16), "dp", scatter_dimension=1, tiled=True
        ).astype(jnp.float32),
        lax.psum_scatter(
            grad_b_value.astype(jnp.bfloat16), "dp", scatter_dimension=1, tiled=True
        ).astype(jnp.float32),
        lax.psum_scatter(
            grad_w_out.astype(jnp.bfloat16), "dp", scatter_dimension=1, tiled=True
        ).astype(jnp.float32),
        lax.psum_scatter(
            grad_w_up.astype(jnp.bfloat16), "dp", scatter_dimension=0, tiled=True
        ).astype(jnp.float32),
        lax.psum_scatter(
            grad_w_down.astype(jnp.bfloat16), "dp", scatter_dimension=1, tiled=True
        ).astype(jnp.float32),
        lax.psum_scatter(
            grad_b_up.astype(jnp.bfloat16), "dp", scatter_dimension=1, tiled=True
        ).astype(jnp.float32),
    )
    (
        sum_w_query,
        sum_w_key,
        sum_w_value,
        sum_b_query,
        sum_b_value,
        sum_w_out,
        sum_w_up,
        sum_w_down,
        sum_b_up,
    ) = every_sum
    vector_sums = (
        lax.psum_scatter(grad_b_out, ("dp", "mp"), scatter_dimension=0, tiled=True),
        lax.psum_scatter(grad_b_down, ("dp", "mp"), scatter_dimension=0, tiled=True),
        lax.psum_scatter(grad_gain_one, ("dp", "mp"), scatter_dimension=0, tiled=True),
        lax.psum_scatter(grad_shift_one, ("dp", "mp"), scatter_dimension=0, tiled=True),
        lax.psum_scatter(grad_gain_two, ("dp", "mp"), scatter_dimension=0, tiled=True),
        lax.psum_scatter(grad_shift_two, ("dp", "mp"), scatter_dimension=0, tiled=True),
    )
    sum_b_out, sum_b_down, sum_gain_one, sum_shift_one, sum_gain_two, sum_shift_two = vector_sums
    return (
        result,
        grad_inputs,
        sum_w_query,
        sum_w_key,
        sum_w_value,
        sum_b_query,
        sum_b_value,
        sum_w_out,
        sum_b_out,
        sum_w_up,
        sum_b_up,
        sum_w_down,
        sum_b_down,
        sum_gain_one,
        sum_shift_one,
        sum_gain_two,
        sum_shift_two,
    )


def solution(mesh):
    return jax.shard_map(
        body,
        mesh=mesh,
        in_specs=(
            P("dp", "mp", None),
            P("dp"),
            P(None, "mp"),
            P(None, "mp"),
            P(None, "mp"),
            P("mp", None),
            P("mp", None),
            P("mp", None),
            P(),
            P(None, "mp"),
            P("mp", None),
            P("mp", None),
            P(),
            P(),
            P(),
            P(),
            P(),
            P("dp", "mp", None),
        ),
        out_specs=(
            P("dp", "mp", None),
            P("dp", "mp", None),
            P("dp", "mp"),
            P("dp", "mp"),
            P("dp", "mp"),
            P("mp", "dp"),
            P("mp", "dp"),
            P("mp", "dp"),
            P(("dp", "mp")),
            P("dp", "mp"),
            P("mp", "dp"),
            P("mp", "dp"),
            P(("dp", "mp")),
            P(("dp", "mp")),
            P(("dp", "mp")),
            P(("dp", "mp")),
            P(("dp", "mp")),
        ),
        check_vma=False,
    )
```

```python
from functools import partial

import jax
import jax.numpy as jnp
from jax import lax
from jax.sharding import PartitionSpec as P

HEAD_DIM = 128


def _pairs(n, flip):
    return [(m, m ^ flip) for m in range(n)]


def gather_rows(x, axis=1):
    n = lax.axis_size("mp")
    if n != 4:
        return lax.all_gather(x, "mp", axis=axis, tiled=True)
    me = lax.axis_index("mp")
    rows = x.shape[axis]
    half = rows // 2
    from_x = lax.ppermute(x, "mp", _pairs(n, 1))
    from_y = lax.ppermute(x, "mp", _pairs(n, 2))
    diag_a = lax.ppermute(lax.slice_in_dim(from_y, 0, half, axis=axis), "mp", _pairs(n, 1))
    diag_b = lax.ppermute(lax.slice_in_dim(from_x, half, rows, axis=axis), "mp", _pairs(n, 2))
    diag = jnp.concatenate([diag_a, diag_b], axis=axis)
    shape = list(x.shape)
    shape[axis] = rows * n
    full = jnp.zeros(shape, x.dtype)
    for flip, piece in ((0, x), (1, from_x), (2, from_y), (3, diag)):
        start = [0] * x.ndim
        start[axis] = (me ^ flip) * rows
        full = lax.dynamic_update_slice(full, piece, start)
    return full


def scatter_rows(y, axis=1):
    n = lax.axis_size("mp")
    if n != 4:
        return lax.psum_scatter(
            y.astype(jnp.bfloat16), "mp", scatter_dimension=axis, tiled=True
        ).astype(jnp.float32)
    me = lax.axis_index("mp")
    rows = y.shape[axis] // n
    half = rows // 2

    def part(flip, lo, hi):
        return lax.dynamic_slice_in_dim(y, (me ^ flip) * rows + lo, hi - lo, axis=axis)

    bf16 = jnp.bfloat16
    send_x = jnp.stack([part(1, 0, half), part(3, 0, half)]).astype(bf16)
    send_y = jnp.stack([part(2, half, rows), part(3, half, rows)]).astype(bf16)
    got_x = lax.ppermute(send_x, "mp", _pairs(n, 1))
    got_y = lax.ppermute(send_y, "mp", _pairs(n, 2))
    fwd_y = (got_x[1].astype(jnp.float32) + part(2, 0, half)).astype(bf16)
    fwd_x = (got_y[1].astype(jnp.float32) + part(1, half, rows)).astype(bf16)
    last_y = lax.ppermute(fwd_y, "mp", _pairs(n, 2))
    last_x = lax.ppermute(fwd_x, "mp", _pairs(n, 1))
    low = part(0, 0, half) + got_x[0].astype(jnp.float32) + last_y.astype(jnp.float32)
    high = part(0, half, rows) + got_y[0].astype(jnp.float32) + last_x.astype(jnp.float32)
    return jnp.concatenate([low, high], axis=axis)


def layer_norm(values, gain, shift):
    centre = values - jnp.mean(values, axis=-1, keepdims=True)
    spread = jnp.mean(centre * centre, axis=-1, keepdims=True)
    return centre * lax.rsqrt(spread + 1e-05) * gain + shift


def allowed_keys(lengths, seq_len):
    places = jnp.arange(seq_len)
    causal = places[None, :] <= places[:, None]
    inside = places[None, None, :] < lengths[:, None, None]
    return (causal[None] & inside)[:, None]


def head_scores(query_heads, key_heads, allowed):
    scores = jnp.einsum(
        "iqhd,ikhd->ihqk", query_heads, key_heads, preferred_element_type=jnp.float32
    ) * HEAD_DIM ** (-0.5)
    return jnp.where(allowed, scores, -1e30)


def halving_scatter(values, name, dim):
    n = lax.axis_size(name)
    if n & (n - 1):
        return lax.psum_scatter(values, name, scatter_dimension=dim, tiled=True)
    me = lax.axis_index(name)
    bit = n // 2
    while bit:
        half = values.shape[dim] // 2
        upper = (me & bit) != 0
        keep = lax.dynamic_slice_in_dim(values, jnp.where(upper, half, 0), half, axis=dim)
        give = lax.dynamic_slice_in_dim(values, jnp.where(upper, 0, half), half, axis=dim)
        values = keep + lax.ppermute(give, name, _pairs(n, bit))
        bit //= 2
    return values


def forward_item(rows_in, length, p):
    f32 = jnp.float32
    bf16 = jnp.bfloat16
    normed_one = layer_norm(rows_in, p["norm1_gain"], p["norm1_shift"]).astype(bf16)
    full_one = gather_rows(normed_one)
    items, seq_len = (full_one.shape[0], full_one.shape[1])
    heads_here = p["w_query"].shape[1] // HEAD_DIM
    split = (items, seq_len, heads_here, HEAD_DIM)

    def project(weight):
        return jnp.einsum("isd,de->ise", full_one, weight, preferred_element_type=f32)

    queries = (project(p["w_query"]) + p["b_query"].reshape(-1)).astype(bf16)
    keys_all = project(p["w_key"]).astype(bf16)
    values_all = (project(p["w_value"]) + p["b_value"].reshape(-1)).astype(bf16)
    query_heads = queries.reshape(split)
    key_heads = keys_all.reshape(split)
    value_heads = values_all.reshape(split)
    allowed = allowed_keys(length, seq_len)
    scores = head_scores(query_heads, key_heads, allowed)
    row_max = jnp.max(scores, axis=-1, keepdims=True)
    raw_weights = jnp.exp(scores - row_max)
    row_total = jnp.sum(raw_weights, axis=-1, keepdims=True)
    probs = (raw_weights / row_total).astype(bf16)
    mixed = (
        jnp.einsum("ihqk,ikhd->iqhd", probs, value_heads, preferred_element_type=f32)
        .reshape(items, seq_len, -1)
        .astype(bf16)
    )
    attn_terms = jnp.einsum("ise,ed->isd", mixed, p["w_out"], preferred_element_type=f32)
    attn_rows = scatter_rows(attn_terms)
    middle = rows_in + attn_rows + p["b_out"]
    normed_two = layer_norm(middle, p["norm2_gain"], p["norm2_shift"]).astype(bf16)
    full_two = gather_rows(normed_two)
    hidden_pre = jnp.einsum(
        "isd,df->isf", full_two, p["w_up"], preferred_element_type=f32
    ) + p["b_up"].reshape(-1)
    hidden = jax.nn.gelu(hidden_pre, approximate=False).astype(bf16)
    ffn_terms = jnp.einsum("isf,fd->isd", hidden, p["w_down"], preferred_element_type=f32)
    ffn_rows = scatter_rows(ffn_terms)
    result = (middle + ffn_rows + p["b_down"]).astype(bf16)
    kept = dict(
        full_one=full_one, query_heads=query_heads, key_heads=key_heads,
        value_heads=value_heads, allowed=allowed, row_max=row_max, row_total=row_total,
        mixed=mixed, middle=middle, full_two=full_two, hidden_pre=hidden_pre, hidden=hidden,
    )
    return result, kept


def backward_item(rows_in, cotangent, k, p):
    f32 = jnp.float32
    bf16 = jnp.bfloat16
    items, seq_len = k["full_one"].shape[:2]
    heads_here = p["w_query"].shape[1] // HEAD_DIM
    split = (items, seq_len, heads_here, HEAD_DIM)
    grad_out = cotangent.astype(f32)
    grad_full = gather_rows(cotangent)
    grad_hidden = jnp.einsum("isd,fd->isf", grad_full, p["w_down"], preferred_element_type=f32)
    _, gelu_back = jax.vjp(partial(jax.nn.gelu, approximate=False), k["hidden_pre"])
    grad_pre = gelu_back(grad_hidden)[0].astype(bf16)
    back_terms = jnp.einsum("isf,df->isd", grad_pre, p["w_up"], preferred_element_type=f32)
    back_rows = scatter_rows(back_terms)
    _, second_back = jax.vjp(layer_norm, k["middle"], p["norm2_gain"], p["norm2_shift"])
    grad_mid_norm, grad_gain_two, grad_shift_two = second_back(back_rows)
    grad_middle = grad_out + grad_mid_norm
    middle_full = gather_rows(grad_middle.astype(bf16))
    grad_mixed = (
        jnp.einsum("isd,ed->ise", middle_full, p["w_out"], preferred_element_type=f32)
        .astype(bf16)
        .reshape(split)
    )
    query_heads, key_heads, value_heads = k["query_heads"], k["key_heads"], k["value_heads"]
    again = head_scores(query_heads, key_heads, k["allowed"])
    probs_full = jnp.exp(again - k["row_max"]) / k["row_total"]
    probs_low = probs_full.astype(bf16)
    grad_value = (
        jnp.einsum("ihqk,iqhd->ikhd", probs_low, grad_mixed, preferred_element_type=f32)
        .astype(bf16)
        .reshape(items, seq_len, -1)
    )
    grad_probs = jnp.einsum("iqhd,ikhd->ihqk", grad_mixed, value_heads, preferred_element_type=f32)
    inner = jnp.sum(probs_full * grad_probs, axis=-1, keepdims=True)
    grad_scores = (probs_full * (grad_probs - inner)).astype(bf16)
    grad_query = (
        (
            jnp.einsum("ihqk,ikhd->iqhd", grad_scores, key_heads, preferred_element_type=f32)
            * HEAD_DIM ** (-0.5)
        )
        .astype(bf16)
        .reshape(items, seq_len, -1)
    )
    grad_key = (
        (
            jnp.einsum("ihqk,iqhd->ikhd", grad_scores, query_heads, preferred_element_type=f32)
            * HEAD_DIM ** (-0.5)
        )
        .astype(bf16)
        .reshape(items, seq_len, -1)
    )
    back_one = (
        jnp.einsum("ise,de->isd", grad_query, p["w_query"], preferred_element_type=f32)
        + jnp.einsum("ise,de->isd", grad_key, p["w_key"], preferred_element_type=f32)
        + jnp.einsum("ise,de->isd", grad_value, p["w_value"], preferred_element_type=f32)
    )
    rows_one = scatter_rows(back_one)
    _, first_back = jax.vjp(layer_norm, rows_in, p["norm1_gain"], p["norm1_shift"])
    grad_in_norm, grad_gain_one, grad_shift_one = first_back(rows_one)
    grad_inputs = (grad_middle + grad_in_norm).astype(bf16)
    g = dict(
        grad_full=grad_full, grad_pre=grad_pre, middle_full=middle_full,
        grad_query=grad_query, grad_key=grad_key, grad_value=grad_value,
        grad_b_out=jnp.sum(grad_middle, axis=(0, 1)),
        grad_b_down=jnp.sum(grad_out, axis=(0, 1)),
        grad_gain_one=grad_gain_one, grad_shift_one=grad_shift_one,
        grad_gain_two=grad_gain_two, grad_shift_two=grad_shift_two,
    )
    return grad_inputs, g


def body(
    tokens,
    lengths,
    w_query,
    w_key,
    w_value,
    b_query,
    b_value,
    w_out,
    b_out,
    w_up,
    b_up,
    w_down,
    b_down,
    norm1_gain,
    norm1_shift,
    norm2_gain,
    norm2_shift,
    cotangent,
):
    f32 = jnp.float32
    bf16 = jnp.bfloat16
    p = dict(
        w_query=w_query, w_key=w_key, w_value=w_value, b_query=b_query, b_value=b_value,
        w_out=w_out, b_out=b_out, w_up=w_up, b_up=b_up, w_down=w_down, b_down=b_down,
        norm1_gain=norm1_gain, norm1_shift=norm1_shift,
        norm2_gain=norm2_gain, norm2_shift=norm2_shift,
    )
    count = tokens.shape[0]
    results, kept, grads, grad_ins = [], [], [], []
    for i in range(count):
        rows_in = tokens[i : i + 1].astype(f32)
        result, k = forward_item(rows_in, lengths[i : i + 1], p)
        results.append(result)
        kept.append((rows_in, k))
    for i in range(count):
        rows_in, k = kept[i]
        grad_in, g = backward_item(rows_in, cotangent[i : i + 1], k, p)
        grad_ins.append(grad_in)
        grads.append(g)

    def cat(source, key):
        return jnp.concatenate([entry[key] for entry in source], axis=0)

    hidden = cat([k for _, k in kept], "hidden")
    full_two = cat([k for _, k in kept], "full_two")
    full_one = cat([k for _, k in kept], "full_one")
    mixed = cat([k for _, k in kept], "mixed")
    grad_full = cat(grads, "grad_full")
    grad_pre = cat(grads, "grad_pre")
    middle_full = cat(grads, "middle_full")
    grad_query = cat(grads, "grad_query")
    grad_key = cat(grads, "grad_key")
    grad_value = cat(grads, "grad_value")

    def dp_sum(grad, dim):
        return lax.psum_scatter(
            grad.astype(bf16), "dp", scatter_dimension=dim, tiled=True
        ).astype(f32)

    grad_w_down = jnp.einsum("isf,isd->fd", hidden, grad_full, preferred_element_type=f32)
    sum_w_down = dp_sum(grad_w_down, 1)
    grad_w_up = jnp.einsum("isd,isf->df", full_two, grad_pre, preferred_element_type=f32)
    sum_w_up = dp_sum(grad_w_up, 0)
    grad_w_out = jnp.einsum("ise,isd->ed", mixed, middle_full, preferred_element_type=f32)
    sum_w_out = dp_sum(grad_w_out, 1)
    grad_qkv = jnp.einsum(
        "isd,ise->de",
        full_one,
        jnp.concatenate([grad_query, grad_key, grad_value], axis=-1),
        preferred_element_type=f32,
    )
    sum_qkv = dp_sum(grad_qkv, 0)
    width = w_query.shape[1]
    sum_w_query = sum_qkv[:, :width]
    sum_w_key = sum_qkv[:, width : 2 * width]
    sum_w_value = sum_qkv[:, 2 * width :]

    grad_b_up = jnp.sum(grad_pre, axis=(0, 1), dtype=f32).reshape(b_up.shape)
    grad_b_query = jnp.sum(grad_query, axis=(0, 1), dtype=f32).reshape(b_query.shape)
    grad_b_value = jnp.sum(grad_value, axis=(0, 1), dtype=f32).reshape(b_value.shape)
    sum_b_up = halving_scatter(grad_b_up, "dp", 1)
    sum_b_query = halving_scatter(grad_b_query, "dp", 1)
    sum_b_value = halving_scatter(grad_b_value, "dp", 1)

    names = ["grad_b_out", "grad_b_down", "grad_gain_one", "grad_shift_one", "grad_gain_two", "grad_shift_two"]
    vectors = jnp.stack([sum(g[key] for g in grads) for key in names])
    vectors = halving_scatter(halving_scatter(vectors, "dp", 1), "mp", 1)
    sum_b_out, sum_b_down, sum_gain_one, sum_shift_one, sum_gain_two, sum_shift_two = (
        vectors[j] for j in range(len(names))
    )
    return (
        jnp.concatenate(results, axis=0),
        jnp.concatenate(grad_ins, axis=0),
        sum_w_query,
        sum_w_key,
        sum_w_value,
        sum_b_query,
        sum_b_value,
        sum_w_out,
        sum_b_out,
        sum_w_up,
        sum_b_up,
        sum_w_down,
        sum_b_down,
        sum_gain_one,
        sum_shift_one,
        sum_gain_two,
        sum_shift_two,
    )


def solution(mesh):
    return jax.shard_map(
        body,
        mesh=mesh,
        in_specs=(
            P("dp", "mp", None),
            P("dp"),
            P(None, "mp"),
            P(None, "mp"),
            P(None, "mp"),
            P("mp", None),
            P("mp", None),
            P("mp", None),
            P(),
            P(None, "mp"),
            P("mp", None),
            P("mp", None),
            P(),
            P(),
            P(),
            P(),
            P(),
            P("dp", "mp", None),
        ),
        out_specs=(
            P("dp", "mp", None),
            P("dp", "mp", None),
            P("dp", "mp"),
            P("dp", "mp"),
            P("dp", "mp"),
            P("mp", "dp"),
            P("mp", "dp"),
            P("mp", "dp"),
            P(("dp", "mp")),
            P("dp", "mp"),
            P("mp", "dp"),
            P("mp", "dp"),
            P(("dp", "mp")),
            P(("dp", "mp")),
            P(("dp", "mp")),
            P(("dp", "mp")),
            P(("dp", "mp")),
        ),
        check_vma=False,
    )
```

```python
from functools import partial

import jax
import jax.numpy as jnp
from jax import lax
from jax.sharding import PartitionSpec as P

HEAD_DIM = 128


def _pairs(n, flip):
    return [(m, m ^ flip) for m in range(n)]


def gather_rows(x, axis=1):
    n = lax.axis_size("mp")
    if n != 4:
        return lax.all_gather(x, "mp", axis=axis, tiled=True)
    me = lax.axis_index("mp")
    rows = x.shape[axis]
    half = rows // 2
    from_x = lax.ppermute(x, "mp", _pairs(n, 1))
    from_y = lax.ppermute(x, "mp", _pairs(n, 2))
    diag_a = lax.ppermute(lax.slice_in_dim(from_y, 0, half, axis=axis), "mp", _pairs(n, 1))
    diag_b = lax.ppermute(lax.slice_in_dim(from_x, half, rows, axis=axis), "mp", _pairs(n, 2))
    diag = jnp.concatenate([diag_a, diag_b], axis=axis)
    odd_x = (me & 1) != 0
    odd_y = (me & 2) != 0
    own_row = jnp.where(
        odd_x,
        jnp.concatenate([from_x, x], axis=axis),
        jnp.concatenate([x, from_x], axis=axis),
    )
    other_row = jnp.where(
        odd_x,
        jnp.concatenate([diag, from_y], axis=axis),
        jnp.concatenate([from_y, diag], axis=axis),
    )
    return jnp.where(
        odd_y,
        jnp.concatenate([other_row, own_row], axis=axis),
        jnp.concatenate([own_row, other_row], axis=axis),
    )


def scatter_rows(y, axis=1):
    n = lax.axis_size("mp")
    if n != 4:
        return lax.psum_scatter(
            y.astype(jnp.bfloat16), "mp", scatter_dimension=axis, tiled=True
        ).astype(jnp.float32)
    me = lax.axis_index("mp")
    rows = y.shape[axis] // n
    half = rows // 2

    def part(flip, lo, hi):
        return lax.dynamic_slice_in_dim(y, (me ^ flip) * rows + lo, hi - lo, axis=axis)

    bf16 = jnp.bfloat16
    send_x = jnp.stack([part(1, 0, half), part(3, 0, half)]).astype(bf16)
    send_y = jnp.stack([part(2, half, rows), part(3, half, rows)]).astype(bf16)
    got_x = lax.ppermute(send_x, "mp", _pairs(n, 1))
    got_y = lax.ppermute(send_y, "mp", _pairs(n, 2))
    fwd_y = (got_x[1].astype(jnp.float32) + part(2, 0, half)).astype(bf16)
    fwd_x = (got_y[1].astype(jnp.float32) + part(1, half, rows)).astype(bf16)
    last_y = lax.ppermute(fwd_y, "mp", _pairs(n, 2))
    last_x = lax.ppermute(fwd_x, "mp", _pairs(n, 1))
    low = part(0, 0, half) + got_x[0].astype(jnp.float32) + last_y.astype(jnp.float32)
    high = part(0, half, rows) + got_y[0].astype(jnp.float32) + last_x.astype(jnp.float32)
    return jnp.concatenate([low, high], axis=axis)


def layer_norm(values, gain, shift):
    centre = values - jnp.mean(values, axis=-1, keepdims=True)
    spread = jnp.mean(centre * centre, axis=-1, keepdims=True)
    return centre * lax.rsqrt(spread + 1e-05) * gain + shift


def allowed_keys(lengths, seq_len):
    places = jnp.arange(seq_len)
    causal = places[None, :] <= places[:, None]
    inside = places[None, None, :] < lengths[:, None, None]
    return (causal[None] & inside)[:, None]


def head_scores(query_heads, key_heads, allowed):
    scores = jnp.einsum(
        "iqhd,ikhd->ihqk", query_heads, key_heads, preferred_element_type=jnp.float32
    ) * HEAD_DIM ** (-0.5)
    return jnp.where(allowed, scores, -1e30)


def halving_scatter(values, name, dim):
    n = lax.axis_size(name)
    if n & (n - 1):
        return lax.psum_scatter(values, name, scatter_dimension=dim, tiled=True)
    me = lax.axis_index(name)
    bit = n // 2
    while bit:
        half = values.shape[dim] // 2
        upper = (me & bit) != 0
        keep = lax.dynamic_slice_in_dim(values, jnp.where(upper, half, 0), half, axis=dim)
        give = lax.dynamic_slice_in_dim(values, jnp.where(upper, 0, half), half, axis=dim)
        values = keep + lax.ppermute(give, name, _pairs(n, bit))
        bit //= 2
    return values


def forward_item(rows_in, length, p):
    f32 = jnp.float32
    bf16 = jnp.bfloat16
    normed_one = layer_norm(rows_in, p["norm1_gain"], p["norm1_shift"]).astype(bf16)
    full_one = gather_rows(normed_one)
    items, seq_len = (full_one.shape[0], full_one.shape[1])
    heads_here = p["w_query"].shape[1] // HEAD_DIM
    split = (items, seq_len, heads_here, HEAD_DIM)

    def project(weight):
        return jnp.einsum("isd,de->ise", full_one, weight, preferred_element_type=f32)

    queries = (project(p["w_query"]) + p["b_query"].reshape(-1)).astype(bf16)
    keys_all = project(p["w_key"]).astype(bf16)
    values_all = (project(p["w_value"]) + p["b_value"].reshape(-1)).astype(bf16)
    query_heads = queries.reshape(split)
    key_heads = keys_all.reshape(split)
    value_heads = values_all.reshape(split)
    allowed = allowed_keys(length, seq_len)
    scores = head_scores(query_heads, key_heads, allowed)
    row_max = jnp.max(scores, axis=-1, keepdims=True)
    raw_weights = jnp.exp(scores - row_max)
    row_total = jnp.sum(raw_weights, axis=-1, keepdims=True)
    probs = (raw_weights / row_total).astype(bf16)
    mixed = (
        jnp.einsum("ihqk,ikhd->iqhd", probs, value_heads, preferred_element_type=f32)
        .reshape(items, seq_len, -1)
        .astype(bf16)
    )
    attn_terms = jnp.einsum("ise,ed->isd", mixed, p["w_out"], preferred_element_type=f32)
    attn_rows = scatter_rows(attn_terms)
    middle = rows_in + attn_rows + p["b_out"]
    normed_two = layer_norm(middle, p["norm2_gain"], p["norm2_shift"]).astype(bf16)
    full_two = gather_rows(normed_two)
    hidden_pre = jnp.einsum(
        "isd,df->isf", full_two, p["w_up"], preferred_element_type=f32
    ) + p["b_up"].reshape(-1)
    hidden = jax.nn.gelu(hidden_pre, approximate=False).astype(bf16)
    ffn_terms = jnp.einsum("isf,fd->isd", hidden, p["w_down"], preferred_element_type=f32)
    ffn_rows = scatter_rows(ffn_terms)
    result = (middle + ffn_rows + p["b_down"]).astype(bf16)
    kept = dict(
        full_one=full_one, query_heads=query_heads, key_heads=key_heads,
        value_heads=value_heads, allowed=allowed, row_max=row_max, row_total=row_total,
        mixed=mixed, middle=middle, full_two=full_two, hidden_pre=hidden_pre, hidden=hidden,
    )
    return result, kept


def backward_ffn(cotangent, k, p):
    f32 = jnp.float32
    bf16 = jnp.bfloat16
    grad_full = gather_rows(cotangent)
    grad_hidden = jnp.einsum("isd,fd->isf", grad_full, p["w_down"], preferred_element_type=f32)
    _, gelu_back = jax.vjp(partial(jax.nn.gelu, approximate=False), k["hidden_pre"])
    grad_pre = gelu_back(grad_hidden)[0].astype(bf16)
    back_terms = jnp.einsum("isf,df->isd", grad_pre, p["w_up"], preferred_element_type=f32)
    return grad_full, grad_pre, back_terms


def backward_mid(cotangent, back_rows, k, p):
    grad_out = cotangent.astype(jnp.float32)
    _, second_back = jax.vjp(layer_norm, k["middle"], p["norm2_gain"], p["norm2_shift"])
    grad_mid_norm, grad_gain_two, grad_shift_two = second_back(back_rows)
    grad_middle = grad_out + grad_mid_norm
    middle_full = gather_rows(grad_middle.astype(jnp.bfloat16))
    g = dict(
        grad_b_out=jnp.sum(grad_middle, axis=(0, 1)),
        grad_b_down=jnp.sum(grad_out, axis=(0, 1)),
        grad_gain_two=grad_gain_two, grad_shift_two=grad_shift_two,
    )
    return grad_middle, middle_full, g


def backward_attn(rows_in, grad_middle, middle_full, k, p):
    f32 = jnp.float32
    bf16 = jnp.bfloat16
    items, seq_len = k["full_one"].shape[:2]
    heads_here = p["w_query"].shape[1] // HEAD_DIM
    split = (items, seq_len, heads_here, HEAD_DIM)
    grad_mixed = (
        jnp.einsum("isd,ed->ise", middle_full, p["w_out"], preferred_element_type=f32)
        .astype(bf16)
        .reshape(split)
    )
    query_heads, key_heads, value_heads = k["query_heads"], k["key_heads"], k["value_heads"]
    again = head_scores(query_heads, key_heads, k["allowed"])
    probs_full = jnp.exp(again - k["row_max"]) / k["row_total"]
    probs_low = probs_full.astype(bf16)
    grad_value = (
        jnp.einsum("ihqk,iqhd->ikhd", probs_low, grad_mixed, preferred_element_type=f32)
        .astype(bf16)
        .reshape(items, seq_len, -1)
    )
    grad_probs = jnp.einsum("iqhd,ikhd->ihqk", grad_mixed, value_heads, preferred_element_type=f32)
    inner = jnp.sum(probs_full * grad_probs, axis=-1, keepdims=True)
    grad_scores = (probs_full * (grad_probs - inner)).astype(bf16)
    grad_query = (
        (
            jnp.einsum("ihqk,ikhd->iqhd", grad_scores, key_heads, preferred_element_type=f32)
            * HEAD_DIM ** (-0.5)
        )
        .astype(bf16)
        .reshape(items, seq_len, -1)
    )
    grad_key = (
        (
            jnp.einsum("ihqk,iqhd->ikhd", grad_scores, query_heads, preferred_element_type=f32)
            * HEAD_DIM ** (-0.5)
        )
        .astype(bf16)
        .reshape(items, seq_len, -1)
    )
    back_one = (
        jnp.einsum("ise,de->isd", grad_query, p["w_query"], preferred_element_type=f32)
        + jnp.einsum("ise,de->isd", grad_key, p["w_key"], preferred_element_type=f32)
        + jnp.einsum("ise,de->isd", grad_value, p["w_value"], preferred_element_type=f32)
    )
    rows_one = scatter_rows(back_one)
    _, first_back = jax.vjp(layer_norm, rows_in, p["norm1_gain"], p["norm1_shift"])
    grad_in_norm, grad_gain_one, grad_shift_one = first_back(rows_one)
    grad_inputs = (grad_middle + grad_in_norm).astype(bf16)
    g = dict(
        grad_query=grad_query, grad_key=grad_key, grad_value=grad_value,
        grad_gain_one=grad_gain_one, grad_shift_one=grad_shift_one,
    )
    return grad_inputs, g


def body(
    tokens,
    lengths,
    w_query,
    w_key,
    w_value,
    b_query,
    b_value,
    w_out,
    b_out,
    w_up,
    b_up,
    w_down,
    b_down,
    norm1_gain,
    norm1_shift,
    norm2_gain,
    norm2_shift,
    cotangent,
):
    f32 = jnp.float32
    bf16 = jnp.bfloat16
    p = dict(
        w_query=w_query, w_key=w_key, w_value=w_value, b_query=b_query, b_value=b_value,
        w_out=w_out, b_out=b_out, w_up=w_up, b_up=b_up, w_down=w_down, b_down=b_down,
        norm1_gain=norm1_gain, norm1_shift=norm1_shift,
        norm2_gain=norm2_gain, norm2_shift=norm2_shift,
    )
    count = tokens.shape[0]
    results, kept = [], []
    for i in range(count):
        rows_in = tokens[i : i + 1].astype(f32)
        result, k = forward_item(rows_in, lengths[i : i + 1], p)
        results.append(result)
        kept.append((rows_in, k))
    ks = [k for _, k in kept]
    cots = [cotangent[i : i + 1] for i in range(count)]

    def cat(parts):
        return jnp.concatenate(parts, axis=0)

    def dp_sum(grad, dim):
        return lax.psum_scatter(
            grad.astype(bf16), "dp", scatter_dimension=dim, tiled=True
        ).astype(f32)

    ffn = [backward_ffn(cots[i], ks[i], p) for i in range(count)]
    grad_full = cat([f[0] for f in ffn])
    grad_pre = cat([f[1] for f in ffn])
    grad_w_down = jnp.einsum(
        "isf,isd->fd", cat([k["hidden"] for k in ks]), grad_full, preferred_element_type=f32
    )
    grad_w_up = jnp.einsum(
        "isd,isf->df", cat([k["full_two"] for k in ks]), grad_pre, preferred_element_type=f32
    )
    back_rows = [scatter_rows(f[2]) for f in ffn]
    grad_w_down, grad_w_up, back_rows = lax.optimization_barrier((grad_w_down, grad_w_up, back_rows))
    sum_w_down = dp_sum(grad_w_down, 1)
    sum_w_up = dp_sum(grad_w_up, 0)

    mids = [backward_mid(cots[i], back_rows[i], ks[i], p) for i in range(count)]
    middle_fulls = [m[1] for m in mids]
    attn = [
        backward_attn(kept[i][0], mids[i][0], middle_fulls[i], ks[i], p) for i in range(count)
    ]
    grad_ins = [a[0] for a in attn]
    grads = [dict(mids[i][2], **attn[i][1]) for i in range(count)]
    grad_query = cat([g["grad_query"] for g in grads])
    grad_key = cat([g["grad_key"] for g in grads])
    grad_value = cat([g["grad_value"] for g in grads])
    sum_w_down, sum_w_up, grad_query, grad_key, grad_value = lax.optimization_barrier(
        (sum_w_down, sum_w_up, grad_query, grad_key, grad_value)
    )
    grad_qkv = jnp.einsum(
        "isd,ise->de",
        cat([k["full_one"] for k in ks]),
        jnp.concatenate([grad_query, grad_key, grad_value], axis=-1),
        preferred_element_type=f32,
    )
    grad_out_t = jnp.einsum(
        "isd,ise->de",
        cat(middle_fulls),
        cat([k["mixed"] for k in ks]),
        preferred_element_type=f32,
    )
    summed = dp_sum(jnp.concatenate([grad_qkv, grad_out_t], axis=1), 0)
    width = w_query.shape[1]
    sum_w_query = summed[:, :width]
    sum_w_key = summed[:, width : 2 * width]
    sum_w_value = summed[:, 2 * width : 3 * width]
    sum_w_out = summed[:, 3 * width :].T

    grad_b_up = jnp.sum(grad_pre, axis=(0, 1), dtype=f32).reshape(b_up.shape)
    grad_b_query = jnp.sum(grad_query, axis=(0, 1), dtype=f32).reshape(b_query.shape)
    grad_b_value = jnp.sum(grad_value, axis=(0, 1), dtype=f32).reshape(b_value.shape)
    sum_b_up = halving_scatter(grad_b_up, "dp", 1)
    sum_b_query = halving_scatter(grad_b_query, "dp", 1)
    sum_b_value = halving_scatter(grad_b_value, "dp", 1)

    names = ["grad_b_out", "grad_b_down", "grad_gain_one", "grad_shift_one", "grad_gain_two", "grad_shift_two"]
    vectors = jnp.stack([sum(g[key] for g in grads) for key in names])
    vectors = halving_scatter(halving_scatter(vectors, "dp", 1), "mp", 1)
    sum_b_out, sum_b_down, sum_gain_one, sum_shift_one, sum_gain_two, sum_shift_two = (
        vectors[j] for j in range(len(names))
    )
    return (
        jnp.concatenate(results, axis=0),
        jnp.concatenate(grad_ins, axis=0),
        sum_w_query,
        sum_w_key,
        sum_w_value,
        sum_b_query,
        sum_b_value,
        sum_w_out,
        sum_b_out,
        sum_w_up,
        sum_b_up,
        sum_w_down,
        sum_b_down,
        sum_gain_one,
        sum_shift_one,
        sum_gain_two,
        sum_shift_two,
    )


def solution(mesh):
    return jax.shard_map(
        body,
        mesh=mesh,
        in_specs=(
            P("dp", "mp", None),
            P("dp"),
            P(None, "mp"),
            P(None, "mp"),
            P(None, "mp"),
            P("mp", None),
            P("mp", None),
            P("mp", None),
            P(),
            P(None, "mp"),
            P("mp", None),
            P("mp", None),
            P(),
            P(),
            P(),
            P(),
            P(),
            P("dp", "mp", None),
        ),
        out_specs=(
            P("dp", "mp", None),
            P("dp", "mp", None),
            P("dp", "mp"),
            P("dp", "mp"),
            P("dp", "mp"),
            P("mp", "dp"),
            P("mp", "dp"),
            P("mp", "dp"),
            P(("dp", "mp")),
            P("dp", "mp"),
            P("mp", "dp"),
            P("mp", "dp"),
            P(("dp", "mp")),
            P(("dp", "mp")),
            P(("dp", "mp")),
            P(("dp", "mp")),
            P(("dp", "mp")),
        ),
        check_vma=False,
    )
```

```python
from functools import partial

import jax
import jax.numpy as jnp
from jax import lax
from jax.sharding import PartitionSpec as P

HEAD_DIM = 128


def _pairs(n, flip):
    return [(m, m ^ flip) for m in range(n)]


def gather_rows(x, axis=1):
    n = lax.axis_size("mp")
    if n != 4:
        return lax.all_gather(x, "mp", axis=axis, tiled=True)
    me = lax.axis_index("mp")
    rows = x.shape[axis]
    half = rows // 2
    from_x = lax.ppermute(x, "mp", _pairs(n, 1))
    from_y = lax.ppermute(x, "mp", _pairs(n, 2))
    diag_a = lax.ppermute(lax.slice_in_dim(from_y, 0, half, axis=axis), "mp", _pairs(n, 1))
    diag_b = lax.ppermute(lax.slice_in_dim(from_x, half, rows, axis=axis), "mp", _pairs(n, 2))
    diag = jnp.concatenate([diag_a, diag_b], axis=axis)
    odd_x = (me & 1) != 0
    odd_y = (me & 2) != 0
    own_row = jnp.where(
        odd_x,
        jnp.concatenate([from_x, x], axis=axis),
        jnp.concatenate([x, from_x], axis=axis),
    )
    other_row = jnp.where(
        odd_x,
        jnp.concatenate([diag, from_y], axis=axis),
        jnp.concatenate([from_y, diag], axis=axis),
    )
    return jnp.where(
        odd_y,
        jnp.concatenate([other_row, own_row], axis=axis),
        jnp.concatenate([own_row, other_row], axis=axis),
    )


def scatter_rows(y, axis=1):
    n = lax.axis_size("mp")
    if n != 4:
        return lax.psum_scatter(
            y.astype(jnp.bfloat16), "mp", scatter_dimension=axis, tiled=True
        ).astype(jnp.float32)
    me = lax.axis_index("mp")
    rows = y.shape[axis] // n
    half = rows // 2

    def part(flip, lo, hi):
        return lax.dynamic_slice_in_dim(y, (me ^ flip) * rows + lo, hi - lo, axis=axis)

    bf16 = jnp.bfloat16
    send_x = jnp.stack([part(1, 0, half), part(3, 0, half)]).astype(bf16)
    send_y = jnp.stack([part(2, half, rows), part(3, half, rows)]).astype(bf16)
    got_x = lax.ppermute(send_x, "mp", _pairs(n, 1))
    got_y = lax.ppermute(send_y, "mp", _pairs(n, 2))
    fwd_y = (got_x[1].astype(jnp.float32) + part(2, 0, half)).astype(bf16)
    fwd_x = (got_y[1].astype(jnp.float32) + part(1, half, rows)).astype(bf16)
    last_y = lax.ppermute(fwd_y, "mp", _pairs(n, 2))
    last_x = lax.ppermute(fwd_x, "mp", _pairs(n, 1))
    low = part(0, 0, half) + got_x[0].astype(jnp.float32) + last_y.astype(jnp.float32)
    high = part(0, half, rows) + got_y[0].astype(jnp.float32) + last_x.astype(jnp.float32)
    return jnp.concatenate([low, high], axis=axis)


def layer_norm(values, gain, shift):
    centre = values - jnp.mean(values, axis=-1, keepdims=True)
    spread = jnp.mean(centre * centre, axis=-1, keepdims=True)
    return centre * lax.rsqrt(spread + 1e-05) * gain + shift


def allowed_keys(lengths, seq_len):
    places = jnp.arange(seq_len)
    causal = places[None, :] <= places[:, None]
    inside = places[None, None, :] < lengths[:, None, None]
    return (causal[None] & inside)[:, None]


def head_scores(query_heads, key_heads, allowed):
    scores = jnp.einsum(
        "iqhd,ikhd->ihqk", query_heads, key_heads, preferred_element_type=jnp.float32
    ) * HEAD_DIM ** (-0.5)
    return jnp.where(allowed, scores, -1e30)


def halving_scatter(values, name, dim):
    n = lax.axis_size(name)
    if n & (n - 1):
        return lax.psum_scatter(values, name, scatter_dimension=dim, tiled=True)
    me = lax.axis_index(name)
    bit = n // 2
    while bit:
        half = values.shape[dim] // 2
        upper = (me & bit) != 0
        keep = lax.dynamic_slice_in_dim(values, jnp.where(upper, half, 0), half, axis=dim)
        give = lax.dynamic_slice_in_dim(values, jnp.where(upper, 0, half), half, axis=dim)
        values = keep + lax.ppermute(give, name, _pairs(n, bit))
        bit //= 2
    return values


class LinkChain:
    def __init__(self):
        self.last = None

    def run(self, exchange, x, store, key, extra=None):
        if self.last is not None:
            held, slot = self.last
            held[slot], x, extra = lax.optimization_barrier((held[slot], x, extra))
        store[key] = exchange(x)
        self.last = (store, key)
        return extra


def attention_forward(full_one, length, p):
    f32 = jnp.float32
    bf16 = jnp.bfloat16
    items, seq_len = (full_one.shape[0], full_one.shape[1])
    heads_here = p["w_query"].shape[1] // HEAD_DIM
    split = (items, seq_len, heads_here, HEAD_DIM)

    def project(weight):
        return jnp.einsum("isd,de->ise", full_one, weight, preferred_element_type=f32)

    queries = (project(p["w_query"]) + p["b_query"].reshape(-1)).astype(bf16)
    keys_all = project(p["w_key"]).astype(bf16)
    values_all = (project(p["w_value"]) + p["b_value"].reshape(-1)).astype(bf16)
    query_heads = queries.reshape(split)
    key_heads = keys_all.reshape(split)
    value_heads = values_all.reshape(split)
    allowed = allowed_keys(length, seq_len)
    scores = head_scores(query_heads, key_heads, allowed)
    row_max = jnp.max(scores, axis=-1, keepdims=True)
    raw_weights = jnp.exp(scores - row_max)
    row_total = jnp.sum(raw_weights, axis=-1, keepdims=True)
    probs = (raw_weights / row_total).astype(bf16)
    mixed = (
        jnp.einsum("ihqk,ikhd->iqhd", probs, value_heads, preferred_element_type=f32)
        .reshape(items, seq_len, -1)
        .astype(bf16)
    )
    attn_terms = jnp.einsum("ise,ed->isd", mixed, p["w_out"], preferred_element_type=f32)
    kept = dict(
        query_heads=query_heads, key_heads=key_heads, value_heads=value_heads,
        allowed=allowed, row_max=row_max, row_total=row_total, mixed=mixed,
    )
    return attn_terms, kept


def attention_backward(middle_full, k, p):
    f32 = jnp.float32
    bf16 = jnp.bfloat16
    items, seq_len = middle_full.shape[:2]
    heads_here = p["w_query"].shape[1] // HEAD_DIM
    split = (items, seq_len, heads_here, HEAD_DIM)
    grad_mixed = (
        jnp.einsum("isd,ed->ise", middle_full, p["w_out"], preferred_element_type=f32)
        .astype(bf16)
        .reshape(split)
    )
    query_heads, key_heads, value_heads = k["query_heads"], k["key_heads"], k["value_heads"]
    again = head_scores(query_heads, key_heads, k["allowed"])
    probs_full = jnp.exp(again - k["row_max"]) / k["row_total"]
    probs_low = probs_full.astype(bf16)
    grad_value = (
        jnp.einsum("ihqk,iqhd->ikhd", probs_low, grad_mixed, preferred_element_type=f32)
        .astype(bf16)
        .reshape(items, seq_len, -1)
    )
    grad_probs = jnp.einsum("iqhd,ikhd->ihqk", grad_mixed, value_heads, preferred_element_type=f32)
    inner = jnp.sum(probs_full * grad_probs, axis=-1, keepdims=True)
    grad_scores = (probs_full * (grad_probs - inner)).astype(bf16)
    grad_query = (
        (
            jnp.einsum("ihqk,ikhd->iqhd", grad_scores, key_heads, preferred_element_type=f32)
            * HEAD_DIM ** (-0.5)
        )
        .astype(bf16)
        .reshape(items, seq_len, -1)
    )
    grad_key = (
        (
            jnp.einsum("ihqk,iqhd->ikhd", grad_scores, query_heads, preferred_element_type=f32)
            * HEAD_DIM ** (-0.5)
        )
        .astype(bf16)
        .reshape(items, seq_len, -1)
    )
    back_one = (
        jnp.einsum("ise,de->isd", grad_query, p["w_query"], preferred_element_type=f32)
        + jnp.einsum("ise,de->isd", grad_key, p["w_key"], preferred_element_type=f32)
        + jnp.einsum("ise,de->isd", grad_value, p["w_value"], preferred_element_type=f32)
    )
    return back_one, grad_query, grad_key, grad_value


def body(
    tokens,
    lengths,
    w_query,
    w_key,
    w_value,
    b_query,
    b_value,
    w_out,
    b_out,
    w_up,
    b_up,
    w_down,
    b_down,
    norm1_gain,
    norm1_shift,
    norm2_gain,
    norm2_shift,
    cotangent,
):
    f32 = jnp.float32
    bf16 = jnp.bfloat16
    p = dict(
        w_query=w_query, w_key=w_key, w_value=w_value, b_query=b_query, b_value=b_value,
        w_out=w_out, b_out=b_out, w_up=w_up, b_up=b_up, w_down=w_down, b_down=b_down,
        norm1_gain=norm1_gain, norm1_shift=norm1_shift,
        norm2_gain=norm2_gain, norm2_shift=norm2_shift,
    )
    count = tokens.shape[0]
    items = range(count)
    link = LinkChain()
    rows_in = [tokens[i : i + 1].astype(f32) for i in items]
    cots = [cotangent[i : i + 1] for i in items]
    full_one, attn_rows, full_two, ffn_rows = {}, {}, {}, {}
    grad_full, back_rows, middle_full, rows_one = {}, {}, {}, {}
    kept, middle, hidden_pre, hidden = {}, {}, {}, {}
    grad_pre, grad_middle, g2, g_attn = {}, {}, {}, {}

    for i in items:
        normed = layer_norm(rows_in[i], norm1_gain, norm1_shift).astype(bf16)
        link.run(gather_rows, normed, full_one, i)
    for i in items:
        attn_terms, kept[i] = attention_forward(full_one[i], lengths[i : i + 1], p)
        link.run(scatter_rows, attn_terms, attn_rows, i)
    for i in items:
        middle[i] = rows_in[i] + attn_rows[i] + b_out
        normed = layer_norm(middle[i], norm2_gain, norm2_shift).astype(bf16)
        link.run(gather_rows, normed, full_two, i)
    for i in items:
        hidden_pre[i] = jnp.einsum(
            "isd,df->isf", full_two[i], w_up, preferred_element_type=f32
        ) + b_up.reshape(-1)
        hidden[i] = jax.nn.gelu(hidden_pre[i], approximate=False).astype(bf16)
        ffn_terms = jnp.einsum("isf,fd->isd", hidden[i], w_down, preferred_element_type=f32)
        link.run(scatter_rows, ffn_terms, ffn_rows, i)
    for i in items:
        link.run(gather_rows, cots[i], grad_full, i)
    results = [(middle[i] + ffn_rows[i] + b_down).astype(bf16) for i in items]
    for i in items:
        grad_hidden = jnp.einsum("isd,fd->isf", grad_full[i], w_down, preferred_element_type=f32)
        _, gelu_back = jax.vjp(partial(jax.nn.gelu, approximate=False), hidden_pre[i])
        grad_pre[i] = gelu_back(grad_hidden)[0].astype(bf16)
        back_terms = jnp.einsum("isf,df->isd", grad_pre[i], w_up, preferred_element_type=f32)
        link.run(scatter_rows, back_terms, back_rows, i)

    def cat(parts):
        return jnp.concatenate([parts[i] for i in items], axis=0)

    def dp_sum(grad, dim):
        return lax.psum_scatter(
            grad.astype(bf16), "dp", scatter_dimension=dim, tiled=True
        ).astype(f32)

    ffn_grads = None
    for i in items:
        grad_out = cots[i].astype(f32)
        _, second_back = jax.vjp(layer_norm, middle[i], norm2_gain, norm2_shift)
        grad_mid_norm, gain_two, shift_two = second_back(back_rows[i])
        grad_middle[i] = grad_out + grad_mid_norm
        g2[i] = dict(
            grad_b_out=jnp.sum(grad_middle[i], axis=(0, 1)),
            grad_b_down=jnp.sum(grad_out, axis=(0, 1)),
            grad_gain_two=gain_two, grad_shift_two=shift_two,
        )
        if i == 0:
            ffn_grads = (
                jnp.einsum("isf,isd->fd", cat(hidden), cat(grad_full), preferred_element_type=f32),
                jnp.einsum("isd,isf->df", cat(full_two), cat(grad_pre), preferred_element_type=f32),
            )
        tied = link.run(
            gather_rows, grad_middle[i].astype(bf16), middle_full, i, ffn_grads if i == 0 else None
        )
        if i == 0:
            ffn_grads = tied
    sum_w_down = dp_sum(ffn_grads[0], 1)
    sum_w_up = dp_sum(ffn_grads[1], 0)
    for i in items:
        back_one, gq, gk, gv = attention_backward(middle_full[i], kept[i], p)
        g_attn[i] = (gq, gk, gv)
        link.run(scatter_rows, back_one, rows_one, i)
    grad_ins, g1 = [], []
    for i in items:
        _, first_back = jax.vjp(layer_norm, rows_in[i], norm1_gain, norm1_shift)
        grad_in_norm, gain_one, shift_one = first_back(rows_one[i])
        grad_ins.append((grad_middle[i] + grad_in_norm).astype(bf16))
        g1.append(dict(grad_gain_one=gain_one, grad_shift_one=shift_one))

    grad_query = cat({i: g_attn[i][0] for i in items})
    grad_key = cat({i: g_attn[i][1] for i in items})
    grad_value = cat({i: g_attn[i][2] for i in items})
    grad_qkv = jnp.einsum(
        "isd,ise->de",
        cat(full_one),
        jnp.concatenate([grad_query, grad_key, grad_value], axis=-1),
        preferred_element_type=f32,
    )
    grad_out_t = jnp.einsum(
        "isd,ise->de",
        cat(middle_full),
        cat({i: kept[i]["mixed"] for i in items}),
        preferred_element_type=f32,
    )
    summed = dp_sum(jnp.concatenate([grad_qkv, grad_out_t], axis=1), 0)
    width = w_query.shape[1]
    sum_w_query = summed[:, :width]
    sum_w_key = summed[:, width : 2 * width]
    sum_w_value = summed[:, 2 * width : 3 * width]
    sum_w_out = summed[:, 3 * width :].T

    grad_pre_all = cat(grad_pre)
    grad_b_up = jnp.sum(grad_pre_all, axis=(0, 1), dtype=f32).reshape(b_up.shape)
    grad_b_query = jnp.sum(grad_query, axis=(0, 1), dtype=f32).reshape(b_query.shape)
    grad_b_value = jnp.sum(grad_value, axis=(0, 1), dtype=f32).reshape(b_value.shape)
    biases = halving_scatter(jnp.concatenate([grad_b_up, grad_b_query, grad_b_value]), "dp", 1)
    n_up, n_q = b_up.shape[0], b_query.shape[0]
    sum_b_up = biases[:n_up]
    sum_b_query = biases[n_up : n_up + n_q]
    sum_b_value = biases[n_up + n_q :]

    grads = [dict(g2[i], **g1[i]) for i in items]
    names = ["grad_b_out", "grad_b_down", "grad_gain_one", "grad_shift_one", "grad_gain_two", "grad_shift_two"]
    vectors = jnp.stack([sum(g[key] for g in grads) for key in names])
    vectors = halving_scatter(halving_scatter(vectors, "dp", 1), "mp", 1)
    sum_b_out, sum_b_down, sum_gain_one, sum_shift_one, sum_gain_two, sum_shift_two = (
        vectors[j] for j in range(len(names))
    )
    return (
        jnp.concatenate(results, axis=0),
        jnp.concatenate(grad_ins, axis=0),
        sum_w_query,
        sum_w_key,
        sum_w_value,
        sum_b_query,
        sum_b_value,
        sum_w_out,
        sum_b_out,
        sum_w_up,
        sum_b_up,
        sum_w_down,
        sum_b_down,
        sum_gain_one,
        sum_shift_one,
        sum_gain_two,
        sum_shift_two,
    )


def solution(mesh):
    return jax.shard_map(
        body,
        mesh=mesh,
        in_specs=(
            P("dp", "mp", None),
            P("dp"),
            P(None, "mp"),
            P(None, "mp"),
            P(None, "mp"),
            P("mp", None),
            P("mp", None),
            P("mp", None),
            P(),
            P(None, "mp"),
            P("mp", None),
            P("mp", None),
            P(),
            P(),
            P(),
            P(),
            P(),
            P("dp", "mp", None),
        ),
        out_specs=(
            P("dp", "mp", None),
            P("dp", "mp", None),
            P("dp", "mp"),
            P("dp", "mp"),
            P("dp", "mp"),
            P("mp", "dp"),
            P("mp", "dp"),
            P("mp", "dp"),
            P(("dp", "mp")),
            P("dp", "mp"),
            P("mp", "dp"),
            P("mp", "dp"),
            P(("dp", "mp")),
            P(("dp", "mp")),
            P(("dp", "mp")),
            P(("dp", "mp")),
            P(("dp", "mp")),
        ),
        check_vma=False,
    )
```

```python
from functools import partial

import jax
import jax.numpy as jnp
from jax import lax
from jax.sharding import PartitionSpec as P

HEAD_DIM = 128


def _pairs(n, flip):
    return [(m, m ^ flip) for m in range(n)]


def gather_rows(x, axis=1):
    n = lax.axis_size("mp")
    if n != 4:
        return lax.all_gather(x, "mp", axis=axis, tiled=True)
    me = lax.axis_index("mp")
    rows = x.shape[axis]
    half = rows // 2
    from_x = lax.ppermute(x, "mp", _pairs(n, 1))
    from_y = lax.ppermute(x, "mp", _pairs(n, 2))
    diag_a = lax.ppermute(lax.slice_in_dim(from_y, 0, half, axis=axis), "mp", _pairs(n, 1))
    diag_b = lax.ppermute(lax.slice_in_dim(from_x, half, rows, axis=axis), "mp", _pairs(n, 2))
    diag = jnp.concatenate([diag_a, diag_b], axis=axis)
    step_x = (me & 1) * rows
    step_y = (me & 2) * rows
    own_row = lax.dynamic_slice_in_dim(
        jnp.concatenate([x, from_x, x], axis=axis), step_x, 2 * rows, axis=axis
    )
    other_row = lax.dynamic_slice_in_dim(
        jnp.concatenate([from_y, diag, from_y], axis=axis), step_x, 2 * rows, axis=axis
    )
    return lax.dynamic_slice_in_dim(
        jnp.concatenate([own_row, other_row, own_row], axis=axis), step_y, 4 * rows, axis=axis
    )


def scatter_rows(y, axis=1):
    n = lax.axis_size("mp")
    if n != 4:
        return lax.psum_scatter(
            y.astype(jnp.bfloat16), "mp", scatter_dimension=axis, tiled=True
        ).astype(jnp.float32)
    me = lax.axis_index("mp")
    rows = y.shape[axis] // n
    half = rows // 2

    def part(flip, lo, hi):
        return lax.dynamic_slice_in_dim(y, (me ^ flip) * rows + lo, hi - lo, axis=axis)

    bf16 = jnp.bfloat16
    send_x = jnp.stack([part(1, 0, half), part(3, 0, half)]).astype(bf16)
    send_y = jnp.stack([part(2, half, rows), part(3, half, rows)]).astype(bf16)
    got_x = lax.ppermute(send_x, "mp", _pairs(n, 1))
    got_y = lax.ppermute(send_y, "mp", _pairs(n, 2))
    fwd_y = (got_x[1].astype(jnp.float32) + part(2, 0, half)).astype(bf16)
    fwd_x = (got_y[1].astype(jnp.float32) + part(1, half, rows)).astype(bf16)
    last_y = lax.ppermute(fwd_y, "mp", _pairs(n, 2))
    last_x = lax.ppermute(fwd_x, "mp", _pairs(n, 1))
    low = part(0, 0, half) + got_x[0].astype(jnp.float32) + last_y.astype(jnp.float32)
    high = part(0, half, rows) + got_y[0].astype(jnp.float32) + last_x.astype(jnp.float32)
    return jnp.concatenate([low, high], axis=axis)


def layer_norm(values, gain, shift):
    centre = values - jnp.mean(values, axis=-1, keepdims=True)
    spread = jnp.mean(centre * centre, axis=-1, keepdims=True)
    return centre * lax.rsqrt(spread + 1e-05) * gain + shift


def allowed_keys(lengths, seq_len):
    places = jnp.arange(seq_len)
    causal = places[None, :] <= places[:, None]
    inside = places[None, None, :] < lengths[:, None, None]
    return (causal[None] & inside)[:, None]


def head_scores(query_heads, key_heads, allowed):
    scores = jnp.einsum(
        "iqhd,ikhd->ihqk", query_heads, key_heads, preferred_element_type=jnp.float32
    ) * HEAD_DIM ** (-0.5)
    return jnp.where(allowed, scores, -1e30)


def halving_scatter(values, name, dim):
    n = lax.axis_size(name)
    if n & (n - 1):
        return lax.psum_scatter(values, name, scatter_dimension=dim, tiled=True)
    me = lax.axis_index(name)
    bit = n // 2
    while bit:
        half = values.shape[dim] // 2
        upper = (me & bit) != 0
        keep = lax.dynamic_slice_in_dim(values, jnp.where(upper, half, 0), half, axis=dim)
        give = lax.dynamic_slice_in_dim(values, jnp.where(upper, 0, half), half, axis=dim)
        values = keep + lax.ppermute(give, name, _pairs(n, bit))
        bit //= 2
    return values


def forward_item(rows_in, length, p):
    f32 = jnp.float32
    bf16 = jnp.bfloat16
    normed_one = layer_norm(rows_in, p["norm1_gain"], p["norm1_shift"]).astype(bf16)
    full_one = gather_rows(normed_one)
    items, seq_len = (full_one.shape[0], full_one.shape[1])
    heads_here = p["w_query"].shape[1] // HEAD_DIM
    split = (items, seq_len, heads_here, HEAD_DIM)

    def project(weight):
        return jnp.einsum("isd,de->ise", full_one, weight, preferred_element_type=f32)

    queries = (project(p["w_query"]) + p["b_query"].reshape(-1)).astype(bf16)
    keys_all = project(p["w_key"]).astype(bf16)
    values_all = (project(p["w_value"]) + p["b_value"].reshape(-1)).astype(bf16)
    query_heads = queries.reshape(split)
    key_heads = keys_all.reshape(split)
    value_heads = values_all.reshape(split)
    allowed = allowed_keys(length, seq_len)
    scores = head_scores(query_heads, key_heads, allowed)
    row_max = jnp.max(scores, axis=-1, keepdims=True)
    raw_weights = jnp.exp(scores - row_max)
    row_total = jnp.sum(raw_weights, axis=-1, keepdims=True)
    probs = (raw_weights / row_total).astype(bf16)
    mixed = (
        jnp.einsum("ihqk,ikhd->iqhd", probs, value_heads, preferred_element_type=f32)
        .reshape(items, seq_len, -1)
        .astype(bf16)
    )
    attn_terms = jnp.einsum("ise,ed->isd", mixed, p["w_out"], preferred_element_type=f32)
    attn_rows = scatter_rows(attn_terms)
    middle = rows_in + attn_rows + p["b_out"]
    normed_two = layer_norm(middle, p["norm2_gain"], p["norm2_shift"]).astype(bf16)
    full_two = gather_rows(normed_two)
    hidden_pre = jnp.einsum(
        "isd,df->isf", full_two, p["w_up"], preferred_element_type=f32
    ) + p["b_up"].reshape(-1)
    hidden = jax.nn.gelu(hidden_pre, approximate=False).astype(bf16)
    ffn_terms = jnp.einsum("isf,fd->isd", hidden, p["w_down"], preferred_element_type=f32)
    ffn_rows = scatter_rows(ffn_terms)
    result = (middle + ffn_rows + p["b_down"]).astype(bf16)
    kept = dict(
        full_one=full_one, query_heads=query_heads, key_heads=key_heads,
        value_heads=value_heads, allowed=allowed, row_max=row_max, row_total=row_total,
        mixed=mixed, middle=middle, full_two=full_two, hidden_pre=hidden_pre, hidden=hidden,
    )
    return result, kept


def backward_ffn(cotangent, k, p):
    f32 = jnp.float32
    bf16 = jnp.bfloat16
    grad_full = gather_rows(cotangent)
    grad_hidden = jnp.einsum("isd,fd->isf", grad_full, p["w_down"], preferred_element_type=f32)
    _, gelu_back = jax.vjp(partial(jax.nn.gelu, approximate=False), k["hidden_pre"])
    grad_pre = gelu_back(grad_hidden)[0].astype(bf16)
    back_terms = jnp.einsum("isf,df->isd", grad_pre, p["w_up"], preferred_element_type=f32)
    return grad_full, grad_pre, back_terms


def backward_mid(cotangent, back_rows, k, p):
    grad_out = cotangent.astype(jnp.float32)
    _, second_back = jax.vjp(layer_norm, k["middle"], p["norm2_gain"], p["norm2_shift"])
    grad_mid_norm, grad_gain_two, grad_shift_two = second_back(back_rows)
    grad_middle = grad_out + grad_mid_norm
    middle_full = gather_rows(grad_middle.astype(jnp.bfloat16))
    g = dict(
        grad_b_out=jnp.sum(grad_middle, axis=(0, 1)),
        grad_b_down=jnp.sum(grad_out, axis=(0, 1)),
        grad_gain_two=grad_gain_two, grad_shift_two=grad_shift_two,
    )
    return grad_middle, middle_full, g


def backward_attn(rows_in, grad_middle, middle_full, k, p):
    f32 = jnp.float32
    bf16 = jnp.bfloat16
    items, seq_len = k["full_one"].shape[:2]
    heads_here = p["w_query"].shape[1] // HEAD_DIM
    split = (items, seq_len, heads_here, HEAD_DIM)
    grad_mixed = (
        jnp.einsum("isd,ed->ise", middle_full, p["w_out"], preferred_element_type=f32)
        .astype(bf16)
        .reshape(split)
    )
    query_heads, key_heads, value_heads = k["query_heads"], k["key_heads"], k["value_heads"]
    again = head_scores(query_heads, key_heads, k["allowed"])
    probs_full = jnp.exp(again - k["row_max"]) / k["row_total"]
    probs_low = probs_full.astype(bf16)
    grad_value = (
        jnp.einsum("ihqk,iqhd->ikhd", probs_low, grad_mixed, preferred_element_type=f32)
        .astype(bf16)
        .reshape(items, seq_len, -1)
    )
    grad_probs = jnp.einsum("iqhd,ikhd->ihqk", grad_mixed, value_heads, preferred_element_type=f32)
    inner = jnp.sum(probs_full * grad_probs, axis=-1, keepdims=True)
    grad_scores = (probs_full * (grad_probs - inner)).astype(bf16)
    grad_query = (
        (
            jnp.einsum("ihqk,ikhd->iqhd", grad_scores, key_heads, preferred_element_type=f32)
            * HEAD_DIM ** (-0.5)
        )
        .astype(bf16)
        .reshape(items, seq_len, -1)
    )
    grad_key = (
        (
            jnp.einsum("ihqk,iqhd->ikhd", grad_scores, query_heads, preferred_element_type=f32)
            * HEAD_DIM ** (-0.5)
        )
        .astype(bf16)
        .reshape(items, seq_len, -1)
    )
    back_one = (
        jnp.einsum("ise,de->isd", grad_query, p["w_query"], preferred_element_type=f32)
        + jnp.einsum("ise,de->isd", grad_key, p["w_key"], preferred_element_type=f32)
        + jnp.einsum("ise,de->isd", grad_value, p["w_value"], preferred_element_type=f32)
    )
    rows_one = scatter_rows(back_one)
    _, first_back = jax.vjp(layer_norm, rows_in, p["norm1_gain"], p["norm1_shift"])
    grad_in_norm, grad_gain_one, grad_shift_one = first_back(rows_one)
    grad_inputs = (grad_middle + grad_in_norm).astype(bf16)
    g = dict(
        grad_query=grad_query, grad_key=grad_key, grad_value=grad_value,
        grad_gain_one=grad_gain_one, grad_shift_one=grad_shift_one,
    )
    return grad_inputs, g


def body(
    tokens,
    lengths,
    w_query,
    w_key,
    w_value,
    b_query,
    b_value,
    w_out,
    b_out,
    w_up,
    b_up,
    w_down,
    b_down,
    norm1_gain,
    norm1_shift,
    norm2_gain,
    norm2_shift,
    cotangent,
):
    f32 = jnp.float32
    bf16 = jnp.bfloat16
    p = dict(
        w_query=w_query, w_key=w_key, w_value=w_value, b_query=b_query, b_value=b_value,
        w_out=w_out, b_out=b_out, w_up=w_up, b_up=b_up, w_down=w_down, b_down=b_down,
        norm1_gain=norm1_gain, norm1_shift=norm1_shift,
        norm2_gain=norm2_gain, norm2_shift=norm2_shift,
    )
    count = tokens.shape[0]
    results, kept = [], []
    for i in range(count):
        rows_in = tokens[i : i + 1].astype(f32)
        result, k = forward_item(rows_in, lengths[i : i + 1], p)
        results.append(result)
        kept.append((rows_in, k))
    ks = [k for _, k in kept]
    cots = [
        lax.optimization_barrier((ks[i]["full_two"], cotangent[i : i + 1]))[1] for i in range(count)
    ]

    def cat(parts):
        return jnp.concatenate(parts, axis=0)

    def dp_sum(grad, dim):
        return lax.psum_scatter(
            grad.astype(bf16), "dp", scatter_dimension=dim, tiled=True
        ).astype(f32)

    ffn = [backward_ffn(cots[i], ks[i], p) for i in range(count)]
    grad_full = cat([f[0] for f in ffn])
    grad_pre = cat([f[1] for f in ffn])
    grad_w_down = jnp.einsum(
        "isf,isd->fd", cat([k["hidden"] for k in ks]), grad_full, preferred_element_type=f32
    )
    grad_w_up = jnp.einsum(
        "isd,isf->df", cat([k["full_two"] for k in ks]), grad_pre, preferred_element_type=f32
    )
    back_rows = [scatter_rows(f[2]) for f in ffn]
    grad_w_down, grad_w_up, back_rows = lax.optimization_barrier((grad_w_down, grad_w_up, back_rows))
    sum_w_down = dp_sum(grad_w_down, 1)
    sum_w_up = dp_sum(grad_w_up, 0)

    mids = [backward_mid(cots[i], back_rows[i], ks[i], p) for i in range(count)]
    middle_fulls = [m[1] for m in mids]
    attn = [
        backward_attn(kept[i][0], mids[i][0], middle_fulls[i], ks[i], p) for i in range(count)
    ]
    grad_ins = [a[0] for a in attn]
    grads = [dict(mids[i][2], **attn[i][1]) for i in range(count)]
    grad_query = cat([g["grad_query"] for g in grads])
    grad_key = cat([g["grad_key"] for g in grads])
    grad_value = cat([g["grad_value"] for g in grads])
    grad_qkv = jnp.einsum(
        "isd,ise->de",
        cat([k["full_one"] for k in ks]),
        jnp.concatenate([grad_query, grad_key, grad_value], axis=-1),
        preferred_element_type=f32,
    )
    grad_out_t = jnp.einsum(
        "isd,ise->de",
        cat(middle_fulls),
        cat([k["mixed"] for k in ks]),
        preferred_element_type=f32,
    )
    summed = dp_sum(jnp.concatenate([grad_qkv, grad_out_t], axis=1), 0)
    width = w_query.shape[1]
    sum_w_query = summed[:, :width]
    sum_w_key = summed[:, width : 2 * width]
    sum_w_value = summed[:, 2 * width : 3 * width]
    sum_w_out = summed[:, 3 * width :].T

    grad_b_up = jnp.sum(grad_pre, axis=(0, 1), dtype=f32).reshape(b_up.shape)
    grad_b_query = jnp.sum(grad_query, axis=(0, 1), dtype=f32).reshape(b_query.shape)
    grad_b_value = jnp.sum(grad_value, axis=(0, 1), dtype=f32).reshape(b_value.shape)
    biases = halving_scatter(jnp.concatenate([grad_b_up, grad_b_query, grad_b_value]), "dp", 1)
    n_up, n_q = b_up.shape[0], b_query.shape[0]
    sum_b_up = biases[:n_up]
    sum_b_query = biases[n_up : n_up + n_q]
    sum_b_value = biases[n_up + n_q :]

    names = ["grad_b_out", "grad_b_down", "grad_gain_one", "grad_shift_one", "grad_gain_two", "grad_shift_two"]
    vectors = jnp.stack([sum(g[key] for g in grads) for key in names])
    vectors = halving_scatter(halving_scatter(vectors, "dp", 1), "mp", 1)
    sum_b_out, sum_b_down, sum_gain_one, sum_shift_one, sum_gain_two, sum_shift_two = (
        vectors[j] for j in range(len(names))
    )
    return (
        jnp.concatenate(results, axis=0),
        jnp.concatenate(grad_ins, axis=0),
        sum_w_query,
        sum_w_key,
        sum_w_value,
        sum_b_query,
        sum_b_value,
        sum_w_out,
        sum_b_out,
        sum_w_up,
        sum_b_up,
        sum_w_down,
        sum_b_down,
        sum_gain_one,
        sum_shift_one,
        sum_gain_two,
        sum_shift_two,
    )


def solution(mesh):
    return jax.shard_map(
        body,
        mesh=mesh,
        in_specs=(
            P("dp", "mp", None),
            P("dp"),
            P(None, "mp"),
            P(None, "mp"),
            P(None, "mp"),
            P("mp", None),
            P("mp", None),
            P("mp", None),
            P(),
            P(None, "mp"),
            P("mp", None),
            P("mp", None),
            P(),
            P(),
            P(),
            P(),
            P(),
            P("dp", "mp", None),
        ),
        out_specs=(
            P("dp", "mp", None),
            P("dp", "mp", None),
            P("dp", "mp"),
            P("dp", "mp"),
            P("dp", "mp"),
            P("mp", "dp"),
            P("mp", "dp"),
            P("mp", "dp"),
            P(("dp", "mp")),
            P("dp", "mp"),
            P("mp", "dp"),
            P("mp", "dp"),
            P(("dp", "mp")),
            P(("dp", "mp")),
            P(("dp", "mp")),
            P(("dp", "mp")),
            P(("dp", "mp")),
        ),
        check_vma=False,
    )
```

```python
from functools import partial

import jax
import jax.numpy as jnp
from jax import lax
from jax.sharding import PartitionSpec as P

HEAD_DIM = 128


def _pairs(n, flip):
    return [(m, m ^ flip) for m in range(n)]


def gather_rows(x, axis=1):
    n = lax.axis_size("mp")
    if n != 4:
        return lax.all_gather(x, "mp", axis=axis, tiled=True)
    rows = x.shape[axis]
    half = rows // 2
    from_x = lax.ppermute(x, "mp", _pairs(n, 1))
    from_y = lax.ppermute(x, "mp", _pairs(n, 2))
    diag_a = lax.ppermute(lax.slice_in_dim(from_y, 0, half, axis=axis), "mp", _pairs(n, 1))
    diag_b = lax.ppermute(lax.slice_in_dim(from_x, half, rows, axis=axis), "mp", _pairs(n, 2))
    return jnp.concatenate([x, from_x, from_y, diag_a, diag_b], axis=axis)


def gathered_positions(total):
    n = lax.axis_size("mp")
    places = jnp.arange(total)
    if n != 4:
        return places
    rows = total // n
    return ((lax.axis_index("mp") ^ (places // rows)) * rows) + places % rows


def scatter_rows(y, axis=1):
    n = lax.axis_size("mp")
    if n != 4:
        return lax.psum_scatter(
            y.astype(jnp.bfloat16), "mp", scatter_dimension=axis, tiled=True
        ).astype(jnp.float32)
    rows = y.shape[axis] // n
    half = rows // 2

    def part(flip, lo, hi):
        return lax.slice_in_dim(y, flip * rows + lo, flip * rows + hi, axis=axis)

    bf16 = jnp.bfloat16
    send_x = jnp.stack([part(1, 0, half), part(3, 0, half)]).astype(bf16)
    send_y = jnp.stack([part(2, half, rows), part(3, half, rows)]).astype(bf16)
    got_x = lax.ppermute(send_x, "mp", _pairs(n, 1))
    got_y = lax.ppermute(send_y, "mp", _pairs(n, 2))
    fwd_y = (got_x[1].astype(jnp.float32) + part(2, 0, half)).astype(bf16)
    fwd_x = (got_y[1].astype(jnp.float32) + part(1, half, rows)).astype(bf16)
    last_y = lax.ppermute(fwd_y, "mp", _pairs(n, 2))
    last_x = lax.ppermute(fwd_x, "mp", _pairs(n, 1))
    low = part(0, 0, half) + got_x[0].astype(jnp.float32) + last_y.astype(jnp.float32)
    high = part(0, half, rows) + got_y[0].astype(jnp.float32) + last_x.astype(jnp.float32)
    return jnp.concatenate([low, high], axis=axis)


def layer_norm(values, gain, shift):
    centre = values - jnp.mean(values, axis=-1, keepdims=True)
    spread = jnp.mean(centre * centre, axis=-1, keepdims=True)
    return centre * lax.rsqrt(spread + 1e-05) * gain + shift


def allowed_keys(lengths, seq_len):
    places = gathered_positions(seq_len)
    causal = places[None, :] <= places[:, None]
    inside = places[None, None, :] < lengths[:, None, None]
    return (causal[None] & inside)[:, None]


def head_scores(query_heads, key_heads, allowed):
    scores = jnp.einsum(
        "iqhd,ikhd->ihqk", query_heads, key_heads, preferred_element_type=jnp.float32
    ) * HEAD_DIM ** (-0.5)
    return jnp.where(allowed, scores, -1e30)


def halving_scatter(values, name, dim):
    n = lax.axis_size(name)
    if n & (n - 1):
        return lax.psum_scatter(values, name, scatter_dimension=dim, tiled=True)
    me = lax.axis_index(name)
    bit = n // 2
    while bit:
        half = values.shape[dim] // 2
        upper = (me & bit) != 0
        keep = lax.dynamic_slice_in_dim(values, jnp.where(upper, half, 0), half, axis=dim)
        give = lax.dynamic_slice_in_dim(values, jnp.where(upper, 0, half), half, axis=dim)
        values = keep + lax.ppermute(give, name, _pairs(n, bit))
        bit //= 2
    return values


def forward_item(rows_in, length, p):
    f32 = jnp.float32
    bf16 = jnp.bfloat16
    normed_one = layer_norm(rows_in, p["norm1_gain"], p["norm1_shift"]).astype(bf16)
    full_one = gather_rows(normed_one)
    items, seq_len = (full_one.shape[0], full_one.shape[1])
    heads_here = p["w_query"].shape[1] // HEAD_DIM
    split = (items, seq_len, heads_here, HEAD_DIM)

    def project(weight):
        return jnp.einsum("isd,de->ise", full_one, weight, preferred_element_type=f32)

    queries = (project(p["w_query"]) + p["b_query"].reshape(-1)).astype(bf16)
    keys_all = project(p["w_key"]).astype(bf16)
    values_all = (project(p["w_value"]) + p["b_value"].reshape(-1)).astype(bf16)
    query_heads = queries.reshape(split)
    key_heads = keys_all.reshape(split)
    value_heads = values_all.reshape(split)
    allowed = allowed_keys(length, seq_len)
    scores = head_scores(query_heads, key_heads, allowed)
    row_max = jnp.max(scores, axis=-1, keepdims=True)
    raw_weights = jnp.exp(scores - row_max)
    row_total = jnp.sum(raw_weights, axis=-1, keepdims=True)
    probs = (raw_weights / row_total).astype(bf16)
    mixed = (
        jnp.einsum("ihqk,ikhd->iqhd", probs, value_heads, preferred_element_type=f32)
        .reshape(items, seq_len, -1)
        .astype(bf16)
    )
    attn_terms = jnp.einsum("ise,ed->isd", mixed, p["w_out"], preferred_element_type=f32)
    attn_rows = scatter_rows(attn_terms)
    middle = rows_in + attn_rows + p["b_out"]
    normed_two = layer_norm(middle, p["norm2_gain"], p["norm2_shift"]).astype(bf16)
    full_two = gather_rows(normed_two)
    hidden_pre = jnp.einsum(
        "isd,df->isf", full_two, p["w_up"], preferred_element_type=f32
    ) + p["b_up"].reshape(-1)
    hidden = jax.nn.gelu(hidden_pre, approximate=False).astype(bf16)
    ffn_terms = jnp.einsum("isf,fd->isd", hidden, p["w_down"], preferred_element_type=f32)
    ffn_rows = scatter_rows(ffn_terms)
    result = (middle + ffn_rows + p["b_down"]).astype(bf16)
    kept = dict(
        full_one=full_one, query_heads=query_heads, key_heads=key_heads,
        value_heads=value_heads, allowed=allowed, row_max=row_max, row_total=row_total,
        mixed=mixed, middle=middle, full_two=full_two, hidden_pre=hidden_pre, hidden=hidden,
    )
    return result, kept


def backward_ffn(cotangent, k, p):
    f32 = jnp.float32
    bf16 = jnp.bfloat16
    grad_full = gather_rows(cotangent)
    grad_hidden = jnp.einsum("isd,fd->isf", grad_full, p["w_down"], preferred_element_type=f32)
    _, gelu_back = jax.vjp(partial(jax.nn.gelu, approximate=False), k["hidden_pre"])
    grad_pre = gelu_back(grad_hidden)[0].astype(bf16)
    back_terms = jnp.einsum("isf,df->isd", grad_pre, p["w_up"], preferred_element_type=f32)
    return grad_full, grad_pre, back_terms


def backward_mid(cotangent, back_rows, k, p):
    grad_out = cotangent.astype(jnp.float32)
    _, second_back = jax.vjp(layer_norm, k["middle"], p["norm2_gain"], p["norm2_shift"])
    grad_mid_norm, grad_gain_two, grad_shift_two = second_back(back_rows)
    grad_middle = grad_out + grad_mid_norm
    middle_full = gather_rows(grad_middle.astype(jnp.bfloat16))
    g = dict(
        grad_b_out=jnp.sum(grad_middle, axis=(0, 1)),
        grad_b_down=jnp.sum(grad_out, axis=(0, 1)),
        grad_gain_two=grad_gain_two, grad_shift_two=grad_shift_two,
    )
    return grad_middle, middle_full, g


def backward_attn(rows_in, grad_middle, middle_full, k, p):
    f32 = jnp.float32
    bf16 = jnp.bfloat16
    items, seq_len = k["full_one"].shape[:2]
    heads_here = p["w_query"].shape[1] // HEAD_DIM
    split = (items, seq_len, heads_here, HEAD_DIM)
    grad_mixed = (
        jnp.einsum("isd,ed->ise", middle_full, p["w_out"], preferred_element_type=f32)
        .astype(bf16)
        .reshape(split)
    )
    query_heads, key_heads, value_heads = k["query_heads"], k["key_heads"], k["value_heads"]
    again = head_scores(query_heads, key_heads, k["allowed"])
    probs_full = jnp.exp(again - k["row_max"]) / k["row_total"]
    probs_low = probs_full.astype(bf16)
    grad_value = (
        jnp.einsum("ihqk,iqhd->ikhd", probs_low, grad_mixed, preferred_element_type=f32)
        .astype(bf16)
        .reshape(items, seq_len, -1)
    )
    grad_probs = jnp.einsum("iqhd,ikhd->ihqk", grad_mixed, value_heads, preferred_element_type=f32)
    inner = jnp.sum(probs_full * grad_probs, axis=-1, keepdims=True)
    grad_scores = (probs_full * (grad_probs - inner)).astype(bf16)
    grad_query = (
        (
            jnp.einsum("ihqk,ikhd->iqhd", grad_scores, key_heads, preferred_element_type=f32)
            * HEAD_DIM ** (-0.5)
        )
        .astype(bf16)
        .reshape(items, seq_len, -1)
    )
    grad_key = (
        (
            jnp.einsum("ihqk,iqhd->ikhd", grad_scores, query_heads, preferred_element_type=f32)
            * HEAD_DIM ** (-0.5)
        )
        .astype(bf16)
        .reshape(items, seq_len, -1)
    )
    back_one = (
        jnp.einsum("ise,de->isd", grad_query, p["w_query"], preferred_element_type=f32)
        + jnp.einsum("ise,de->isd", grad_key, p["w_key"], preferred_element_type=f32)
        + jnp.einsum("ise,de->isd", grad_value, p["w_value"], preferred_element_type=f32)
    )
    rows_one = scatter_rows(back_one)
    _, first_back = jax.vjp(layer_norm, rows_in, p["norm1_gain"], p["norm1_shift"])
    grad_in_norm, grad_gain_one, grad_shift_one = first_back(rows_one)
    grad_inputs = (grad_middle + grad_in_norm).astype(bf16)
    g = dict(
        grad_query=grad_query, grad_key=grad_key, grad_value=grad_value,
        grad_gain_one=grad_gain_one, grad_shift_one=grad_shift_one,
    )
    return grad_inputs, g


def body(
    tokens,
    lengths,
    w_query,
    w_key,
    w_value,
    b_query,
    b_value,
    w_out,
    b_out,
    w_up,
    b_up,
    w_down,
    b_down,
    norm1_gain,
    norm1_shift,
    norm2_gain,
    norm2_shift,
    cotangent,
):
    f32 = jnp.float32
    bf16 = jnp.bfloat16
    p = dict(
        w_query=w_query, w_key=w_key, w_value=w_value, b_query=b_query, b_value=b_value,
        w_out=w_out, b_out=b_out, w_up=w_up, b_up=b_up, w_down=w_down, b_down=b_down,
        norm1_gain=norm1_gain, norm1_shift=norm1_shift,
        norm2_gain=norm2_gain, norm2_shift=norm2_shift,
    )
    count = tokens.shape[0]
    results, kept = [], []
    for i in range(count):
        rows_in = tokens[i : i + 1].astype(f32)
        result, k = forward_item(rows_in, lengths[i : i + 1], p)
        results.append(result)
        kept.append((rows_in, k))
    ks = [k for _, k in kept]
    cots = [
        lax.optimization_barrier((ks[i]["full_two"], cotangent[i : i + 1]))[1] for i in range(count)
    ]

    def cat(parts):
        return jnp.concatenate(parts, axis=0)

    def dp_sum(grad, dim):
        return lax.psum_scatter(
            grad.astype(bf16), "dp", scatter_dimension=dim, tiled=True
        ).astype(f32)

    ffn = [backward_ffn(cots[i], ks[i], p) for i in range(count)]
    grad_full = cat([f[0] for f in ffn])
    grad_pre = cat([f[1] for f in ffn])
    grad_w_down = jnp.einsum(
        "isf,isd->fd", cat([k["hidden"] for k in ks]), grad_full, preferred_element_type=f32
    )
    grad_w_up = jnp.einsum(
        "isd,isf->df", cat([k["full_two"] for k in ks]), grad_pre, preferred_element_type=f32
    )
    back_rows = [scatter_rows(f[2]) for f in ffn]
    grad_w_down, grad_w_up, back_rows = lax.optimization_barrier((grad_w_down, grad_w_up, back_rows))
    sum_w_down = dp_sum(grad_w_down, 1)
    sum_w_up = dp_sum(grad_w_up, 0)

    mids = [backward_mid(cots[i], back_rows[i], ks[i], p) for i in range(count)]
    middle_fulls = [m[1] for m in mids]
    attn = [
        backward_attn(kept[i][0], mids[i][0], middle_fulls[i], ks[i], p) for i in range(count)
    ]
    grad_ins = [a[0] for a in attn]
    grads = [dict(mids[i][2], **attn[i][1]) for i in range(count)]
    grad_query = cat([g["grad_query"] for g in grads])
    grad_key = cat([g["grad_key"] for g in grads])
    grad_value = cat([g["grad_value"] for g in grads])
    grad_qkv = jnp.einsum(
        "isd,ise->de",
        cat([k["full_one"] for k in ks]),
        jnp.concatenate([grad_query, grad_key, grad_value], axis=-1),
        preferred_element_type=f32,
    )
    grad_out_t = jnp.einsum(
        "isd,ise->de",
        cat(middle_fulls),
        cat([k["mixed"] for k in ks]),
        preferred_element_type=f32,
    )
    summed = dp_sum(jnp.concatenate([grad_qkv, grad_out_t], axis=1), 0)
    width = w_query.shape[1]
    sum_w_query = summed[:, :width]
    sum_w_key = summed[:, width : 2 * width]
    sum_w_value = summed[:, 2 * width : 3 * width]
    sum_w_out = summed[:, 3 * width :].T

    grad_b_up = jnp.sum(grad_pre, axis=(0, 1), dtype=f32).reshape(b_up.shape)
    grad_b_query = jnp.sum(grad_query, axis=(0, 1), dtype=f32).reshape(b_query.shape)
    grad_b_value = jnp.sum(grad_value, axis=(0, 1), dtype=f32).reshape(b_value.shape)
    biases = halving_scatter(jnp.concatenate([grad_b_up, grad_b_query, grad_b_value]), "dp", 1)
    n_up, n_q = b_up.shape[0], b_query.shape[0]
    sum_b_up = biases[:n_up]
    sum_b_query = biases[n_up : n_up + n_q]
    sum_b_value = biases[n_up + n_q :]

    names = ["grad_b_out", "grad_b_down", "grad_gain_one", "grad_shift_one", "grad_gain_two", "grad_shift_two"]
    vectors = jnp.stack([sum(g[key] for g in grads) for key in names])
    vectors = halving_scatter(halving_scatter(vectors, "dp", 1), "mp", 1)
    sum_b_out, sum_b_down, sum_gain_one, sum_shift_one, sum_gain_two, sum_shift_two = (
        vectors[j] for j in range(len(names))
    )
    return (
        jnp.concatenate(results, axis=0),
        jnp.concatenate(grad_ins, axis=0),
        sum_w_query,
        sum_w_key,
        sum_w_value,
        sum_b_query,
        sum_b_value,
        sum_w_out,
        sum_b_out,
        sum_w_up,
        sum_b_up,
        sum_w_down,
        sum_b_down,
        sum_gain_one,
        sum_shift_one,
        sum_gain_two,
        sum_shift_two,
    )


def solution(mesh):
    return jax.shard_map(
        body,
        mesh=mesh,
        in_specs=(
            P("dp", "mp", None),
            P("dp"),
            P(None, "mp"),
            P(None, "mp"),
            P(None, "mp"),
            P("mp", None),
            P("mp", None),
            P("mp", None),
            P(),
            P(None, "mp"),
            P("mp", None),
            P("mp", None),
            P(),
            P(),
            P(),
            P(),
            P(),
            P("dp", "mp", None),
        ),
        out_specs=(
            P("dp", "mp", None),
            P("dp", "mp", None),
            P("dp", "mp"),
            P("dp", "mp"),
            P("dp", "mp"),
            P("mp", "dp"),
            P("mp", "dp"),
            P("mp", "dp"),
            P(("dp", "mp")),
            P("dp", "mp"),
            P("mp", "dp"),
            P("mp", "dp"),
            P(("dp", "mp")),
            P(("dp", "mp")),
            P(("dp", "mp")),
            P(("dp", "mp")),
            P(("dp", "mp")),
        ),
        check_vma=False,
    )
```

```python
from functools import partial

import jax
import jax.numpy as jnp
from jax import lax
from jax.sharding import PartitionSpec as P

HEAD_DIM = 128


def _pairs(n, flip):
    return [(m, m ^ flip) for m in range(n)]


def gather_rows(x, axis=1):
    n = lax.axis_size("mp")
    if n != 4:
        return lax.all_gather(x, "mp", axis=axis, tiled=True)
    rows = x.shape[axis]
    half = rows // 2
    from_x = lax.ppermute(x, "mp", _pairs(n, 1))
    from_y = lax.ppermute(x, "mp", _pairs(n, 2))
    diag_a = lax.ppermute(lax.slice_in_dim(from_y, 0, half, axis=axis), "mp", _pairs(n, 1))
    diag_b = lax.ppermute(lax.slice_in_dim(from_x, half, rows, axis=axis), "mp", _pairs(n, 2))
    return jnp.concatenate([x, from_x, from_y, diag_a, diag_b], axis=axis)


def gathered_positions(total):
    n = lax.axis_size("mp")
    places = jnp.arange(total)
    if n != 4:
        return places
    rows = total // n
    return ((lax.axis_index("mp") ^ (places // rows)) * rows) + places % rows


def scatter_rows(y, axis=1):
    n = lax.axis_size("mp")
    if n != 4:
        return lax.psum_scatter(
            y.astype(jnp.bfloat16), "mp", scatter_dimension=axis, tiled=True
        ).astype(jnp.float32)
    rows = y.shape[axis] // n
    half = rows // 2

    def part(flip, lo, hi):
        return lax.slice_in_dim(y, flip * rows + lo, flip * rows + hi, axis=axis)

    bf16 = jnp.bfloat16
    send_x = jnp.stack([part(1, 0, half), part(3, 0, half)]).astype(bf16)
    send_y = jnp.stack([part(2, half, rows), part(3, half, rows)]).astype(bf16)
    got_x = lax.ppermute(send_x, "mp", _pairs(n, 1))
    got_y = lax.ppermute(send_y, "mp", _pairs(n, 2))
    fwd_y = (got_x[1].astype(jnp.float32) + part(2, 0, half)).astype(bf16)
    fwd_x = (got_y[1].astype(jnp.float32) + part(1, half, rows)).astype(bf16)
    last_y = lax.ppermute(fwd_y, "mp", _pairs(n, 2))
    last_x = lax.ppermute(fwd_x, "mp", _pairs(n, 1))
    low = part(0, 0, half) + got_x[0].astype(jnp.float32) + last_y.astype(jnp.float32)
    high = part(0, half, rows) + got_y[0].astype(jnp.float32) + last_x.astype(jnp.float32)
    return jnp.concatenate([low, high], axis=axis)


def layer_norm(values, gain, shift):
    centre = values - jnp.mean(values, axis=-1, keepdims=True)
    spread = jnp.mean(centre * centre, axis=-1, keepdims=True)
    return centre * lax.rsqrt(spread + 1e-05) * gain + shift


def allowed_keys(lengths, seq_len):
    places = gathered_positions(seq_len)
    causal = places[None, :] <= places[:, None]
    inside = places[None, None, :] < lengths[:, None, None]
    return (causal[None] & inside)[:, None]


def head_scores(query_heads, key_heads, allowed):
    scores = jnp.einsum(
        "iqhd,ikhd->ihqk", query_heads, key_heads, preferred_element_type=jnp.float32
    ) * HEAD_DIM ** (-0.5)
    return jnp.where(allowed, scores, -1e30)


def halving_scatter(values, name, dim):
    n = lax.axis_size(name)
    if n & (n - 1):
        return lax.psum_scatter(values, name, scatter_dimension=dim, tiled=True)
    me = lax.axis_index(name)
    bit = n // 2
    while bit:
        half = values.shape[dim] // 2
        upper = (me & bit) != 0
        keep = lax.dynamic_slice_in_dim(values, jnp.where(upper, half, 0), half, axis=dim)
        give = lax.dynamic_slice_in_dim(values, jnp.where(upper, 0, half), half, axis=dim)
        values = keep + lax.ppermute(give, name, _pairs(n, bit))
        bit //= 2
    return values


def forward_item(rows_in, length, p):
    f32 = jnp.float32
    bf16 = jnp.bfloat16
    normed_one = layer_norm(rows_in, p["norm1_gain"], p["norm1_shift"]).astype(bf16)
    full_one = gather_rows(normed_one)
    items, seq_len = (full_one.shape[0], full_one.shape[1])
    heads_here = p["w_query"].shape[1] // HEAD_DIM
    split = (items, seq_len, heads_here, HEAD_DIM)

    def project(weight):
        return jnp.einsum("isd,de->ise", full_one, weight, preferred_element_type=f32)

    queries = (project(p["w_query"]) + p["b_query"].reshape(-1)).astype(bf16)
    keys_all = project(p["w_key"]).astype(bf16)
    values_all = (project(p["w_value"]) + p["b_value"].reshape(-1)).astype(bf16)
    query_heads = queries.reshape(split)
    key_heads = keys_all.reshape(split)
    value_heads = values_all.reshape(split)
    allowed = allowed_keys(length, seq_len)
    scores = head_scores(query_heads, key_heads, allowed)
    row_max = jnp.max(scores, axis=-1, keepdims=True)
    raw_weights = jnp.exp(scores - row_max)
    row_total = jnp.sum(raw_weights, axis=-1, keepdims=True)
    probs = (raw_weights / row_total).astype(bf16)
    mixed = (
        jnp.einsum("ihqk,ikhd->iqhd", probs, value_heads, preferred_element_type=f32)
        .reshape(items, seq_len, -1)
        .astype(bf16)
    )
    attn_terms = jnp.einsum("ise,ed->isd", mixed, p["w_out"], preferred_element_type=f32)
    attn_rows = scatter_rows(attn_terms)
    middle = rows_in + attn_rows + p["b_out"]
    normed_two = layer_norm(middle, p["norm2_gain"], p["norm2_shift"]).astype(bf16)
    full_two = gather_rows(normed_two)
    hidden_pre = jnp.einsum(
        "isd,df->isf", full_two, p["w_up"], preferred_element_type=f32
    ) + p["b_up"].reshape(-1)
    hidden = jax.nn.gelu(hidden_pre, approximate=False).astype(bf16)
    ffn_terms = jnp.einsum("isf,fd->isd", hidden, p["w_down"], preferred_element_type=f32)
    ffn_rows = scatter_rows(ffn_terms)
    result = (middle + ffn_rows + p["b_down"]).astype(bf16)
    kept = dict(
        full_one=full_one, query_heads=query_heads, key_heads=key_heads,
        value_heads=value_heads, allowed=allowed, row_max=row_max, row_total=row_total,
        mixed=mixed, middle=middle, full_two=full_two, hidden_pre=hidden_pre, hidden=hidden,
    )
    return result, kept


def backward_ffn(grad_full, k, p):
    f32 = jnp.float32
    bf16 = jnp.bfloat16
    grad_hidden = jnp.einsum("isd,fd->isf", grad_full, p["w_down"], preferred_element_type=f32)
    _, gelu_back = jax.vjp(partial(jax.nn.gelu, approximate=False), k["hidden_pre"])
    grad_pre = gelu_back(grad_hidden)[0].astype(bf16)
    back_terms = jnp.einsum("isf,df->isd", grad_pre, p["w_up"], preferred_element_type=f32)
    return grad_full, grad_pre, back_terms


def backward_mid(cotangent, back_rows, k, p):
    grad_out = cotangent.astype(jnp.float32)
    _, second_back = jax.vjp(layer_norm, k["middle"], p["norm2_gain"], p["norm2_shift"])
    grad_mid_norm, grad_gain_two, grad_shift_two = second_back(back_rows)
    grad_middle = grad_out + grad_mid_norm
    middle_full = gather_rows(grad_middle.astype(jnp.bfloat16))
    g = dict(
        grad_b_out=jnp.sum(grad_middle, axis=(0, 1)),
        grad_b_down=jnp.sum(grad_out, axis=(0, 1)),
        grad_gain_two=grad_gain_two, grad_shift_two=grad_shift_two,
    )
    return grad_middle, middle_full, g


def backward_attn(rows_in, grad_middle, middle_full, k, p):
    f32 = jnp.float32
    bf16 = jnp.bfloat16
    items, seq_len = k["full_one"].shape[:2]
    heads_here = p["w_query"].shape[1] // HEAD_DIM
    split = (items, seq_len, heads_here, HEAD_DIM)
    grad_mixed = (
        jnp.einsum("isd,ed->ise", middle_full, p["w_out"], preferred_element_type=f32)
        .astype(bf16)
        .reshape(split)
    )
    query_heads, key_heads, value_heads = k["query_heads"], k["key_heads"], k["value_heads"]
    again = head_scores(query_heads, key_heads, k["allowed"])
    probs_full = jnp.exp(again - k["row_max"]) / k["row_total"]
    probs_low = probs_full.astype(bf16)
    grad_value = (
        jnp.einsum("ihqk,iqhd->ikhd", probs_low, grad_mixed, preferred_element_type=f32)
        .astype(bf16)
        .reshape(items, seq_len, -1)
    )
    grad_probs = jnp.einsum("iqhd,ikhd->ihqk", grad_mixed, value_heads, preferred_element_type=f32)
    inner = jnp.sum(probs_full * grad_probs, axis=-1, keepdims=True)
    grad_scores = (probs_full * (grad_probs - inner)).astype(bf16)
    grad_query = (
        (
            jnp.einsum("ihqk,ikhd->iqhd", grad_scores, key_heads, preferred_element_type=f32)
            * HEAD_DIM ** (-0.5)
        )
        .astype(bf16)
        .reshape(items, seq_len, -1)
    )
    grad_key = (
        (
            jnp.einsum("ihqk,iqhd->ikhd", grad_scores, query_heads, preferred_element_type=f32)
            * HEAD_DIM ** (-0.5)
        )
        .astype(bf16)
        .reshape(items, seq_len, -1)
    )
    back_one = (
        jnp.einsum("ise,de->isd", grad_query, p["w_query"], preferred_element_type=f32)
        + jnp.einsum("ise,de->isd", grad_key, p["w_key"], preferred_element_type=f32)
        + jnp.einsum("ise,de->isd", grad_value, p["w_value"], preferred_element_type=f32)
    )
    rows_one = scatter_rows(back_one)
    _, first_back = jax.vjp(layer_norm, rows_in, p["norm1_gain"], p["norm1_shift"])
    grad_in_norm, grad_gain_one, grad_shift_one = first_back(rows_one)
    grad_inputs = (grad_middle + grad_in_norm).astype(bf16)
    g = dict(
        grad_query=grad_query, grad_key=grad_key, grad_value=grad_value,
        grad_gain_one=grad_gain_one, grad_shift_one=grad_shift_one,
    )
    return grad_inputs, g


def body(
    tokens,
    lengths,
    w_query,
    w_key,
    w_value,
    b_query,
    b_value,
    w_out,
    b_out,
    w_up,
    b_up,
    w_down,
    b_down,
    norm1_gain,
    norm1_shift,
    norm2_gain,
    norm2_shift,
    cotangent,
):
    f32 = jnp.float32
    bf16 = jnp.bfloat16
    p = dict(
        w_query=w_query, w_key=w_key, w_value=w_value, b_query=b_query, b_value=b_value,
        w_out=w_out, b_out=b_out, w_up=w_up, b_up=b_up, w_down=w_down, b_down=b_down,
        norm1_gain=norm1_gain, norm1_shift=norm1_shift,
        norm2_gain=norm2_gain, norm2_shift=norm2_shift,
    )
    count = tokens.shape[0]
    results, kept = [], []
    for i in range(count):
        rows_in = tokens[i : i + 1].astype(f32)
        result, k = forward_item(rows_in, lengths[i : i + 1], p)
        results.append(result)
        kept.append((rows_in, k))
    ks = [k for _, k in kept]
    cots = [
        lax.optimization_barrier((ks[i]["full_two"], cotangent[i : i + 1]))[1] for i in range(count)
    ]

    def cat(parts):
        return jnp.concatenate(parts, axis=0)

    def dp_sum(grad, dim):
        return lax.psum_scatter(
            grad.astype(bf16), "dp", scatter_dimension=dim, tiled=True
        ).astype(f32)

    grad_fulls = [gather_rows(cots[i]) for i in range(count)]
    grad_full = cat(grad_fulls)
    grad_w_down = jnp.einsum(
        "isf,isd->fd", cat([k["hidden"] for k in ks]), grad_full, preferred_element_type=f32
    )
    ffn = [backward_ffn(grad_fulls[i], ks[i], p) for i in range(count)]
    grad_w_down, back_terms = lax.optimization_barrier((grad_w_down, [f[2] for f in ffn]))
    sum_w_down = dp_sum(grad_w_down, 1)
    grad_pre = cat([f[1] for f in ffn])
    grad_w_up = jnp.einsum(
        "isd,isf->df", cat([k["full_two"] for k in ks]), grad_pre, preferred_element_type=f32
    )
    back_rows = [scatter_rows(t) for t in back_terms]
    grad_w_up, back_rows = lax.optimization_barrier((grad_w_up, back_rows))
    sum_w_up = dp_sum(grad_w_up, 0)

    mids = [backward_mid(cots[i], back_rows[i], ks[i], p) for i in range(count)]
    middle_fulls = [m[1] for m in mids]
    attn = [
        backward_attn(kept[i][0], mids[i][0], middle_fulls[i], ks[i], p) for i in range(count)
    ]
    grad_ins = [a[0] for a in attn]
    grads = [dict(mids[i][2], **attn[i][1]) for i in range(count)]
    grad_query = cat([g["grad_query"] for g in grads])
    grad_key = cat([g["grad_key"] for g in grads])
    grad_value = cat([g["grad_value"] for g in grads])
    grad_qkv = jnp.einsum(
        "isd,ise->de",
        cat([k["full_one"] for k in ks]),
        jnp.concatenate([grad_query, grad_key, grad_value], axis=-1),
        preferred_element_type=f32,
    )
    grad_out_t = jnp.einsum(
        "isd,ise->de",
        cat(middle_fulls),
        cat([k["mixed"] for k in ks]),
        preferred_element_type=f32,
    )
    summed = dp_sum(jnp.concatenate([grad_qkv, grad_out_t], axis=1), 0)
    width = w_query.shape[1]
    sum_w_query = summed[:, :width]
    sum_w_key = summed[:, width : 2 * width]
    sum_w_value = summed[:, 2 * width : 3 * width]
    sum_w_out = summed[:, 3 * width :].T

    grad_b_up = jnp.sum(grad_pre, axis=(0, 1), dtype=f32).reshape(b_up.shape)
    grad_b_query = jnp.sum(grad_query, axis=(0, 1), dtype=f32).reshape(b_query.shape)
    grad_b_value = jnp.sum(grad_value, axis=(0, 1), dtype=f32).reshape(b_value.shape)
    biases = halving_scatter(jnp.concatenate([grad_b_up, grad_b_query, grad_b_value]), "dp", 1)
    n_up, n_q = b_up.shape[0], b_query.shape[0]
    sum_b_up = biases[:n_up]
    sum_b_query = biases[n_up : n_up + n_q]
    sum_b_value = biases[n_up + n_q :]

    names = ["grad_b_out", "grad_b_down", "grad_gain_one", "grad_shift_one", "grad_gain_two", "grad_shift_two"]
    vectors = jnp.stack([sum(g[key] for g in grads) for key in names])
    vectors = halving_scatter(halving_scatter(vectors, "dp", 1), "mp", 1)
    sum_b_out, sum_b_down, sum_gain_one, sum_shift_one, sum_gain_two, sum_shift_two = (
        vectors[j] for j in range(len(names))
    )
    return (
        jnp.concatenate(results, axis=0),
        jnp.concatenate(grad_ins, axis=0),
        sum_w_query,
        sum_w_key,
        sum_w_value,
        sum_b_query,
        sum_b_value,
        sum_w_out,
        sum_b_out,
        sum_w_up,
        sum_b_up,
        sum_w_down,
        sum_b_down,
        sum_gain_one,
        sum_shift_one,
        sum_gain_two,
        sum_shift_two,
    )


def solution(mesh):
    return jax.shard_map(
        body,
        mesh=mesh,
        in_specs=(
            P("dp", "mp", None),
            P("dp"),
            P(None, "mp"),
            P(None, "mp"),
            P(None, "mp"),
            P("mp", None),
            P("mp", None),
            P("mp", None),
            P(),
            P(None, "mp"),
            P("mp", None),
            P("mp", None),
            P(),
            P(),
            P(),
            P(),
            P(),
            P("dp", "mp", None),
        ),
        out_specs=(
            P("dp", "mp", None),
            P("dp", "mp", None),
            P("dp", "mp"),
            P("dp", "mp"),
            P("dp", "mp"),
            P("mp", "dp"),
            P("mp", "dp"),
            P("mp", "dp"),
            P(("dp", "mp")),
            P("dp", "mp"),
            P("mp", "dp"),
            P("mp", "dp"),
            P(("dp", "mp")),
            P(("dp", "mp")),
            P(("dp", "mp")),
            P(("dp", "mp")),
            P(("dp", "mp")),
        ),
        check_vma=False,
    )
```

```python
from functools import partial

import jax
import jax.numpy as jnp
from jax import lax
from jax.sharding import PartitionSpec as P


HEAD_DIM = 128


def _pairs(n, flip):
    return [(m, m ^ flip) for m in range(n)]


def gather_rows(x, axis=1):
    n = lax.axis_size("mp")
    if n != 4:
        return lax.all_gather(x, "mp", axis=axis, tiled=True)
    rows = x.shape[axis]
    half = rows // 2
    from_x = lax.ppermute(x, "mp", _pairs(n, 1))
    from_y = lax.ppermute(x, "mp", _pairs(n, 2))
    diag_a = lax.ppermute(lax.slice_in_dim(from_y, 0, half, axis=axis), "mp", _pairs(n, 1))
    diag_b = lax.ppermute(lax.slice_in_dim(from_x, half, rows, axis=axis), "mp", _pairs(n, 2))
    return jnp.concatenate([x, from_x, from_y, diag_a, diag_b], axis=axis)


def gathered_positions(total):
    n = lax.axis_size("mp")
    places = jnp.arange(total)
    if n != 4:
        return places
    rows = total // n
    return ((lax.axis_index("mp") ^ (places // rows)) * rows) + places % rows


def scatter_rows(y, axis=1):
    n = lax.axis_size("mp")
    if n != 4:
        return lax.psum_scatter(
            y.astype(jnp.bfloat16), "mp", scatter_dimension=axis, tiled=True
        ).astype(jnp.float32)
    rows = y.shape[axis] // n
    half = rows // 2

    def part(flip, lo, hi):
        return lax.slice_in_dim(y, flip * rows + lo, flip * rows + hi, axis=axis)

    bf16 = jnp.bfloat16
    send_x = jnp.stack([part(1, 0, half), part(3, 0, half)]).astype(bf16)
    send_y = jnp.stack([part(2, half, rows), part(3, half, rows)]).astype(bf16)
    got_x = lax.ppermute(send_x, "mp", _pairs(n, 1))
    got_y = lax.ppermute(send_y, "mp", _pairs(n, 2))
    fwd_y = (got_x[1].astype(jnp.float32) + part(2, 0, half)).astype(bf16)
    fwd_x = (got_y[1].astype(jnp.float32) + part(1, half, rows)).astype(bf16)
    last_y = lax.ppermute(fwd_y, "mp", _pairs(n, 2))
    last_x = lax.ppermute(fwd_x, "mp", _pairs(n, 1))
    low = part(0, 0, half) + got_x[0].astype(jnp.float32) + last_y.astype(jnp.float32)
    high = part(0, half, rows) + got_y[0].astype(jnp.float32) + last_x.astype(jnp.float32)
    return jnp.concatenate([low, high], axis=axis)


def layer_norm(values, gain, shift):
    centre = values - jnp.mean(values, axis=-1, keepdims=True)
    spread = jnp.mean(centre * centre, axis=-1, keepdims=True)
    return centre * lax.rsqrt(spread + 1e-05) * gain + shift


def allowed_keys(lengths, seq_len):
    places = gathered_positions(seq_len)
    causal = places[None, :] <= places[:, None]
    inside = places[None, None, :] < lengths[:, None, None]
    return (causal[None] & inside)[:, None]


def head_scores(query_heads, key_heads, allowed):
    scores = jnp.einsum(
        "iqhd,ikhd->ihqk", query_heads, key_heads, preferred_element_type=jnp.float32
    ) * HEAD_DIM ** (-0.5)
    return jnp.where(allowed, scores, -1e30)


def halving_scatter(values, name, dim):
    n = lax.axis_size(name)
    if n & (n - 1):
        return lax.psum_scatter(values, name, scatter_dimension=dim, tiled=True)
    me = lax.axis_index(name)
    bit = n // 2
    while bit:
        half = values.shape[dim] // 2
        upper = (me & bit) != 0
        keep = lax.dynamic_slice_in_dim(values, jnp.where(upper, half, 0), half, axis=dim)
        give = lax.dynamic_slice_in_dim(values, jnp.where(upper, 0, half), half, axis=dim)
        values = keep + lax.ppermute(give, name, _pairs(n, bit))
        bit //= 2
    return values


def forward_item(rows_in, length, p):
    bf16 = jnp.bfloat16
    normed_one = layer_norm(rows_in, p["norm1_gain"], p["norm1_shift"]).astype(bf16)
    full_one = gather_rows(normed_one)
    return _forward_attn(length, p, full_one)


def _forward_attn(length, p, full_one):
    f32 = jnp.float32
    bf16 = jnp.bfloat16
    items, seq_len = (full_one.shape[0], full_one.shape[1])
    heads_here = p["w_query"].shape[1] // HEAD_DIM
    split = (items, seq_len, heads_here, HEAD_DIM)

    def project(weight):
        return jnp.einsum("isd,de->ise", full_one, weight, preferred_element_type=f32)

    queries = (project(p["w_query"]) + p["b_query"].reshape(-1)).astype(bf16)
    keys_all = project(p["w_key"]).astype(bf16)
    values_all = (project(p["w_value"]) + p["b_value"].reshape(-1)).astype(bf16)
    query_heads = queries.reshape(split)
    key_heads = keys_all.reshape(split)
    value_heads = values_all.reshape(split)
    allowed = allowed_keys(length, seq_len)
    scores = head_scores(query_heads, key_heads, allowed)
    row_max = jnp.max(scores, axis=-1, keepdims=True)
    raw_weights = jnp.exp(scores - row_max)
    row_total = jnp.sum(raw_weights, axis=-1, keepdims=True)
    probs = (raw_weights / row_total).astype(bf16)
    mixed = (
        jnp.einsum("ihqk,ikhd->iqhd", probs, value_heads, preferred_element_type=f32)
        .reshape(items, seq_len, -1)
        .astype(bf16)
    )
    attn_terms = jnp.einsum("ise,ed->isd", mixed, p["w_out"], preferred_element_type=f32)
    return attn_terms, full_one, query_heads, key_heads, value_heads, allowed, row_max, row_total, mixed


def forward_tail(rows_in, p, attn_terms):
    f32 = jnp.float32
    bf16 = jnp.bfloat16
    attn_rows = scatter_rows(attn_terms)
    middle = rows_in + attn_rows + p["b_out"]
    normed_two = layer_norm(middle, p["norm2_gain"], p["norm2_shift"]).astype(bf16)
    full_two = gather_rows(normed_two)
    hidden_pre = jnp.einsum(
        "isd,df->isf", full_two, p["w_up"], preferred_element_type=f32
    ) + p["b_up"].reshape(-1)
    hidden = jax.nn.gelu(hidden_pre, approximate=False).astype(bf16)
    ffn_terms = jnp.einsum("isf,fd->isd", hidden, p["w_down"], preferred_element_type=f32)
    ffn_rows = scatter_rows(ffn_terms)
    result = (middle + ffn_rows + p["b_down"]).astype(bf16)
    kept = dict(middle=middle, full_two=full_two, hidden_pre=hidden_pre, hidden=hidden)
    return result, kept


def backward_ffn(grad_full, k, p):
    f32 = jnp.float32
    bf16 = jnp.bfloat16
    grad_hidden = jnp.einsum("isd,fd->isf", grad_full, p["w_down"], preferred_element_type=f32)
    _, gelu_back = jax.vjp(partial(jax.nn.gelu, approximate=False), k["hidden_pre"])
    grad_pre = gelu_back(grad_hidden)[0].astype(bf16)
    back_terms = jnp.einsum("isf,df->isd", grad_pre, p["w_up"], preferred_element_type=f32)
    return grad_full, grad_pre, back_terms


def backward_mid(cotangent, back_rows, k, p):
    grad_out = cotangent.astype(jnp.float32)
    _, second_back = jax.vjp(layer_norm, k["middle"], p["norm2_gain"], p["norm2_shift"])
    grad_mid_norm, grad_gain_two, grad_shift_two = second_back(back_rows)
    grad_middle = grad_out + grad_mid_norm
    middle_full = gather_rows(grad_middle.astype(jnp.bfloat16))
    g = dict(
        grad_b_out=jnp.sum(grad_middle, axis=(0, 1)),
        grad_b_down=jnp.sum(grad_out, axis=(0, 1)),
        grad_gain_two=grad_gain_two, grad_shift_two=grad_shift_two,
    )
    return grad_middle, middle_full, g


def backward_attn(rows_in, grad_middle, middle_full, k, p):
    f32 = jnp.float32
    bf16 = jnp.bfloat16
    items, seq_len = k["full_one"].shape[:2]
    heads_here = p["w_query"].shape[1] // HEAD_DIM
    split = (items, seq_len, heads_here, HEAD_DIM)
    grad_mixed = (
        jnp.einsum("isd,ed->ise", middle_full, p["w_out"], preferred_element_type=f32)
        .astype(bf16)
        .reshape(split)
    )
    query_heads, key_heads, value_heads = k["query_heads"], k["key_heads"], k["value_heads"]
    again = head_scores(query_heads, key_heads, k["allowed"])
    probs_full = jnp.exp(again - k["row_max"]) / k["row_total"]
    probs_low = probs_full.astype(bf16)
    grad_value = (
        jnp.einsum("ihqk,iqhd->ikhd", probs_low, grad_mixed, preferred_element_type=f32)
        .astype(bf16)
        .reshape(items, seq_len, -1)
    )
    grad_probs = jnp.einsum("iqhd,ikhd->ihqk", grad_mixed, value_heads, preferred_element_type=f32)
    inner = jnp.sum(probs_full * grad_probs, axis=-1, keepdims=True)
    grad_scores = (probs_full * (grad_probs - inner)).astype(bf16)
    grad_query = (
        (
            jnp.einsum("ihqk,ikhd->iqhd", grad_scores, key_heads, preferred_element_type=f32)
            * HEAD_DIM ** (-0.5)
        )
        .astype(bf16)
        .reshape(items, seq_len, -1)
    )
    grad_key = (
        (
            jnp.einsum("ihqk,iqhd->ikhd", grad_scores, query_heads, preferred_element_type=f32)
            * HEAD_DIM ** (-0.5)
        )
        .astype(bf16)
        .reshape(items, seq_len, -1)
    )
    back_one = (
        jnp.einsum("ise,de->isd", grad_query, p["w_query"], preferred_element_type=f32)
        + jnp.einsum("ise,de->isd", grad_key, p["w_key"], preferred_element_type=f32)
        + jnp.einsum("ise,de->isd", grad_value, p["w_value"], preferred_element_type=f32)
    )
    rows_one = scatter_rows(back_one)
    _, first_back = jax.vjp(layer_norm, rows_in, p["norm1_gain"], p["norm1_shift"])
    grad_in_norm, grad_gain_one, grad_shift_one = first_back(rows_one)
    grad_inputs = (grad_middle + grad_in_norm).astype(bf16)
    g = dict(
        grad_query=grad_query, grad_key=grad_key, grad_value=grad_value,
        grad_gain_one=grad_gain_one, grad_shift_one=grad_shift_one,
    )
    return grad_inputs, g


def _body(
    tokens,
    lengths,
    w_query,
    w_key,
    w_value,
    b_query,
    b_value,
    w_out,
    b_out,
    w_up,
    b_up,
    w_down,
    b_down,
    norm1_gain,
    norm1_shift,
    norm2_gain,
    norm2_shift,
    cotangent,
):
    f32 = jnp.float32
    bf16 = jnp.bfloat16
    p = dict(
        w_query=w_query, w_key=w_key, w_value=w_value, b_query=b_query, b_value=b_value,
        w_out=w_out, b_out=b_out, w_up=w_up, b_up=b_up, w_down=w_down, b_down=b_down,
        norm1_gain=norm1_gain, norm1_shift=norm1_shift,
        norm2_gain=norm2_gain, norm2_shift=norm2_shift,
    )
    count = tokens.shape[0]
    results, kept = [], []
    for i in range(count):
        rows_in = tokens[i : i + 1].astype(f32)
        attn_terms, full_one, qh, kh, vh, allowed, row_max, row_total, mixed = forward_item(
            rows_in, lengths[i : i + 1], p
        )
        result, k = forward_tail(rows_in, p, attn_terms)
        k.update(
            full_one=full_one, query_heads=qh, key_heads=kh, value_heads=vh, allowed=allowed,
            row_max=row_max, row_total=row_total, mixed=mixed,
        )
        results.append(result)
        kept.append((rows_in, k))
    ks = [k for _, k in kept]
    cots = [
        lax.optimization_barrier((ks[i]["full_two"], cotangent[i : i + 1]))[1] for i in range(count)
    ]

    def cat(parts):
        return jnp.concatenate(parts, axis=0)

    def dp_sum(grad, dim):
        return lax.psum_scatter(
            grad.astype(bf16), "dp", scatter_dimension=dim, tiled=True
        ).astype(f32)

    grad_fulls = []
    for i in range(count):
        grad_fulls.append(gather_rows(cots[i]))
    grad_full = cat(grad_fulls)
    grad_w_down = jnp.einsum(
        "isf,isd->fd", cat([k["hidden"] for k in ks]), grad_full, preferred_element_type=f32
    )
    ffn = []
    for i in range(count):
        ffn.append(backward_ffn(grad_fulls[i], ks[i], p))
    back_terms = [f[2] for f in ffn]
    grad_w_down, back_terms[0] = lax.optimization_barrier((grad_w_down, back_terms[0]))
    sum_w_down = dp_sum(grad_w_down, 1)
    grad_pre = cat([f[1] for f in ffn])
    grad_w_up = jnp.einsum(
        "isd,isf->df", cat([k["full_two"] for k in ks]), grad_pre, preferred_element_type=f32
    )
    back_rows = []
    for i in range(count):
        back_rows.append(scatter_rows(back_terms[i]))
    grad_w_up, back_rows = lax.optimization_barrier((grad_w_up, back_rows))
    sum_w_up = dp_sum(grad_w_up, 0)

    mids = [backward_mid(cots[i], back_rows[i], ks[i], p) for i in range(count)]
    middle_fulls = [m[1] for m in mids]
    attn = [backward_attn(kept[i][0], mids[i][0], middle_fulls[i], ks[i], p) for i in range(count)]
    grad_ins = [a[0] for a in attn]
    grads = [dict(mids[i][2], **attn[i][1]) for i in range(count)]
    grad_query = cat([g["grad_query"] for g in grads])
    grad_key = cat([g["grad_key"] for g in grads])
    grad_value = cat([g["grad_value"] for g in grads])
    grad_qkv = jnp.einsum(
        "isd,ise->de",
        cat([k["full_one"] for k in ks]),
        jnp.concatenate([grad_query, grad_key, grad_value], axis=-1),
        preferred_element_type=f32,
    )
    grad_out_t = jnp.einsum(
        "isd,ise->de",
        cat(middle_fulls),
        cat([k["mixed"] for k in ks]),
        preferred_element_type=f32,
    )
    summed = dp_sum(jnp.concatenate([grad_qkv, grad_out_t], axis=1), 0)
    width = w_query.shape[1]
    sum_w_query = summed[:, :width]
    sum_w_key = summed[:, width : 2 * width]
    sum_w_value = summed[:, 2 * width : 3 * width]
    sum_w_out = summed[:, 3 * width :].T

    grad_b_up = jnp.sum(grad_pre, axis=(0, 1), dtype=f32).reshape(b_up.shape)
    grad_b_query = jnp.sum(grad_query, axis=(0, 1), dtype=f32).reshape(b_query.shape)
    grad_b_value = jnp.sum(grad_value, axis=(0, 1), dtype=f32).reshape(b_value.shape)
    biases = halving_scatter(jnp.concatenate([grad_b_up, grad_b_query, grad_b_value]), "dp", 1)
    n_up, n_q = b_up.shape[0], b_query.shape[0]
    sum_b_up = biases[:n_up]
    sum_b_query = biases[n_up : n_up + n_q]
    sum_b_value = biases[n_up + n_q :]

    names = ["grad_b_out", "grad_b_down", "grad_gain_one", "grad_shift_one", "grad_gain_two", "grad_shift_two"]
    vectors = jnp.stack([sum(g[key] for g in grads) for key in names])
    vectors = halving_scatter(halving_scatter(vectors, "dp", 1), "mp", 1)
    sum_b_out, sum_b_down, sum_gain_one, sum_shift_one, sum_gain_two, sum_shift_two = (
        vectors[j] for j in range(len(names))
    )
    return (
        jnp.concatenate(results, axis=0),
        jnp.concatenate(grad_ins, axis=0),
        sum_w_query,
        sum_w_key,
        sum_w_value,
        sum_b_query,
        sum_b_value,
        sum_w_out,
        sum_b_out,
        sum_w_up,
        sum_b_up,
        sum_w_down,
        sum_b_down,
        sum_gain_one,
        sum_shift_one,
        sum_gain_two,
        sum_shift_two,
    )


def solution(mesh):
    return jax.shard_map(
        _body,
        mesh=mesh,
        in_specs=(
            P("dp", "mp", None),
            P("dp"),
            P(None, "mp"),
            P(None, "mp"),
            P(None, "mp"),
            P("mp", None),
            P("mp", None),
            P("mp", None),
            P(),
            P(None, "mp"),
            P("mp", None),
            P("mp", None),
            P(),
            P(),
            P(),
            P(),
            P(),
            P("dp", "mp", None),
        ),
        out_specs=(
            P("dp", "mp", None),
            P("dp", "mp", None),
            P("dp", "mp"),
            P("dp", "mp"),
            P("dp", "mp"),
            P("mp", "dp"),
            P("mp", "dp"),
            P("mp", "dp"),
            P(("dp", "mp")),
            P("dp", "mp"),
            P("mp", "dp"),
            P("mp", "dp"),
            P(("dp", "mp")),
            P(("dp", "mp")),
            P(("dp", "mp")),
            P(("dp", "mp")),
            P(("dp", "mp")),
        ),
        check_vma=False,
    )
```

```python
from functools import partial

import jax
import jax.numpy as jnp
from jax import lax
from jax.sharding import PartitionSpec as P

HEAD_DIM = 128


GROUP = 0


def _pairs(n, flip):
    return [(m, m ^ flip) for m in range(n)]


def gather_rows(x, axis=1):
    n = lax.axis_size("mp")
    if n != 4:
        return lax.all_gather(x, "mp", axis=axis, tiled=True)
    rows = x.shape[axis]
    half = rows // 2
    from_x = lax.ppermute(x, "mp", _pairs(n, 1))
    from_y = lax.ppermute(x, "mp", _pairs(n, 2))
    diag_a = lax.ppermute(lax.slice_in_dim(from_y, 0, half, axis=axis), "mp", _pairs(n, 1))
    diag_b = lax.ppermute(lax.slice_in_dim(from_x, half, rows, axis=axis), "mp", _pairs(n, 2))
    return jnp.concatenate([x, from_x, from_y, diag_a, diag_b], axis=axis)


def gathered_positions(total):
    n = lax.axis_size("mp")
    places = jnp.arange(total)
    if n != 4:
        return places
    rows = total // n
    return ((lax.axis_index("mp") ^ (places // rows)) * rows) + places % rows


def scatter_rows(y, axis=1):
    n = lax.axis_size("mp")
    if n != 4:
        return lax.psum_scatter(
            y.astype(jnp.bfloat16), "mp", scatter_dimension=axis, tiled=True
        ).astype(jnp.float32)
    rows = y.shape[axis] // n
    half = rows // 2

    def part(flip, lo, hi):
        return lax.slice_in_dim(y, flip * rows + lo, flip * rows + hi, axis=axis)

    bf16 = jnp.bfloat16
    send_x = jnp.stack([part(1, 0, half), part(3, 0, half)]).astype(bf16)
    send_y = jnp.stack([part(2, half, rows), part(3, half, rows)]).astype(bf16)
    got_x = lax.ppermute(send_x, "mp", _pairs(n, 1))
    got_y = lax.ppermute(send_y, "mp", _pairs(n, 2))
    fwd_y = (got_x[1].astype(jnp.float32) + part(2, 0, half)).astype(bf16)
    fwd_x = (got_y[1].astype(jnp.float32) + part(1, half, rows)).astype(bf16)
    last_y = lax.ppermute(fwd_y, "mp", _pairs(n, 2))
    last_x = lax.ppermute(fwd_x, "mp", _pairs(n, 1))
    low = part(0, 0, half) + got_x[0].astype(jnp.float32) + last_y.astype(jnp.float32)
    high = part(0, half, rows) + got_y[0].astype(jnp.float32) + last_x.astype(jnp.float32)
    return jnp.concatenate([low, high], axis=axis)


def layer_norm(values, gain, shift):
    centre = values - jnp.mean(values, axis=-1, keepdims=True)
    spread = jnp.mean(centre * centre, axis=-1, keepdims=True)
    return centre * lax.rsqrt(spread + 1e-05) * gain + shift


def allowed_keys(lengths, seq_len):
    places = gathered_positions(seq_len)
    causal = places[None, :] <= places[:, None]
    inside = places[None, None, :] < lengths[:, None, None]
    return (causal[None] & inside)[:, None]


def head_scores(query_heads, key_heads, allowed):
    scores = jnp.einsum(
        "iqhd,ikhd->ihqk", query_heads, key_heads, preferred_element_type=jnp.float32
    ) * HEAD_DIM ** (-0.5)
    return jnp.where(allowed, scores, -1e30)


def halving_scatter(values, name, dim):
    n = lax.axis_size(name)
    if n & (n - 1):
        return lax.psum_scatter(values, name, scatter_dimension=dim, tiled=True)
    me = lax.axis_index(name)
    bit = n // 2
    while bit:
        half = values.shape[dim] // 2
        upper = (me & bit) != 0
        keep = lax.dynamic_slice_in_dim(values, jnp.where(upper, half, 0), half, axis=dim)
        give = lax.dynamic_slice_in_dim(values, jnp.where(upper, 0, half), half, axis=dim)
        values = keep + lax.ppermute(give, name, _pairs(n, bit))
        bit //= 2
    return values


def forward_item(rows_in, length, p):
    f32 = jnp.float32
    bf16 = jnp.bfloat16
    normed_one = layer_norm(rows_in, p["norm1_gain"], p["norm1_shift"]).astype(bf16)
    full_one = gather_rows(normed_one)
    items, seq_len = (full_one.shape[0], full_one.shape[1])
    heads_here = p["w_query"].shape[1] // HEAD_DIM
    split = (items, seq_len, heads_here, HEAD_DIM)

    def project(weight):
        return jnp.einsum("isd,de->ise", full_one, weight, preferred_element_type=f32)

    queries = (project(p["w_query"]) + p["b_query"].reshape(-1)).astype(bf16)
    keys_all = project(p["w_key"]).astype(bf16)
    values_all = (project(p["w_value"]) + p["b_value"].reshape(-1)).astype(bf16)
    query_heads = queries.reshape(split)
    key_heads = keys_all.reshape(split)
    value_heads = values_all.reshape(split)
    allowed = allowed_keys(length, seq_len)
    scores = head_scores(query_heads, key_heads, allowed)
    row_max = jnp.max(scores, axis=-1, keepdims=True)
    raw_weights = jnp.exp(scores - row_max)
    row_total = jnp.sum(raw_weights, axis=-1, keepdims=True)
    probs = (raw_weights / row_total).astype(bf16)
    mixed = (
        jnp.einsum("ihqk,ikhd->iqhd", probs, value_heads, preferred_element_type=f32)
        .reshape(items, seq_len, -1)
        .astype(bf16)
    )
    attn_terms = jnp.einsum("ise,ed->isd", mixed, p["w_out"], preferred_element_type=f32)
    attn_rows = scatter_rows(attn_terms)
    middle = rows_in + attn_rows + p["b_out"]
    normed_two = layer_norm(middle, p["norm2_gain"], p["norm2_shift"]).astype(bf16)
    full_two = gather_rows(normed_two)
    hidden_pre = jnp.einsum(
        "isd,df->isf", full_two, p["w_up"], preferred_element_type=f32
    ) + p["b_up"].reshape(-1)
    hidden = jax.nn.gelu(hidden_pre, approximate=False).astype(bf16)
    ffn_terms = jnp.einsum("isf,fd->isd", hidden, p["w_down"], preferred_element_type=f32)
    ffn_rows = scatter_rows(ffn_terms)
    result = (middle + ffn_rows + p["b_down"]).astype(bf16)
    kept = dict(
        full_one=full_one, query_heads=query_heads, key_heads=key_heads,
        value_heads=value_heads, allowed=allowed, row_max=row_max, row_total=row_total,
        mixed=mixed, middle=middle, full_two=full_two, hidden_pre=hidden_pre, hidden=hidden,
    )
    return result, kept


def backward_ffn(grad_full, k, p):
    f32 = jnp.float32
    bf16 = jnp.bfloat16
    grad_hidden = jnp.einsum("isd,fd->isf", grad_full, p["w_down"], preferred_element_type=f32)
    _, gelu_back = jax.vjp(partial(jax.nn.gelu, approximate=False), k["hidden_pre"])
    grad_pre = gelu_back(grad_hidden)[0].astype(bf16)
    back_terms = jnp.einsum("isf,df->isd", grad_pre, p["w_up"], preferred_element_type=f32)
    return grad_full, grad_pre, back_terms


def backward_mid(cotangent, back_rows, k, p):
    grad_out = cotangent.astype(jnp.float32)
    _, second_back = jax.vjp(layer_norm, k["middle"], p["norm2_gain"], p["norm2_shift"])
    grad_mid_norm, grad_gain_two, grad_shift_two = second_back(back_rows)
    grad_middle = grad_out + grad_mid_norm
    middle_full = gather_rows(grad_middle.astype(jnp.bfloat16))
    g = dict(
        grad_b_out=jnp.sum(grad_middle, axis=(0, 1)),
        grad_b_down=jnp.sum(grad_out, axis=(0, 1)),
        grad_gain_two=grad_gain_two, grad_shift_two=grad_shift_two,
    )
    return grad_middle, middle_full, g


def backward_attn(rows_in, grad_middle, middle_full, k, p):
    f32 = jnp.float32
    bf16 = jnp.bfloat16
    items, seq_len = k["full_one"].shape[:2]
    heads_here = p["w_query"].shape[1] // HEAD_DIM
    split = (items, seq_len, heads_here, HEAD_DIM)
    grad_mixed = (
        jnp.einsum("isd,ed->ise", middle_full, p["w_out"], preferred_element_type=f32)
        .astype(bf16)
        .reshape(split)
    )
    query_heads, key_heads, value_heads = k["query_heads"], k["key_heads"], k["value_heads"]
    again = head_scores(query_heads, key_heads, k["allowed"])
    probs_full = jnp.exp(again - k["row_max"]) / k["row_total"]
    probs_low = probs_full.astype(bf16)
    grad_value = (
        jnp.einsum("ihqk,iqhd->ikhd", probs_low, grad_mixed, preferred_element_type=f32)
        .astype(bf16)
        .reshape(items, seq_len, -1)
    )
    grad_probs = jnp.einsum("iqhd,ikhd->ihqk", grad_mixed, value_heads, preferred_element_type=f32)
    inner = jnp.sum(probs_full * grad_probs, axis=-1, keepdims=True)
    grad_scores = (probs_full * (grad_probs - inner)).astype(bf16)
    grad_query = (
        (
            jnp.einsum("ihqk,ikhd->iqhd", grad_scores, key_heads, preferred_element_type=f32)
            * HEAD_DIM ** (-0.5)
        )
        .astype(bf16)
        .reshape(items, seq_len, -1)
    )
    grad_key = (
        (
            jnp.einsum("ihqk,iqhd->ikhd", grad_scores, query_heads, preferred_element_type=f32)
            * HEAD_DIM ** (-0.5)
        )
        .astype(bf16)
        .reshape(items, seq_len, -1)
    )
    back_one = (
        jnp.einsum("ise,de->isd", grad_query, p["w_query"], preferred_element_type=f32)
        + jnp.einsum("ise,de->isd", grad_key, p["w_key"], preferred_element_type=f32)
        + jnp.einsum("ise,de->isd", grad_value, p["w_value"], preferred_element_type=f32)
    )
    rows_one = scatter_rows(back_one)
    _, first_back = jax.vjp(layer_norm, rows_in, p["norm1_gain"], p["norm1_shift"])
    grad_in_norm, grad_gain_one, grad_shift_one = first_back(rows_one)
    grad_inputs = (grad_middle + grad_in_norm).astype(bf16)
    g = dict(
        grad_query=grad_query, grad_key=grad_key, grad_value=grad_value,
        grad_gain_one=grad_gain_one, grad_shift_one=grad_shift_one,
    )
    return grad_inputs, g


def body(
    tokens,
    lengths,
    w_query,
    w_key,
    w_value,
    b_query,
    b_value,
    w_out,
    b_out,
    w_up,
    b_up,
    w_down,
    b_down,
    norm1_gain,
    norm1_shift,
    norm2_gain,
    norm2_shift,
    cotangent,
):
    f32 = jnp.float32
    bf16 = jnp.bfloat16
    p = dict(
        w_query=w_query, w_key=w_key, w_value=w_value, b_query=b_query, b_value=b_value,
        w_out=w_out, b_out=b_out, w_up=w_up, b_up=b_up, w_down=w_down, b_down=b_down,
        norm1_gain=norm1_gain, norm1_shift=norm1_shift,
        norm2_gain=norm2_gain, norm2_shift=norm2_shift,
    )
    size = GROUP or tokens.shape[0]
    count = tokens.shape[0] // size
    results, kept = [], []
    for i in range(count):
        rows_in = tokens[i * size : (i + 1) * size].astype(f32)
        result, k = forward_item(rows_in, lengths[i * size : (i + 1) * size], p)
        results.append(result)
        kept.append((rows_in, k))
    ks = [k for _, k in kept]
    cots = [
        lax.optimization_barrier((ks[i]["full_two"], cotangent[i * size : (i + 1) * size]))[1]
        for i in range(count)
    ]

    def cat(parts):
        return jnp.concatenate(parts, axis=0)

    def dp_sum(grad, dim):
        return lax.psum_scatter(
            grad.astype(bf16), "dp", scatter_dimension=dim, tiled=True
        ).astype(f32)

    grad_fulls = [gather_rows(cots[i]) for i in range(count)]
    grad_full = cat(grad_fulls)
    grad_w_down = jnp.einsum(
        "isf,isd->fd", cat([k["hidden"] for k in ks]), grad_full, preferred_element_type=f32
    )
    ffn = [backward_ffn(grad_fulls[i], ks[i], p) for i in range(count)]
    grad_w_down, back_terms = lax.optimization_barrier((grad_w_down, [f[2] for f in ffn]))
    sum_w_down = dp_sum(grad_w_down, 1)
    grad_pre = cat([f[1] for f in ffn])
    grad_w_up = jnp.einsum(
        "isd,isf->df", cat([k["full_two"] for k in ks]), grad_pre, preferred_element_type=f32
    )
    back_rows = [scatter_rows(t) for t in back_terms]
    grad_w_up, back_rows = lax.optimization_barrier((grad_w_up, back_rows))
    sum_w_up = dp_sum(grad_w_up, 0)

    mids = [backward_mid(cots[i], back_rows[i], ks[i], p) for i in range(count)]
    middle_fulls = [m[1] for m in mids]
    attn = [
        backward_attn(kept[i][0], mids[i][0], middle_fulls[i], ks[i], p) for i in range(count)
    ]
    grad_ins = [a[0] for a in attn]
    grads = [dict(mids[i][2], **attn[i][1]) for i in range(count)]
    grad_query = cat([g["grad_query"] for g in grads])
    grad_key = cat([g["grad_key"] for g in grads])
    grad_value = cat([g["grad_value"] for g in grads])
    grad_qkv = jnp.einsum(
        "isd,ise->de",
        cat([k["full_one"] for k in ks]),
        jnp.concatenate([grad_query, grad_key, grad_value], axis=-1),
        preferred_element_type=f32,
    )
    grad_out_t = jnp.einsum(
        "isd,ise->de",
        cat(middle_fulls),
        cat([k["mixed"] for k in ks]),
        preferred_element_type=f32,
    )
    summed = dp_sum(jnp.concatenate([grad_qkv, grad_out_t], axis=1), 0)
    width = w_query.shape[1]
    sum_w_query = summed[:, :width]
    sum_w_key = summed[:, width : 2 * width]
    sum_w_value = summed[:, 2 * width : 3 * width]
    sum_w_out = summed[:, 3 * width :].T

    grad_b_up = jnp.sum(grad_pre, axis=(0, 1), dtype=f32).reshape(b_up.shape)
    grad_b_query = jnp.sum(grad_query, axis=(0, 1), dtype=f32).reshape(b_query.shape)
    grad_b_value = jnp.sum(grad_value, axis=(0, 1), dtype=f32).reshape(b_value.shape)
    biases = halving_scatter(jnp.concatenate([grad_b_up, grad_b_query, grad_b_value]), "dp", 1)
    n_up, n_q = b_up.shape[0], b_query.shape[0]
    sum_b_up = biases[:n_up]
    sum_b_query = biases[n_up : n_up + n_q]
    sum_b_value = biases[n_up + n_q :]

    names = ["grad_b_out", "grad_b_down", "grad_gain_one", "grad_shift_one", "grad_gain_two", "grad_shift_two"]
    vectors = jnp.stack([sum(g[key] for g in grads) for key in names])
    vectors = halving_scatter(halving_scatter(vectors, "dp", 1), "mp", 1)
    sum_b_out, sum_b_down, sum_gain_one, sum_shift_one, sum_gain_two, sum_shift_two = (
        vectors[j] for j in range(len(names))
    )
    return (
        jnp.concatenate(results, axis=0),
        jnp.concatenate(grad_ins, axis=0),
        sum_w_query,
        sum_w_key,
        sum_w_value,
        sum_b_query,
        sum_b_value,
        sum_w_out,
        sum_b_out,
        sum_w_up,
        sum_b_up,
        sum_w_down,
        sum_b_down,
        sum_gain_one,
        sum_shift_one,
        sum_gain_two,
        sum_shift_two,
    )


def solution(mesh):
    return jax.shard_map(
        body,
        mesh=mesh,
        in_specs=(
            P("dp", "mp", None),
            P("dp"),
            P(None, "mp"),
            P(None, "mp"),
            P(None, "mp"),
            P("mp", None),
            P("mp", None),
            P("mp", None),
            P(),
            P(None, "mp"),
            P("mp", None),
            P("mp", None),
            P(),
            P(),
            P(),
            P(),
            P(),
            P("dp", "mp", None),
        ),
        out_specs=(
            P("dp", "mp", None),
            P("dp", "mp", None),
            P("dp", "mp"),
            P("dp", "mp"),
            P("dp", "mp"),
            P("mp", "dp"),
            P("mp", "dp"),
            P("mp", "dp"),
            P(("dp", "mp")),
            P("dp", "mp"),
            P("mp", "dp"),
            P("mp", "dp"),
            P(("dp", "mp")),
            P(("dp", "mp")),
            P(("dp", "mp")),
            P(("dp", "mp")),
            P(("dp", "mp")),
        ),
        check_vma=False,
    )
```

```python
from functools import partial

import jax
import jax.numpy as jnp
from jax import lax
from jax.sharding import PartitionSpec as P

HEAD_DIM = 128


def _pairs(n, flip):
    return [(m, m ^ flip) for m in range(n)]


def gather_rows(x, axis=1):
    n = lax.axis_size("mp")
    if n != 4:
        return lax.all_gather(x, "mp", axis=axis, tiled=True)
    rows = x.shape[axis]
    half = rows // 2
    from_x = lax.ppermute(x, "mp", _pairs(n, 1))
    from_y = lax.ppermute(x, "mp", _pairs(n, 2))
    diag_a = lax.ppermute(lax.slice_in_dim(from_y, 0, half, axis=axis), "mp", _pairs(n, 1))
    diag_b = lax.ppermute(lax.slice_in_dim(from_x, half, rows, axis=axis), "mp", _pairs(n, 2))
    return jnp.concatenate([x, from_x, from_y, diag_a, diag_b], axis=axis)


def gathered_positions(total):
    n = lax.axis_size("mp")
    places = jnp.arange(total)
    if n != 4:
        return places
    rows = total // n
    return ((lax.axis_index("mp") ^ (places // rows)) * rows) + places % rows


def scatter_rows(y, axis=1):
    n = lax.axis_size("mp")
    if n != 4:
        return lax.psum_scatter(
            y.astype(jnp.bfloat16), "mp", scatter_dimension=axis, tiled=True
        ).astype(jnp.float32)
    rows = y.shape[axis] // n
    half = rows // 2

    def part(flip, lo, hi):
        return lax.slice_in_dim(y, flip * rows + lo, flip * rows + hi, axis=axis)

    bf16 = jnp.bfloat16
    send_x = jnp.stack([part(1, 0, half), part(3, 0, half)]).astype(bf16)
    send_y = jnp.stack([part(2, half, rows), part(3, half, rows)]).astype(bf16)
    got_x = lax.ppermute(send_x, "mp", _pairs(n, 1))
    got_y = lax.ppermute(send_y, "mp", _pairs(n, 2))
    fwd_y = (got_x[1].astype(jnp.float32) + part(2, 0, half)).astype(bf16)
    fwd_x = (got_y[1].astype(jnp.float32) + part(1, half, rows)).astype(bf16)
    last_y = lax.ppermute(fwd_y, "mp", _pairs(n, 2))
    last_x = lax.ppermute(fwd_x, "mp", _pairs(n, 1))
    low = part(0, 0, half) + got_x[0].astype(jnp.float32) + last_y.astype(jnp.float32)
    high = part(0, half, rows) + got_y[0].astype(jnp.float32) + last_x.astype(jnp.float32)
    return jnp.concatenate([low, high], axis=axis)


def layer_norm(values, gain, shift):
    centre = values - jnp.mean(values, axis=-1, keepdims=True)
    spread = jnp.mean(centre * centre, axis=-1, keepdims=True)
    return centre * lax.rsqrt(spread + 1e-05) * gain + shift


def allowed_keys(lengths, seq_len):
    places = gathered_positions(seq_len)
    causal = places[None, :] <= places[:, None]
    inside = places[None, None, :] < lengths[:, None, None]
    return (causal[None] & inside)[:, None]


def head_scores(query_heads, key_heads, allowed):
    scores = jnp.einsum(
        "iqhd,ikhd->ihqk", query_heads, key_heads, preferred_element_type=jnp.float32
    ) * HEAD_DIM ** (-0.5)
    return jnp.where(allowed, scores, -1e30)


def halving_scatter(values, name, dim):
    n = lax.axis_size(name)
    if n & (n - 1):
        return lax.psum_scatter(values, name, scatter_dimension=dim, tiled=True)
    me = lax.axis_index(name)
    bit = n // 2
    while bit:
        half = values.shape[dim] // 2
        upper = (me & bit) != 0
        keep = lax.dynamic_slice_in_dim(values, jnp.where(upper, half, 0), half, axis=dim)
        give = lax.dynamic_slice_in_dim(values, jnp.where(upper, 0, half), half, axis=dim)
        values = keep + lax.ppermute(give, name, _pairs(n, bit))
        bit //= 2
    return values


def forward_item(rows_in, length, p, after=None):
    f32 = jnp.float32
    bf16 = jnp.bfloat16
    normed_one = layer_norm(rows_in, p["norm1_gain"], p["norm1_shift"]).astype(bf16)
    if after is not None:
        normed_one = lax.optimization_barrier((after, normed_one))[1]
    full_one = gather_rows(normed_one)
    items, seq_len = (full_one.shape[0], full_one.shape[1])
    heads_here = p["w_query"].shape[1] // HEAD_DIM
    split = (items, seq_len, heads_here, HEAD_DIM)

    def project(weight):
        return jnp.einsum("isd,de->ise", full_one, weight, preferred_element_type=f32)

    queries = (project(p["w_query"]) + p["b_query"].reshape(-1)).astype(bf16)
    keys_all = project(p["w_key"]).astype(bf16)
    values_all = (project(p["w_value"]) + p["b_value"].reshape(-1)).astype(bf16)
    query_heads = queries.reshape(split)
    key_heads = keys_all.reshape(split)
    value_heads = values_all.reshape(split)
    allowed = allowed_keys(length, seq_len)
    scores = head_scores(query_heads, key_heads, allowed)
    row_max = jnp.max(scores, axis=-1, keepdims=True)
    raw_weights = jnp.exp(scores - row_max)
    row_total = jnp.sum(raw_weights, axis=-1, keepdims=True)
    probs = (raw_weights / row_total).astype(bf16)
    mixed = (
        jnp.einsum("ihqk,ikhd->iqhd", probs, value_heads, preferred_element_type=f32)
        .reshape(items, seq_len, -1)
        .astype(bf16)
    )
    attn_terms = jnp.einsum("ise,ed->isd", mixed, p["w_out"], preferred_element_type=f32)
    attn_rows = scatter_rows(attn_terms)
    middle = rows_in + attn_rows + p["b_out"]
    normed_two = layer_norm(middle, p["norm2_gain"], p["norm2_shift"]).astype(bf16)
    full_two = gather_rows(normed_two)
    hidden_pre = jnp.einsum(
        "isd,df->isf", full_two, p["w_up"], preferred_element_type=f32
    ) + p["b_up"].reshape(-1)
    hidden = jax.nn.gelu(hidden_pre, approximate=False).astype(bf16)
    ffn_terms = jnp.einsum("isf,fd->isd", hidden, p["w_down"], preferred_element_type=f32)
    ffn_rows = scatter_rows(ffn_terms)
    result = (middle + ffn_rows + p["b_down"]).astype(bf16)
    kept = dict(
        full_one=full_one, query_heads=query_heads, key_heads=key_heads,
        value_heads=value_heads, allowed=allowed, row_max=row_max, row_total=row_total,
        mixed=mixed, middle=middle, full_two=full_two, hidden_pre=hidden_pre, hidden=hidden,
    )
    return result, kept


def backward_ffn(grad_full, k, p):
    f32 = jnp.float32
    bf16 = jnp.bfloat16
    grad_hidden = jnp.einsum("isd,fd->isf", grad_full, p["w_down"], preferred_element_type=f32)
    _, gelu_back = jax.vjp(partial(jax.nn.gelu, approximate=False), k["hidden_pre"])
    grad_pre = gelu_back(grad_hidden)[0].astype(bf16)
    back_terms = jnp.einsum("isf,df->isd", grad_pre, p["w_up"], preferred_element_type=f32)
    return grad_full, grad_pre, back_terms


def backward_mid(cotangent, back_rows, k, p):
    grad_out = cotangent.astype(jnp.float32)
    _, second_back = jax.vjp(layer_norm, k["middle"], p["norm2_gain"], p["norm2_shift"])
    grad_mid_norm, grad_gain_two, grad_shift_two = second_back(back_rows)
    grad_middle = grad_out + grad_mid_norm
    middle_full = gather_rows(grad_middle.astype(jnp.bfloat16))
    g = dict(
        grad_b_out=jnp.sum(grad_middle, axis=(0, 1)),
        grad_b_down=jnp.sum(grad_out, axis=(0, 1)),
        grad_gain_two=grad_gain_two, grad_shift_two=grad_shift_two,
    )
    return grad_middle, middle_full, g


def backward_attn(rows_in, grad_middle, middle_full, k, p):
    f32 = jnp.float32
    bf16 = jnp.bfloat16
    items, seq_len = k["full_one"].shape[:2]
    heads_here = p["w_query"].shape[1] // HEAD_DIM
    split = (items, seq_len, heads_here, HEAD_DIM)
    grad_mixed = (
        jnp.einsum("isd,ed->ise", middle_full, p["w_out"], preferred_element_type=f32)
        .astype(bf16)
        .reshape(split)
    )
    query_heads, key_heads, value_heads = k["query_heads"], k["key_heads"], k["value_heads"]
    again = head_scores(query_heads, key_heads, k["allowed"])
    probs_full = jnp.exp(again - k["row_max"]) / k["row_total"]
    probs_low = probs_full.astype(bf16)
    grad_value = (
        jnp.einsum("ihqk,iqhd->ikhd", probs_low, grad_mixed, preferred_element_type=f32)
        .astype(bf16)
        .reshape(items, seq_len, -1)
    )
    grad_probs = jnp.einsum("iqhd,ikhd->ihqk", grad_mixed, value_heads, preferred_element_type=f32)
    inner = jnp.sum(probs_full * grad_probs, axis=-1, keepdims=True)
    grad_scores = (probs_full * (grad_probs - inner)).astype(bf16)
    grad_query = (
        (
            jnp.einsum("ihqk,ikhd->iqhd", grad_scores, key_heads, preferred_element_type=f32)
            * HEAD_DIM ** (-0.5)
        )
        .astype(bf16)
        .reshape(items, seq_len, -1)
    )
    grad_key = (
        (
            jnp.einsum("ihqk,iqhd->ikhd", grad_scores, query_heads, preferred_element_type=f32)
            * HEAD_DIM ** (-0.5)
        )
        .astype(bf16)
        .reshape(items, seq_len, -1)
    )
    back_one = (
        jnp.einsum("ise,de->isd", grad_query, p["w_query"], preferred_element_type=f32)
        + jnp.einsum("ise,de->isd", grad_key, p["w_key"], preferred_element_type=f32)
        + jnp.einsum("ise,de->isd", grad_value, p["w_value"], preferred_element_type=f32)
    )
    rows_one = scatter_rows(back_one)
    _, first_back = jax.vjp(layer_norm, rows_in, p["norm1_gain"], p["norm1_shift"])
    grad_in_norm, grad_gain_one, grad_shift_one = first_back(rows_one)
    grad_inputs = (grad_middle + grad_in_norm).astype(bf16)
    g = dict(
        grad_query=grad_query, grad_key=grad_key, grad_value=grad_value,
        grad_gain_one=grad_gain_one, grad_shift_one=grad_shift_one,
    )
    return grad_inputs, g


def body(
    tokens,
    lengths,
    w_query,
    w_key,
    w_value,
    b_query,
    b_value,
    w_out,
    b_out,
    w_up,
    b_up,
    w_down,
    b_down,
    norm1_gain,
    norm1_shift,
    norm2_gain,
    norm2_shift,
    cotangent,
):
    f32 = jnp.float32
    bf16 = jnp.bfloat16
    p = dict(
        w_query=w_query, w_key=w_key, w_value=w_value, b_query=b_query, b_value=b_value,
        w_out=w_out, b_out=b_out, w_up=w_up, b_up=b_up, w_down=w_down, b_down=b_down,
        norm1_gain=norm1_gain, norm1_shift=norm1_shift,
        norm2_gain=norm2_gain, norm2_shift=norm2_shift,
    )
    count = tokens.shape[0]
    results, kept = [], []
    for i in range(count):
        rows_in = tokens[i : i + 1].astype(f32)
        after = kept[-1][1]["full_one"] if kept else None
        result, k = forward_item(rows_in, lengths[i : i + 1], p, after)
        results.append(result)
        kept.append((rows_in, k))
    ks = [k for _, k in kept]
    cots = [
        lax.optimization_barrier((ks[i]["full_two"], cotangent[i : i + 1]))[1] for i in range(count)
    ]

    def cat(parts):
        return jnp.concatenate(parts, axis=0)

    def dp_sum(grad, dim):
        return lax.psum_scatter(
            grad.astype(bf16), "dp", scatter_dimension=dim, tiled=True
        ).astype(f32)

    grad_fulls = [gather_rows(cots[i]) for i in range(count)]
    grad_full = cat(grad_fulls)
    grad_w_down = jnp.einsum(
        "isf,isd->fd", cat([k["hidden"] for k in ks]), grad_full, preferred_element_type=f32
    )
    ffn = [backward_ffn(grad_fulls[i], ks[i], p) for i in range(count)]
    grad_w_down, back_terms = lax.optimization_barrier((grad_w_down, [f[2] for f in ffn]))
    sum_w_down = dp_sum(grad_w_down, 1)
    grad_pre = cat([f[1] for f in ffn])
    grad_w_up = jnp.einsum(
        "isd,isf->df", cat([k["full_two"] for k in ks]), grad_pre, preferred_element_type=f32
    )
    back_rows = [scatter_rows(t) for t in back_terms]
    grad_w_up, back_rows = lax.optimization_barrier((grad_w_up, back_rows))
    sum_w_up = dp_sum(grad_w_up, 0)

    mids = [backward_mid(cots[i], back_rows[i], ks[i], p) for i in range(count)]
    middle_fulls = [m[1] for m in mids]
    attn = [
        backward_attn(kept[i][0], mids[i][0], middle_fulls[i], ks[i], p) for i in range(count)
    ]
    grad_ins = [a[0] for a in attn]
    grads = [dict(mids[i][2], **attn[i][1]) for i in range(count)]
    grad_query = cat([g["grad_query"] for g in grads])
    grad_key = cat([g["grad_key"] for g in grads])
    grad_value = cat([g["grad_value"] for g in grads])
    grad_qkv = jnp.einsum(
        "isd,ise->de",
        cat([k["full_one"] for k in ks]),
        jnp.concatenate([grad_query, grad_key, grad_value], axis=-1),
        preferred_element_type=f32,
    )
    grad_out_t = jnp.einsum(
        "isd,ise->de",
        cat(middle_fulls),
        cat([k["mixed"] for k in ks]),
        preferred_element_type=f32,
    )
    summed = dp_sum(jnp.concatenate([grad_qkv, grad_out_t], axis=1), 0)
    width = w_query.shape[1]
    sum_w_query = summed[:, :width]
    sum_w_key = summed[:, width : 2 * width]
    sum_w_value = summed[:, 2 * width : 3 * width]
    sum_w_out = summed[:, 3 * width :].T

    grad_b_up = jnp.sum(grad_pre, axis=(0, 1), dtype=f32).reshape(b_up.shape)
    grad_b_query = jnp.sum(grad_query, axis=(0, 1), dtype=f32).reshape(b_query.shape)
    grad_b_value = jnp.sum(grad_value, axis=(0, 1), dtype=f32).reshape(b_value.shape)
    biases = halving_scatter(jnp.concatenate([grad_b_up, grad_b_query, grad_b_value]), "dp", 1)
    n_up, n_q = b_up.shape[0], b_query.shape[0]
    sum_b_up = biases[:n_up]
    sum_b_query = biases[n_up : n_up + n_q]
    sum_b_value = biases[n_up + n_q :]

    names = ["grad_b_out", "grad_b_down", "grad_gain_one", "grad_shift_one", "grad_gain_two", "grad_shift_two"]
    vectors = jnp.stack([sum(g[key] for g in grads) for key in names])
    vectors = halving_scatter(halving_scatter(vectors, "dp", 1), "mp", 1)
    sum_b_out, sum_b_down, sum_gain_one, sum_shift_one, sum_gain_two, sum_shift_two = (
        vectors[j] for j in range(len(names))
    )
    return (
        jnp.concatenate(results, axis=0),
        jnp.concatenate(grad_ins, axis=0),
        sum_w_query,
        sum_w_key,
        sum_w_value,
        sum_b_query,
        sum_b_value,
        sum_w_out,
        sum_b_out,
        sum_w_up,
        sum_b_up,
        sum_w_down,
        sum_b_down,
        sum_gain_one,
        sum_shift_one,
        sum_gain_two,
        sum_shift_two,
    )


def solution(mesh):
    return jax.shard_map(
        body,
        mesh=mesh,
        in_specs=(
            P("dp", "mp", None),
            P("dp"),
            P(None, "mp"),
            P(None, "mp"),
            P(None, "mp"),
            P("mp", None),
            P("mp", None),
            P("mp", None),
            P(),
            P(None, "mp"),
            P("mp", None),
            P("mp", None),
            P(),
            P(),
            P(),
            P(),
            P(),
            P("dp", "mp", None),
        ),
        out_specs=(
            P("dp", "mp", None),
            P("dp", "mp", None),
            P("dp", "mp"),
            P("dp", "mp"),
            P("dp", "mp"),
            P("mp", "dp"),
            P("mp", "dp"),
            P("mp", "dp"),
            P(("dp", "mp")),
            P("dp", "mp"),
            P("mp", "dp"),
            P("mp", "dp"),
            P(("dp", "mp")),
            P(("dp", "mp")),
            P(("dp", "mp")),
            P(("dp", "mp")),
            P(("dp", "mp")),
        ),
        check_vma=False,
    )
```

```python
import math
from functools import partial

import jax
import jax.numpy as jnp
from jax import lax
from jax.sharding import PartitionSpec as P

HEAD_DIM = 128


def _pairs(n, flip):
    return [(m, m ^ flip) for m in range(n)]


def gather_rows(x, axis=1):
    n = lax.axis_size("mp")
    if n != 4:
        return lax.all_gather(x, "mp", axis=axis, tiled=True)
    rows = x.shape[axis]
    half = rows // 2
    from_x = lax.ppermute(x, "mp", _pairs(n, 1))
    from_y = lax.ppermute(x, "mp", _pairs(n, 2))
    diag_a = lax.ppermute(lax.slice_in_dim(from_y, 0, half, axis=axis), "mp", _pairs(n, 1))
    diag_b = lax.ppermute(lax.slice_in_dim(from_x, half, rows, axis=axis), "mp", _pairs(n, 2))
    return jnp.concatenate([x, from_x, from_y, diag_a, diag_b], axis=axis)


def gathered_positions(total):
    n = lax.axis_size("mp")
    places = jnp.arange(total)
    if n != 4:
        return places
    rows = total // n
    return ((lax.axis_index("mp") ^ (places // rows)) * rows) + places % rows


def scatter_rows(y, axis=1):
    n = lax.axis_size("mp")
    if n != 4:
        return lax.psum_scatter(
            y.astype(jnp.bfloat16), "mp", scatter_dimension=axis, tiled=True
        ).astype(jnp.float32)
    rows = y.shape[axis] // n
    half = rows // 2

    def part(flip, lo, hi):
        return lax.slice_in_dim(y, flip * rows + lo, flip * rows + hi, axis=axis)

    bf16 = jnp.bfloat16
    send_x = jnp.stack([part(1, 0, half), part(3, 0, half)]).astype(bf16)
    send_y = jnp.stack([part(2, half, rows), part(3, half, rows)]).astype(bf16)
    got_x = lax.ppermute(send_x, "mp", _pairs(n, 1))
    got_y = lax.ppermute(send_y, "mp", _pairs(n, 2))
    fwd_y = (got_x[1].astype(jnp.float32) + part(2, 0, half)).astype(bf16)
    fwd_x = (got_y[1].astype(jnp.float32) + part(1, half, rows)).astype(bf16)
    last_y = lax.ppermute(fwd_y, "mp", _pairs(n, 2))
    last_x = lax.ppermute(fwd_x, "mp", _pairs(n, 1))
    low = part(0, 0, half) + got_x[0].astype(jnp.float32) + last_y.astype(jnp.float32)
    high = part(0, half, rows) + got_y[0].astype(jnp.float32) + last_x.astype(jnp.float32)
    return jnp.concatenate([low, high], axis=axis)


def layer_norm(values, gain, shift):
    centre = values - jnp.mean(values, axis=-1, keepdims=True)
    spread = jnp.mean(centre * centre, axis=-1, keepdims=True)
    return centre * lax.rsqrt(spread + 1e-05) * gain + shift


def allowed_keys(lengths, seq_len):
    places = gathered_positions(seq_len)
    causal = places[None, :] <= places[:, None]
    inside = places[None, None, :] < lengths[:, None, None]
    return (causal[None] & inside)[:, None]


def head_scores(query_heads, key_heads, allowed):
    scores = jnp.einsum(
        "iqhd,ikhd->ihqk", query_heads, key_heads, preferred_element_type=jnp.float32
    ) * HEAD_DIM ** (-0.5)
    return jnp.where(allowed, scores, -1e30)


def halving_scatter(values, name, dim):
    n = lax.axis_size(name)
    if n & (n - 1):
        return lax.psum_scatter(values, name, scatter_dimension=dim, tiled=True)
    me = lax.axis_index(name)
    bit = n // 2
    while bit:
        half = values.shape[dim] // 2
        upper = (me & bit) != 0
        keep = lax.dynamic_slice_in_dim(values, jnp.where(upper, half, 0), half, axis=dim)
        give = lax.dynamic_slice_in_dim(values, jnp.where(upper, 0, half), half, axis=dim)
        values = keep + lax.ppermute(give, name, _pairs(n, bit))
        bit //= 2
    return values


def forward_item(rows_in, length, p):
    f32 = jnp.float32
    bf16 = jnp.bfloat16
    normed_one = layer_norm(rows_in, p["norm1_gain"], p["norm1_shift"]).astype(bf16)
    full_one = gather_rows(normed_one)
    items, seq_len = (full_one.shape[0], full_one.shape[1])
    heads_here = p["w_query"].shape[1] // HEAD_DIM
    split = (items, seq_len, heads_here, HEAD_DIM)

    def project(weight):
        return jnp.einsum("isd,de->ise", full_one, weight, preferred_element_type=f32)

    queries = (project(p["w_query"]) + p["b_query"].reshape(-1)).astype(bf16)
    keys_all = project(p["w_key"]).astype(bf16)
    values_all = (project(p["w_value"]) + p["b_value"].reshape(-1)).astype(bf16)
    query_heads = queries.reshape(split)
    key_heads = keys_all.reshape(split)
    value_heads = values_all.reshape(split)
    allowed = allowed_keys(length, seq_len)
    scores = head_scores(query_heads, key_heads, allowed)
    row_max = jnp.max(scores, axis=-1, keepdims=True)
    raw_weights = jnp.exp(scores - row_max)
    row_total = jnp.sum(raw_weights, axis=-1, keepdims=True)
    probs = (raw_weights / row_total).astype(bf16)
    mixed = (
        jnp.einsum("ihqk,ikhd->iqhd", probs, value_heads, preferred_element_type=f32)
        .reshape(items, seq_len, -1)
        .astype(bf16)
    )
    attn_terms = jnp.einsum("ise,ed->isd", mixed, p["w_out"], preferred_element_type=f32)
    attn_rows = scatter_rows(attn_terms)
    middle = rows_in + attn_rows + p["b_out"]
    normed_two = layer_norm(middle, p["norm2_gain"], p["norm2_shift"]).astype(bf16)
    full_two = gather_rows(normed_two)
    hidden_pre = jnp.einsum(
        "isd,df->isf", full_two, p["w_up"], preferred_element_type=f32
    ) + p["b_up"].reshape(-1)
    normal_cdf = (lax.erf(hidden_pre * (2.0 ** -0.5)) + 1.0) * 0.5
    hidden = (hidden_pre * normal_cdf).astype(bf16)
    ffn_terms = jnp.einsum("isf,fd->isd", hidden, p["w_down"], preferred_element_type=f32)
    ffn_rows = scatter_rows(ffn_terms)
    result = (middle + ffn_rows + p["b_down"]).astype(bf16)
    kept = dict(
        full_one=full_one, query_heads=query_heads, key_heads=key_heads,
        value_heads=value_heads, allowed=allowed, row_max=row_max, row_total=row_total,
        mixed=mixed, middle=middle, full_two=full_two, hidden_pre=hidden_pre, hidden=hidden,
        normal_cdf=normal_cdf,
    )
    return result, kept


def backward_ffn(grad_full, k, p):
    f32 = jnp.float32
    bf16 = jnp.bfloat16
    grad_hidden = jnp.einsum("isd,fd->isf", grad_full, p["w_down"], preferred_element_type=f32)
    u = k["hidden_pre"]
    density = jnp.exp(u * u * -0.5) * (2.0 * math.pi) ** -0.5
    grad_pre = (grad_hidden * (k["normal_cdf"] + u * density)).astype(bf16)
    back_terms = jnp.einsum("isf,df->isd", grad_pre, p["w_up"], preferred_element_type=f32)
    return grad_full, grad_pre, back_terms


def backward_mid(cotangent, back_rows, k, p):
    grad_out = cotangent.astype(jnp.float32)
    _, second_back = jax.vjp(layer_norm, k["middle"], p["norm2_gain"], p["norm2_shift"])
    grad_mid_norm, grad_gain_two, grad_shift_two = second_back(back_rows)
    grad_middle = grad_out + grad_mid_norm
    middle_full = gather_rows(grad_middle.astype(jnp.bfloat16))
    g = dict(
        grad_b_out=jnp.sum(grad_middle, axis=(0, 1)),
        grad_b_down=jnp.sum(grad_out, axis=(0, 1)),
        grad_gain_two=grad_gain_two, grad_shift_two=grad_shift_two,
    )
    return grad_middle, middle_full, g


def backward_attn(rows_in, grad_middle, middle_full, k, p):
    f32 = jnp.float32
    bf16 = jnp.bfloat16
    items, seq_len = k["full_one"].shape[:2]
    heads_here = p["w_query"].shape[1] // HEAD_DIM
    split = (items, seq_len, heads_here, HEAD_DIM)
    grad_mixed = (
        jnp.einsum("isd,ed->ise", middle_full, p["w_out"], preferred_element_type=f32)
        .astype(bf16)
        .reshape(split)
    )
    query_heads, key_heads, value_heads = k["query_heads"], k["key_heads"], k["value_heads"]
    again = head_scores(query_heads, key_heads, k["allowed"])
    probs_full = jnp.exp(again - k["row_max"]) / k["row_total"]
    probs_low = probs_full.astype(bf16)
    grad_value = (
        jnp.einsum("ihqk,iqhd->ikhd", probs_low, grad_mixed, preferred_element_type=f32)
        .astype(bf16)
        .reshape(items, seq_len, -1)
    )
    grad_probs = jnp.einsum("iqhd,ikhd->ihqk", grad_mixed, value_heads, preferred_element_type=f32)
    inner = jnp.sum(probs_full * grad_probs, axis=-1, keepdims=True)
    grad_scores = (probs_full * (grad_probs - inner)).astype(bf16)
    grad_query = (
        (
            jnp.einsum("ihqk,ikhd->iqhd", grad_scores, key_heads, preferred_element_type=f32)
            * HEAD_DIM ** (-0.5)
        )
        .astype(bf16)
        .reshape(items, seq_len, -1)
    )
    grad_key = (
        (
            jnp.einsum("ihqk,iqhd->ikhd", grad_scores, query_heads, preferred_element_type=f32)
            * HEAD_DIM ** (-0.5)
        )
        .astype(bf16)
        .reshape(items, seq_len, -1)
    )
    back_one = (
        jnp.einsum("ise,de->isd", grad_query, p["w_query"], preferred_element_type=f32)
        + jnp.einsum("ise,de->isd", grad_key, p["w_key"], preferred_element_type=f32)
        + jnp.einsum("ise,de->isd", grad_value, p["w_value"], preferred_element_type=f32)
    )
    rows_one = scatter_rows(back_one)
    _, first_back = jax.vjp(layer_norm, rows_in, p["norm1_gain"], p["norm1_shift"])
    grad_in_norm, grad_gain_one, grad_shift_one = first_back(rows_one)
    grad_inputs = (grad_middle + grad_in_norm).astype(bf16)
    g = dict(
        grad_query=grad_query, grad_key=grad_key, grad_value=grad_value,
        grad_gain_one=grad_gain_one, grad_shift_one=grad_shift_one,
    )
    return grad_inputs, g


def body(
    tokens,
    lengths,
    w_query,
    w_key,
    w_value,
    b_query,
    b_value,
    w_out,
    b_out,
    w_up,
    b_up,
    w_down,
    b_down,
    norm1_gain,
    norm1_shift,
    norm2_gain,
    norm2_shift,
    cotangent,
):
    f32 = jnp.float32
    bf16 = jnp.bfloat16
    p = dict(
        w_query=w_query, w_key=w_key, w_value=w_value, b_query=b_query, b_value=b_value,
        w_out=w_out, b_out=b_out, w_up=w_up, b_up=b_up, w_down=w_down, b_down=b_down,
        norm1_gain=norm1_gain, norm1_shift=norm1_shift,
        norm2_gain=norm2_gain, norm2_shift=norm2_shift,
    )
    count = tokens.shape[0]
    results, kept = [], []
    for i in range(count):
        rows_in = tokens[i : i + 1].astype(f32)
        result, k = forward_item(rows_in, lengths[i : i + 1], p)
        results.append(result)
        kept.append((rows_in, k))
    ks = [k for _, k in kept]
    cots = [
        lax.optimization_barrier((ks[i]["full_two"], cotangent[i : i + 1]))[1] for i in range(count)
    ]

    def cat(parts):
        return jnp.concatenate(parts, axis=0)

    def dp_sum(grad, dim):
        return lax.psum_scatter(
            grad.astype(bf16), "dp", scatter_dimension=dim, tiled=True
        ).astype(f32)

    grad_fulls = [gather_rows(cots[i]) for i in range(count)]
    grad_full = cat(grad_fulls)
    grad_w_down = jnp.einsum(
        "isf,isd->fd", cat([k["hidden"] for k in ks]), grad_full, preferred_element_type=f32
    )
    ffn = [backward_ffn(grad_fulls[i], ks[i], p) for i in range(count)]
    grad_w_down, back_terms = lax.optimization_barrier((grad_w_down, [f[2] for f in ffn]))
    sum_w_down = dp_sum(grad_w_down, 1)
    grad_pre = cat([f[1] for f in ffn])
    grad_w_up = jnp.einsum(
        "isd,isf->df", cat([k["full_two"] for k in ks]), grad_pre, preferred_element_type=f32
    )
    back_rows = [scatter_rows(t) for t in back_terms]
    grad_w_up, back_rows = lax.optimization_barrier((grad_w_up, back_rows))
    sum_w_up = dp_sum(grad_w_up, 0)

    mids = [backward_mid(cots[i], back_rows[i], ks[i], p) for i in range(count)]
    middle_fulls = [m[1] for m in mids]
    attn = [
        backward_attn(kept[i][0], mids[i][0], middle_fulls[i], ks[i], p) for i in range(count)
    ]
    grad_ins = [a[0] for a in attn]
    grads = [dict(mids[i][2], **attn[i][1]) for i in range(count)]
    grad_query = cat([g["grad_query"] for g in grads])
    grad_key = cat([g["grad_key"] for g in grads])
    grad_value = cat([g["grad_value"] for g in grads])
    grad_qkv = jnp.einsum(
        "isd,ise->de",
        cat([k["full_one"] for k in ks]),
        jnp.concatenate([grad_query, grad_key, grad_value], axis=-1),
        preferred_element_type=f32,
    )
    grad_out_t = jnp.einsum(
        "isd,ise->de",
        cat(middle_fulls),
        cat([k["mixed"] for k in ks]),
        preferred_element_type=f32,
    )
    summed = dp_sum(jnp.concatenate([grad_qkv, grad_out_t], axis=1), 0)
    width = w_query.shape[1]
    sum_w_query = summed[:, :width]
    sum_w_key = summed[:, width : 2 * width]
    sum_w_value = summed[:, 2 * width : 3 * width]
    sum_w_out = summed[:, 3 * width :].T

    grad_b_up = jnp.sum(grad_pre, axis=(0, 1), dtype=f32).reshape(b_up.shape)
    grad_b_query = jnp.sum(grad_query, axis=(0, 1), dtype=f32).reshape(b_query.shape)
    grad_b_value = jnp.sum(grad_value, axis=(0, 1), dtype=f32).reshape(b_value.shape)
    biases = halving_scatter(jnp.concatenate([grad_b_up, grad_b_query, grad_b_value]), "dp", 1)
    n_up, n_q = b_up.shape[0], b_query.shape[0]
    sum_b_up = biases[:n_up]
    sum_b_query = biases[n_up : n_up + n_q]
    sum_b_value = biases[n_up + n_q :]

    names = ["grad_b_out", "grad_b_down", "grad_gain_one", "grad_shift_one", "grad_gain_two", "grad_shift_two"]
    vectors = jnp.stack([sum(g[key] for g in grads) for key in names])
    vectors = halving_scatter(halving_scatter(vectors, "dp", 1), "mp", 1)
    sum_b_out, sum_b_down, sum_gain_one, sum_shift_one, sum_gain_two, sum_shift_two = (
        vectors[j] for j in range(len(names))
    )
    return (
        jnp.concatenate(results, axis=0),
        jnp.concatenate(grad_ins, axis=0),
        sum_w_query,
        sum_w_key,
        sum_w_value,
        sum_b_query,
        sum_b_value,
        sum_w_out,
        sum_b_out,
        sum_w_up,
        sum_b_up,
        sum_w_down,
        sum_b_down,
        sum_gain_one,
        sum_shift_one,
        sum_gain_two,
        sum_shift_two,
    )


def solution(mesh):
    return jax.shard_map(
        body,
        mesh=mesh,
        in_specs=(
            P("dp", "mp", None),
            P("dp"),
            P(None, "mp"),
            P(None, "mp"),
            P(None, "mp"),
            P("mp", None),
            P("mp", None),
            P("mp", None),
            P(),
            P(None, "mp"),
            P("mp", None),
            P("mp", None),
            P(),
            P(),
            P(),
            P(),
            P(),
            P("dp", "mp", None),
        ),
        out_specs=(
            P("dp", "mp", None),
            P("dp", "mp", None),
            P("dp", "mp"),
            P("dp", "mp"),
            P("dp", "mp"),
            P("mp", "dp"),
            P("mp", "dp"),
            P("mp", "dp"),
            P(("dp", "mp")),
            P("dp", "mp"),
            P("mp", "dp"),
            P("mp", "dp"),
            P(("dp", "mp")),
            P(("dp", "mp")),
            P(("dp", "mp")),
            P(("dp", "mp")),
            P(("dp", "mp")),
        ),
        check_vma=False,
    )
```

```python
import math
from functools import partial

import jax
import jax.numpy as jnp
from jax import lax
from jax.sharding import PartitionSpec as P

HEAD_DIM = 128


def _pairs(n, flip):
    return [(m, m ^ flip) for m in range(n)]


def gather_rows(x, axis=1):
    n = lax.axis_size("mp")
    if n != 4:
        return lax.all_gather(x, "mp", axis=axis, tiled=True)
    rows = x.shape[axis]
    half = rows // 2
    from_x = lax.ppermute(x, "mp", _pairs(n, 1))
    from_y = lax.ppermute(x, "mp", _pairs(n, 2))
    diag_a = lax.ppermute(lax.slice_in_dim(from_y, 0, half, axis=axis), "mp", _pairs(n, 1))
    diag_b = lax.ppermute(lax.slice_in_dim(from_x, half, rows, axis=axis), "mp", _pairs(n, 2))
    return jnp.concatenate([x, from_x, from_y, diag_a, diag_b], axis=axis)


def gathered_positions(total):
    n = lax.axis_size("mp")
    places = jnp.arange(total)
    if n != 4:
        return places
    rows = total // n
    return ((lax.axis_index("mp") ^ (places // rows)) * rows) + places % rows


def scatter_rows(y, axis=1):
    n = lax.axis_size("mp")
    if n != 4:
        return lax.psum_scatter(
            y.astype(jnp.bfloat16), "mp", scatter_dimension=axis, tiled=True
        ).astype(jnp.float32)
    rows = y.shape[axis] // n
    half = rows // 2

    def part(flip, lo, hi):
        return lax.slice_in_dim(y, flip * rows + lo, flip * rows + hi, axis=axis)

    bf16 = jnp.bfloat16
    send_x = jnp.stack([part(1, 0, half), part(3, 0, half)]).astype(bf16)
    send_y = jnp.stack([part(2, half, rows), part(3, half, rows)]).astype(bf16)
    got_x = lax.ppermute(send_x, "mp", _pairs(n, 1))
    got_y = lax.ppermute(send_y, "mp", _pairs(n, 2))
    fwd_y = (got_x[1].astype(jnp.float32) + part(2, 0, half)).astype(bf16)
    fwd_x = (got_y[1].astype(jnp.float32) + part(1, half, rows)).astype(bf16)
    last_y = lax.ppermute(fwd_y, "mp", _pairs(n, 2))
    last_x = lax.ppermute(fwd_x, "mp", _pairs(n, 1))
    low = part(0, 0, half) + got_x[0].astype(jnp.float32) + last_y.astype(jnp.float32)
    high = part(0, half, rows) + got_y[0].astype(jnp.float32) + last_x.astype(jnp.float32)
    return jnp.concatenate([low, high], axis=axis)


def pairwise_scatter(values, name):
    n = lax.axis_size(name)
    if n & (n - 1):
        return lax.psum_scatter(
            values.astype(jnp.bfloat16), name, scatter_dimension=0, tiled=True
        ).astype(jnp.float32)
    bits = n.bit_length() - 1
    rows = values.shape[0] // n
    rest = values.shape[1:]
    order = values.reshape((2,) * bits + (rows,) + rest)
    order = order.transpose(tuple(reversed(range(bits))) + tuple(range(bits, order.ndim)))
    values = order.reshape((n * rows,) + rest)
    me = lax.axis_index(name)
    bit = 1
    while bit < n:
        half = values.shape[0] // 2
        upper = (me & bit) != 0
        keep = lax.dynamic_slice_in_dim(values, jnp.where(upper, half, 0), half, axis=0)
        give = lax.dynamic_slice_in_dim(values, jnp.where(upper, 0, half), half, axis=0)
        got = lax.ppermute(give.astype(jnp.bfloat16), name, _pairs(n, bit))
        values = keep + got.astype(jnp.float32)
        bit *= 2
    return values


def layer_norm(values, gain, shift):
    centre = values - jnp.mean(values, axis=-1, keepdims=True)
    spread = jnp.mean(centre * centre, axis=-1, keepdims=True)
    return centre * lax.rsqrt(spread + 1e-05) * gain + shift


def allowed_keys(lengths, seq_len):
    places = gathered_positions(seq_len)
    causal = places[None, :] <= places[:, None]
    inside = places[None, None, :] < lengths[:, None, None]
    return (causal[None] & inside)[:, None]


def head_scores(query_heads, key_heads, allowed):
    scores = jnp.einsum(
        "iqhd,ikhd->ihqk", query_heads, key_heads, preferred_element_type=jnp.float32
    ) * HEAD_DIM ** (-0.5)
    return jnp.where(allowed, scores, -1e30)


def halving_scatter(values, name, dim):
    n = lax.axis_size(name)
    if n & (n - 1):
        return lax.psum_scatter(values, name, scatter_dimension=dim, tiled=True)
    me = lax.axis_index(name)
    bit = n // 2
    while bit:
        half = values.shape[dim] // 2
        upper = (me & bit) != 0
        keep = lax.dynamic_slice_in_dim(values, jnp.where(upper, half, 0), half, axis=dim)
        give = lax.dynamic_slice_in_dim(values, jnp.where(upper, 0, half), half, axis=dim)
        values = keep + lax.ppermute(give, name, _pairs(n, bit))
        bit //= 2
    return values


def forward_item(rows_in, length, p):
    f32 = jnp.float32
    bf16 = jnp.bfloat16
    normed_one = layer_norm(rows_in, p["norm1_gain"], p["norm1_shift"]).astype(bf16)
    full_one = gather_rows(normed_one)
    items, seq_len = (full_one.shape[0], full_one.shape[1])
    heads_here = p["w_query"].shape[1] // HEAD_DIM
    split = (items, seq_len, heads_here, HEAD_DIM)

    def project(weight):
        return jnp.einsum("isd,de->ise", full_one, weight, preferred_element_type=f32)

    queries = (project(p["w_query"]) + p["b_query"].reshape(-1)).astype(bf16)
    keys_all = project(p["w_key"]).astype(bf16)
    values_all = (project(p["w_value"]) + p["b_value"].reshape(-1)).astype(bf16)
    query_heads = queries.reshape(split)
    key_heads = keys_all.reshape(split)
    value_heads = values_all.reshape(split)
    allowed = allowed_keys(length, seq_len)
    scores = head_scores(query_heads, key_heads, allowed)
    row_max = jnp.max(scores, axis=-1, keepdims=True)
    raw_weights = jnp.exp(scores - row_max)
    row_total = jnp.sum(raw_weights, axis=-1, keepdims=True)
    probs = (raw_weights / row_total).astype(bf16)
    mixed = (
        jnp.einsum("ihqk,ikhd->iqhd", probs, value_heads, preferred_element_type=f32)
        .reshape(items, seq_len, -1)
        .astype(bf16)
    )
    attn_terms = jnp.einsum("ise,ed->isd", mixed, p["w_out"], preferred_element_type=f32)
    attn_rows = scatter_rows(attn_terms)
    middle = rows_in + attn_rows + p["b_out"]
    normed_two = layer_norm(middle, p["norm2_gain"], p["norm2_shift"]).astype(bf16)
    full_two = gather_rows(normed_two)
    hidden_pre = jnp.einsum(
        "isd,df->isf", full_two, p["w_up"], preferred_element_type=f32
    ) + p["b_up"].reshape(-1)
    normal_cdf = (lax.erf(hidden_pre * (2.0 ** -0.5)) + 1.0) * 0.5
    hidden = (hidden_pre * normal_cdf).astype(bf16)
    ffn_terms = jnp.einsum("isf,fd->isd", hidden, p["w_down"], preferred_element_type=f32)
    ffn_rows = scatter_rows(ffn_terms)
    result = (middle + ffn_rows + p["b_down"]).astype(bf16)
    kept = dict(
        full_one=full_one, query_heads=query_heads, key_heads=key_heads,
        value_heads=value_heads, allowed=allowed, row_max=row_max, row_total=row_total,
        mixed=mixed, middle=middle, full_two=full_two, hidden_pre=hidden_pre, hidden=hidden,
        normal_cdf=normal_cdf,
    )
    return result, kept


def backward_ffn(grad_full, k, p):
    f32 = jnp.float32
    bf16 = jnp.bfloat16
    grad_hidden = jnp.einsum("isd,fd->isf", grad_full, p["w_down"], preferred_element_type=f32)
    u = k["hidden_pre"]
    density = jnp.exp(u * u * -0.5) * (2.0 * math.pi) ** -0.5
    grad_pre = (grad_hidden * (k["normal_cdf"] + u * density)).astype(bf16)
    back_terms = jnp.einsum("isf,df->isd", grad_pre, p["w_up"], preferred_element_type=f32)
    return grad_full, grad_pre, back_terms


def backward_mid(cotangent, back_rows, k, p):
    grad_out = cotangent.astype(jnp.float32)
    _, second_back = jax.vjp(layer_norm, k["middle"], p["norm2_gain"], p["norm2_shift"])
    grad_mid_norm, grad_gain_two, grad_shift_two = second_back(back_rows)
    grad_middle = grad_out + grad_mid_norm
    middle_full = gather_rows(grad_middle.astype(jnp.bfloat16))
    g = dict(
        grad_b_out=jnp.sum(grad_middle, axis=(0, 1)),
        grad_b_down=jnp.sum(grad_out, axis=(0, 1)),
        grad_gain_two=grad_gain_two, grad_shift_two=grad_shift_two,
    )
    return grad_middle, middle_full, g


def backward_attn(rows_in, grad_middle, middle_full, k, p):
    f32 = jnp.float32
    bf16 = jnp.bfloat16
    items, seq_len = k["full_one"].shape[:2]
    heads_here = p["w_query"].shape[1] // HEAD_DIM
    split = (items, seq_len, heads_here, HEAD_DIM)
    grad_mixed = (
        jnp.einsum("isd,ed->ise", middle_full, p["w_out"], preferred_element_type=f32)
        .astype(bf16)
        .reshape(split)
    )
    query_heads, key_heads, value_heads = k["query_heads"], k["key_heads"], k["value_heads"]
    again = head_scores(query_heads, key_heads, k["allowed"])
    probs_full = jnp.exp(again - k["row_max"]) / k["row_total"]
    probs_low = probs_full.astype(bf16)
    grad_value = (
        jnp.einsum("ihqk,iqhd->ikhd", probs_low, grad_mixed, preferred_element_type=f32)
        .astype(bf16)
        .reshape(items, seq_len, -1)
    )
    grad_probs = jnp.einsum("iqhd,ikhd->ihqk", grad_mixed, value_heads, preferred_element_type=f32)
    inner = jnp.sum(probs_full * grad_probs, axis=-1, keepdims=True)
    grad_scores = (probs_full * (grad_probs - inner)).astype(bf16)
    grad_query = (
        (
            jnp.einsum("ihqk,ikhd->iqhd", grad_scores, key_heads, preferred_element_type=f32)
            * HEAD_DIM ** (-0.5)
        )
        .astype(bf16)
        .reshape(items, seq_len, -1)
    )
    grad_key = (
        (
            jnp.einsum("ihqk,iqhd->ikhd", grad_scores, query_heads, preferred_element_type=f32)
            * HEAD_DIM ** (-0.5)
        )
        .astype(bf16)
        .reshape(items, seq_len, -1)
    )
    back_one = (
        jnp.einsum("ise,de->isd", grad_query, p["w_query"], preferred_element_type=f32)
        + jnp.einsum("ise,de->isd", grad_key, p["w_key"], preferred_element_type=f32)
        + jnp.einsum("ise,de->isd", grad_value, p["w_value"], preferred_element_type=f32)
    )
    rows_one = scatter_rows(back_one)
    _, first_back = jax.vjp(layer_norm, rows_in, p["norm1_gain"], p["norm1_shift"])
    grad_in_norm, grad_gain_one, grad_shift_one = first_back(rows_one)
    grad_inputs = (grad_middle + grad_in_norm).astype(bf16)
    g = dict(
        grad_query=grad_query, grad_key=grad_key, grad_value=grad_value,
        grad_gain_one=grad_gain_one, grad_shift_one=grad_shift_one,
    )
    return grad_inputs, g


def body(
    tokens,
    lengths,
    w_query,
    w_key,
    w_value,
    b_query,
    b_value,
    w_out,
    b_out,
    w_up,
    b_up,
    w_down,
    b_down,
    norm1_gain,
    norm1_shift,
    norm2_gain,
    norm2_shift,
    cotangent,
):
    f32 = jnp.float32
    bf16 = jnp.bfloat16
    p = dict(
        w_query=w_query, w_key=w_key, w_value=w_value, b_query=b_query, b_value=b_value,
        w_out=w_out, b_out=b_out, w_up=w_up, b_up=b_up, w_down=w_down, b_down=b_down,
        norm1_gain=norm1_gain, norm1_shift=norm1_shift,
        norm2_gain=norm2_gain, norm2_shift=norm2_shift,
    )
    count = tokens.shape[0]
    results, kept = [], []
    for i in range(count):
        rows_in = tokens[i : i + 1].astype(f32)
        result, k = forward_item(rows_in, lengths[i : i + 1], p)
        results.append(result)
        kept.append((rows_in, k))
    ks = [k for _, k in kept]
    cots = [
        lax.optimization_barrier((ks[i]["full_two"], cotangent[i : i + 1]))[1] for i in range(count)
    ]

    def cat(parts):
        return jnp.concatenate(parts, axis=0)

    def dp_sum(grad, dim):
        return lax.psum_scatter(
            grad.astype(bf16), "dp", scatter_dimension=dim, tiled=True
        ).astype(f32)

    grad_fulls = [gather_rows(cots[i]) for i in range(count)]
    grad_full = cat(grad_fulls)
    grad_w_down = jnp.einsum(
        "isf,isd->fd", cat([k["hidden"] for k in ks]), grad_full, preferred_element_type=f32
    )
    ffn = [backward_ffn(grad_fulls[i], ks[i], p) for i in range(count)]
    grad_w_down, back_terms = lax.optimization_barrier((grad_w_down, [f[2] for f in ffn]))
    sum_w_down = dp_sum(grad_w_down, 1)
    grad_pre = cat([f[1] for f in ffn])
    grad_w_up = jnp.einsum(
        "isd,isf->df", cat([k["full_two"] for k in ks]), grad_pre, preferred_element_type=f32
    )
    back_rows = [scatter_rows(t) for t in back_terms]
    grad_w_up, back_rows = lax.optimization_barrier((grad_w_up, back_rows))
    sum_w_up = dp_sum(grad_w_up, 0)

    mids = [backward_mid(cots[i], back_rows[i], ks[i], p) for i in range(count)]
    middle_fulls = [m[1] for m in mids]
    attn = [
        backward_attn(kept[i][0], mids[i][0], middle_fulls[i], ks[i], p) for i in range(count)
    ]
    grad_ins = [a[0] for a in attn]
    grads = [dict(mids[i][2], **attn[i][1]) for i in range(count)]
    grad_query = cat([g["grad_query"] for g in grads])
    grad_key = cat([g["grad_key"] for g in grads])
    grad_value = cat([g["grad_value"] for g in grads])
    grad_qkv = jnp.einsum(
        "isd,ise->de",
        cat([k["full_one"] for k in ks]),
        jnp.concatenate([grad_query, grad_key, grad_value], axis=-1),
        preferred_element_type=f32,
    )
    grad_out_t = jnp.einsum(
        "isd,ise->de",
        cat(middle_fulls),
        cat([k["mixed"] for k in ks]),
        preferred_element_type=f32,
    )
    width = w_query.shape[1]
    by_queue = dp_sum(grad_qkv[:, : 2 * width], 0)
    by_permute = pairwise_scatter(jnp.concatenate([grad_qkv[:, 2 * width :], grad_out_t], axis=1), "dp")
    sum_w_query = by_queue[:, :width]
    sum_w_key = by_queue[:, width:]
    sum_w_value = by_permute[:, :width]
    sum_w_out = by_permute[:, width:].T

    grad_b_up = jnp.sum(grad_pre, axis=(0, 1), dtype=f32).reshape(b_up.shape)
    grad_b_query = jnp.sum(grad_query, axis=(0, 1), dtype=f32).reshape(b_query.shape)
    grad_b_value = jnp.sum(grad_value, axis=(0, 1), dtype=f32).reshape(b_value.shape)
    biases = halving_scatter(jnp.concatenate([grad_b_up, grad_b_query, grad_b_value]), "dp", 1)
    n_up, n_q = b_up.shape[0], b_query.shape[0]
    sum_b_up = biases[:n_up]
    sum_b_query = biases[n_up : n_up + n_q]
    sum_b_value = biases[n_up + n_q :]

    names = ["grad_b_out", "grad_b_down", "grad_gain_one", "grad_shift_one", "grad_gain_two", "grad_shift_two"]
    vectors = jnp.stack([sum(g[key] for g in grads) for key in names])
    vectors = halving_scatter(halving_scatter(vectors, "dp", 1), "mp", 1)
    sum_b_out, sum_b_down, sum_gain_one, sum_shift_one, sum_gain_two, sum_shift_two = (
        vectors[j] for j in range(len(names))
    )
    return (
        jnp.concatenate(results, axis=0),
        jnp.concatenate(grad_ins, axis=0),
        sum_w_query,
        sum_w_key,
        sum_w_value,
        sum_b_query,
        sum_b_value,
        sum_w_out,
        sum_b_out,
        sum_w_up,
        sum_b_up,
        sum_w_down,
        sum_b_down,
        sum_gain_one,
        sum_shift_one,
        sum_gain_two,
        sum_shift_two,
    )


def solution(mesh):
    return jax.shard_map(
        body,
        mesh=mesh,
        in_specs=(
            P("dp", "mp", None),
            P("dp"),
            P(None, "mp"),
            P(None, "mp"),
            P(None, "mp"),
            P("mp", None),
            P("mp", None),
            P("mp", None),
            P(),
            P(None, "mp"),
            P("mp", None),
            P("mp", None),
            P(),
            P(),
            P(),
            P(),
            P(),
            P("dp", "mp", None),
        ),
        out_specs=(
            P("dp", "mp", None),
            P("dp", "mp", None),
            P("dp", "mp"),
            P("dp", "mp"),
            P("dp", "mp"),
            P("mp", "dp"),
            P("mp", "dp"),
            P("mp", "dp"),
            P(("dp", "mp")),
            P("dp", "mp"),
            P("mp", "dp"),
            P("mp", "dp"),
            P(("dp", "mp")),
            P(("dp", "mp")),
            P(("dp", "mp")),
            P(("dp", "mp")),
            P(("dp", "mp")),
        ),
        check_vma=False,
    )
```

```python
import math
from functools import partial

import jax
import jax.numpy as jnp
from jax import lax
from jax.sharding import PartitionSpec as P

HEAD_DIM = 128


def _pairs(n, flip):
    return [(m, m ^ flip) for m in range(n)]


def gather_rows(x, axis=1):
    n = lax.axis_size("mp")
    if n != 4:
        return lax.all_gather(x, "mp", axis=axis, tiled=True)
    rows = x.shape[axis]
    half = rows // 2
    from_x = lax.ppermute(x, "mp", _pairs(n, 1))
    from_y = lax.ppermute(x, "mp", _pairs(n, 2))
    diag_a = lax.ppermute(lax.slice_in_dim(from_y, 0, half, axis=axis), "mp", _pairs(n, 1))
    diag_b = lax.ppermute(lax.slice_in_dim(from_x, half, rows, axis=axis), "mp", _pairs(n, 2))
    return jnp.concatenate([x, from_x, from_y, diag_a, diag_b], axis=axis)


def gathered_positions(total):
    n = lax.axis_size("mp")
    places = jnp.arange(total)
    if n != 4:
        return places
    rows = total // n
    return ((lax.axis_index("mp") ^ (places // rows)) * rows) + places % rows


def scatter_rows(y, axis=1):
    n = lax.axis_size("mp")
    if n != 4:
        return lax.psum_scatter(
            y.astype(jnp.bfloat16), "mp", scatter_dimension=axis, tiled=True
        ).astype(jnp.float32)
    rows = y.shape[axis] // n
    half = rows // 2

    def part(flip, lo, hi):
        return lax.slice_in_dim(y, flip * rows + lo, flip * rows + hi, axis=axis)

    bf16 = jnp.bfloat16
    send_x = jnp.stack([part(1, 0, half), part(3, 0, half)]).astype(bf16)
    send_y = jnp.stack([part(2, half, rows), part(3, half, rows)]).astype(bf16)
    got_x = lax.ppermute(send_x, "mp", _pairs(n, 1))
    got_y = lax.ppermute(send_y, "mp", _pairs(n, 2))
    fwd_y = (got_x[1].astype(jnp.float32) + part(2, 0, half)).astype(bf16)
    fwd_x = (got_y[1].astype(jnp.float32) + part(1, half, rows)).astype(bf16)
    last_y = lax.ppermute(fwd_y, "mp", _pairs(n, 2))
    last_x = lax.ppermute(fwd_x, "mp", _pairs(n, 1))
    low = part(0, 0, half) + got_x[0].astype(jnp.float32) + last_y.astype(jnp.float32)
    high = part(0, half, rows) + got_y[0].astype(jnp.float32) + last_x.astype(jnp.float32)
    return jnp.concatenate([low, high], axis=axis)


def layer_norm(values, gain, shift):
    centre = values - jnp.mean(values, axis=-1, keepdims=True)
    spread = jnp.mean(centre * centre, axis=-1, keepdims=True)
    return centre * lax.rsqrt(spread + 1e-05) * gain + shift


def allowed_keys(lengths, seq_len):
    places = gathered_positions(seq_len)
    causal = places[None, :] <= places[:, None]
    inside = places[None, None, :] < lengths[:, None, None]
    return (causal[None] & inside)[:, None]


def head_scores(query_heads, key_heads, allowed):
    scores = jnp.einsum(
        "iqhd,ikhd->ihqk", query_heads, key_heads, preferred_element_type=jnp.float32
    ) * HEAD_DIM ** (-0.5)
    return jnp.where(allowed, scores, -1e30)


def halving_scatter(values, name, dim):
    n = lax.axis_size(name)
    if n & (n - 1):
        return lax.psum_scatter(values, name, scatter_dimension=dim, tiled=True)
    me = lax.axis_index(name)
    bit = n // 2
    while bit:
        half = values.shape[dim] // 2
        upper = (me & bit) != 0
        keep = lax.dynamic_slice_in_dim(values, jnp.where(upper, half, 0), half, axis=dim)
        give = lax.dynamic_slice_in_dim(values, jnp.where(upper, 0, half), half, axis=dim)
        values = keep + lax.ppermute(give, name, _pairs(n, bit))
        bit //= 2
    return values


def forward_item(rows_in, length, p):
    f32 = jnp.float32
    bf16 = jnp.bfloat16
    normed_one = layer_norm(rows_in, p["norm1_gain"], p["norm1_shift"]).astype(bf16)
    full_one = gather_rows(normed_one)
    items, seq_len = (full_one.shape[0], full_one.shape[1])
    heads_here = p["w_query"].shape[1] // HEAD_DIM
    split = (items, seq_len, heads_here, HEAD_DIM)

    def project(weight):
        return jnp.einsum("isd,de->ise", full_one, weight, preferred_element_type=f32)

    queries = (project(p["w_query"]) + p["b_query"].reshape(-1)).astype(bf16)
    keys_all = project(p["w_key"]).astype(bf16)
    values_all = (project(p["w_value"]) + p["b_value"].reshape(-1)).astype(bf16)
    query_heads = queries.reshape(split)
    key_heads = keys_all.reshape(split)
    value_heads = values_all.reshape(split)
    allowed = allowed_keys(length, seq_len)
    scores = head_scores(query_heads, key_heads, allowed)
    row_max = jnp.max(scores, axis=-1, keepdims=True)
    raw_weights = jnp.exp(scores - row_max)
    row_total = jnp.sum(raw_weights, axis=-1, keepdims=True)
    probs = (raw_weights / row_total).astype(bf16)
    mixed = (
        jnp.einsum("ihqk,ikhd->iqhd", probs, value_heads, preferred_element_type=f32)
        .reshape(items, seq_len, -1)
        .astype(bf16)
    )
    attn_terms = jnp.einsum("ise,ed->isd", mixed, p["w_out"], preferred_element_type=f32)
    attn_rows = scatter_rows(attn_terms)
    middle = rows_in + attn_rows + p["b_out"]
    normed_two = layer_norm(middle, p["norm2_gain"], p["norm2_shift"]).astype(bf16)
    full_two = gather_rows(normed_two)
    hidden_pre = jnp.einsum(
        "isd,df->isf", full_two, p["w_up"], preferred_element_type=f32
    ) + p["b_up"].reshape(-1)
    normal_cdf = (lax.erf(hidden_pre * (2.0 ** -0.5)) + 1.0) * 0.5
    hidden = (hidden_pre * normal_cdf).astype(bf16)
    ffn_terms = jnp.einsum("isf,fd->isd", hidden, p["w_down"], preferred_element_type=f32)
    ffn_rows = scatter_rows(ffn_terms)
    result = (middle + ffn_rows + p["b_down"]).astype(bf16)
    kept = dict(
        full_one=full_one, query_heads=query_heads, key_heads=key_heads,
        value_heads=value_heads, allowed=allowed, row_max=row_max, row_total=row_total,
        mixed=mixed, middle=middle, full_two=full_two, hidden_pre=hidden_pre, hidden=hidden,
        normal_cdf=normal_cdf,
    )
    return result, kept


def backward_ffn(grad_full, k, p):
    f32 = jnp.float32
    bf16 = jnp.bfloat16
    grad_hidden = jnp.einsum("isd,fd->isf", grad_full, p["w_down"], preferred_element_type=f32)
    u = k["hidden_pre"]
    density = jnp.exp(u * u * -0.5) * (2.0 * math.pi) ** -0.5
    grad_pre = (grad_hidden * (k["normal_cdf"] + u * density)).astype(bf16)
    back_terms = jnp.einsum("isf,df->isd", grad_pre, p["w_up"], preferred_element_type=f32)
    return grad_full, grad_pre, back_terms


def backward_mid(cotangent, back_rows, k, p):
    grad_out = cotangent.astype(jnp.float32)
    _, second_back = jax.vjp(layer_norm, k["middle"], p["norm2_gain"], p["norm2_shift"])
    grad_mid_norm, grad_gain_two, grad_shift_two = second_back(back_rows)
    grad_middle = grad_out + grad_mid_norm
    middle_full = gather_rows(grad_middle.astype(jnp.bfloat16))
    g = dict(
        grad_b_out=jnp.sum(grad_middle, axis=(0, 1)),
        grad_b_down=jnp.sum(grad_out, axis=(0, 1)),
        grad_gain_two=grad_gain_two, grad_shift_two=grad_shift_two,
    )
    return grad_middle, middle_full, g


def backward_attn(rows_in, grad_middle, middle_full, k, p):
    f32 = jnp.float32
    bf16 = jnp.bfloat16
    items, seq_len = k["full_one"].shape[:2]
    heads_here = p["w_query"].shape[1] // HEAD_DIM
    split = (items, seq_len, heads_here, HEAD_DIM)
    grad_mixed = (
        jnp.einsum("isd,ed->ise", middle_full, p["w_out"], preferred_element_type=f32)
        .astype(bf16)
        .reshape(split)
    )
    query_heads, key_heads, value_heads = k["query_heads"], k["key_heads"], k["value_heads"]
    again = head_scores(query_heads, key_heads, k["allowed"])
    probs_full = jnp.exp(again - k["row_max"]) / k["row_total"]
    probs_low = probs_full.astype(bf16)
    grad_value = (
        jnp.einsum("ihqk,iqhd->ikhd", probs_low, grad_mixed, preferred_element_type=f32)
        .astype(bf16)
        .reshape(items, seq_len, -1)
    )
    grad_probs = jnp.einsum("iqhd,ikhd->ihqk", grad_mixed, value_heads, preferred_element_type=f32)
    inner = jnp.sum(probs_full * grad_probs, axis=-1, keepdims=True)
    grad_scores = (probs_full * (grad_probs - inner)).astype(bf16)
    grad_query = (
        (
            jnp.einsum("ihqk,ikhd->iqhd", grad_scores, key_heads, preferred_element_type=f32)
            * HEAD_DIM ** (-0.5)
        )
        .astype(bf16)
        .reshape(items, seq_len, -1)
    )
    grad_key = (
        (
            jnp.einsum("ihqk,iqhd->ikhd", grad_scores, query_heads, preferred_element_type=f32)
            * HEAD_DIM ** (-0.5)
        )
        .astype(bf16)
        .reshape(items, seq_len, -1)
    )
    back_one = (
        jnp.einsum("ise,de->isd", grad_query, p["w_query"], preferred_element_type=f32)
        + jnp.einsum("ise,de->isd", grad_key, p["w_key"], preferred_element_type=f32)
        + jnp.einsum("ise,de->isd", grad_value, p["w_value"], preferred_element_type=f32)
    )
    g = dict(grad_query=grad_query, grad_key=grad_key, grad_value=grad_value)
    return back_one, g


def backward_first(rows_in, grad_middle, back_one, p):
    rows_one = scatter_rows(back_one)
    _, first_back = jax.vjp(layer_norm, rows_in, p["norm1_gain"], p["norm1_shift"])
    grad_in_norm, grad_gain_one, grad_shift_one = first_back(rows_one)
    grad_inputs = (grad_middle + grad_in_norm).astype(jnp.bfloat16)
    return grad_inputs, dict(grad_gain_one=grad_gain_one, grad_shift_one=grad_shift_one)


def body(
    tokens,
    lengths,
    w_query,
    w_key,
    w_value,
    b_query,
    b_value,
    w_out,
    b_out,
    w_up,
    b_up,
    w_down,
    b_down,
    norm1_gain,
    norm1_shift,
    norm2_gain,
    norm2_shift,
    cotangent,
):
    f32 = jnp.float32
    bf16 = jnp.bfloat16
    p = dict(
        w_query=w_query, w_key=w_key, w_value=w_value, b_query=b_query, b_value=b_value,
        w_out=w_out, b_out=b_out, w_up=w_up, b_up=b_up, w_down=w_down, b_down=b_down,
        norm1_gain=norm1_gain, norm1_shift=norm1_shift,
        norm2_gain=norm2_gain, norm2_shift=norm2_shift,
    )
    count = tokens.shape[0]
    results, kept = [], []
    for i in range(count):
        rows_in = tokens[i : i + 1].astype(f32)
        result, k = forward_item(rows_in, lengths[i : i + 1], p)
        results.append(result)
        kept.append((rows_in, k))
    ks = [k for _, k in kept]
    cots = [
        lax.optimization_barrier((ks[i]["full_two"], cotangent[i : i + 1]))[1] for i in range(count)
    ]

    def cat(parts):
        return jnp.concatenate(parts, axis=0)

    def dp_sum(grad, dim):
        return lax.psum_scatter(
            grad.astype(bf16), "dp", scatter_dimension=dim, tiled=True
        ).astype(f32)

    grad_fulls = [gather_rows(cots[i]) for i in range(count)]
    grad_full = cat(grad_fulls)
    grad_w_down = jnp.einsum(
        "isf,isd->fd", cat([k["hidden"] for k in ks]), grad_full, preferred_element_type=f32
    )
    ffn = [backward_ffn(grad_fulls[i], ks[i], p) for i in range(count)]
    grad_w_down, back_terms = lax.optimization_barrier((grad_w_down, [f[2] for f in ffn]))
    sum_w_down = dp_sum(grad_w_down, 1)
    grad_pre = cat([f[1] for f in ffn])
    grad_w_up = jnp.einsum(
        "isd,isf->df", cat([k["full_two"] for k in ks]), grad_pre, preferred_element_type=f32
    )
    back_rows = [scatter_rows(t) for t in back_terms]
    grad_w_up, back_rows = lax.optimization_barrier((grad_w_up, back_rows))
    sum_w_up = dp_sum(grad_w_up, 0)

    mids = [backward_mid(cots[i], back_rows[i], ks[i], p) for i in range(count)]
    middle_fulls = [m[1] for m in mids]
    attn = [
        backward_attn(kept[i][0], mids[i][0], middle_fulls[i], ks[i], p) for i in range(count)
    ]
    grads = [dict(mids[i][2], **attn[i][1]) for i in range(count)]
    grad_query = cat([g["grad_query"] for g in grads])
    grad_key = cat([g["grad_key"] for g in grads])
    grad_value = cat([g["grad_value"] for g in grads])
    grad_qkv = jnp.einsum(
        "isd,ise->de",
        cat([k["full_one"] for k in ks]),
        jnp.concatenate([grad_query, grad_key, grad_value], axis=-1),
        preferred_element_type=f32,
    )
    grad_out_t = jnp.einsum(
        "isd,ise->de",
        cat(middle_fulls),
        cat([k["mixed"] for k in ks]),
        preferred_element_type=f32,
    )
    weight_grads, back_ones = lax.optimization_barrier(
        (jnp.concatenate([grad_qkv, grad_out_t], axis=1), [a[0] for a in attn])
    )
    summed = dp_sum(weight_grads, 0)
    firsts = [
        backward_first(kept[i][0], mids[i][0], back_ones[i], p) for i in range(count)
    ]
    grad_ins = [f[0] for f in firsts]
    for i in range(count):
        grads[i].update(firsts[i][1])
    width = w_query.shape[1]
    sum_w_query = summed[:, :width]
    sum_w_key = summed[:, width : 2 * width]
    sum_w_value = summed[:, 2 * width : 3 * width]
    sum_w_out = summed[:, 3 * width :].T

    grad_b_up = jnp.sum(grad_pre, axis=(0, 1), dtype=f32).reshape(b_up.shape)
    grad_b_query = jnp.sum(grad_query, axis=(0, 1), dtype=f32).reshape(b_query.shape)
    grad_b_value = jnp.sum(grad_value, axis=(0, 1), dtype=f32).reshape(b_value.shape)
    biases = halving_scatter(jnp.concatenate([grad_b_up, grad_b_query, grad_b_value]), "dp", 1)
    n_up, n_q = b_up.shape[0], b_query.shape[0]
    sum_b_up = biases[:n_up]
    sum_b_query = biases[n_up : n_up + n_q]
    sum_b_value = biases[n_up + n_q :]

    names = ["grad_b_out", "grad_b_down", "grad_gain_one", "grad_shift_one", "grad_gain_two", "grad_shift_two"]
    vectors = jnp.stack([sum(g[key] for g in grads) for key in names])
    vectors = halving_scatter(halving_scatter(vectors, "dp", 1), "mp", 1)
    sum_b_out, sum_b_down, sum_gain_one, sum_shift_one, sum_gain_two, sum_shift_two = (
        vectors[j] for j in range(len(names))
    )
    return (
        jnp.concatenate(results, axis=0),
        jnp.concatenate(grad_ins, axis=0),
        sum_w_query,
        sum_w_key,
        sum_w_value,
        sum_b_query,
        sum_b_value,
        sum_w_out,
        sum_b_out,
        sum_w_up,
        sum_b_up,
        sum_w_down,
        sum_b_down,
        sum_gain_one,
        sum_shift_one,
        sum_gain_two,
        sum_shift_two,
    )


def solution(mesh):
    return jax.shard_map(
        body,
        mesh=mesh,
        in_specs=(
            P("dp", "mp", None),
            P("dp"),
            P(None, "mp"),
            P(None, "mp"),
            P(None, "mp"),
            P("mp", None),
            P("mp", None),
            P("mp", None),
            P(),
            P(None, "mp"),
            P("mp", None),
            P("mp", None),
            P(),
            P(),
            P(),
            P(),
            P(),
            P("dp", "mp", None),
        ),
        out_specs=(
            P("dp", "mp", None),
            P("dp", "mp", None),
            P("dp", "mp"),
            P("dp", "mp"),
            P("dp", "mp"),
            P("mp", "dp"),
            P("mp", "dp"),
            P("mp", "dp"),
            P(("dp", "mp")),
            P("dp", "mp"),
            P("mp", "dp"),
            P("mp", "dp"),
            P(("dp", "mp")),
            P(("dp", "mp")),
            P(("dp", "mp")),
            P(("dp", "mp")),
            P(("dp", "mp")),
        ),
        check_vma=False,
    )
```

```python
import math
from functools import partial

import jax
import jax.numpy as jnp
from jax import lax
from jax.sharding import PartitionSpec as P

HEAD_DIM = 128


def _pairs(n, flip):
    return [(m, m ^ flip) for m in range(n)]


def gather_rows(x, axis=1):
    n = lax.axis_size("mp")
    if n != 4:
        return lax.all_gather(x, "mp", axis=axis, tiled=True)
    rows = x.shape[axis]
    half = rows // 2
    from_x = lax.ppermute(x, "mp", _pairs(n, 1))
    from_y = lax.ppermute(x, "mp", _pairs(n, 2))
    diag_a = lax.ppermute(lax.slice_in_dim(from_y, 0, half, axis=axis), "mp", _pairs(n, 1))
    diag_b = lax.ppermute(lax.slice_in_dim(from_x, half, rows, axis=axis), "mp", _pairs(n, 2))
    return jnp.concatenate([x, from_x, from_y, diag_a, diag_b], axis=axis)


def gathered_positions(total):
    n = lax.axis_size("mp")
    places = jnp.arange(total)
    if n != 4:
        return places
    rows = total // n
    return ((lax.axis_index("mp") ^ (places // rows)) * rows) + places % rows


def scatter_rows(y, axis=1):
    n = lax.axis_size("mp")
    if n != 4:
        return lax.psum_scatter(
            y.astype(jnp.bfloat16), "mp", scatter_dimension=axis, tiled=True
        ).astype(jnp.float32)
    rows = y.shape[axis] // n
    half = rows // 2

    def part(flip, lo, hi):
        return lax.slice_in_dim(y, flip * rows + lo, flip * rows + hi, axis=axis)

    bf16 = jnp.bfloat16
    send_x = jnp.stack([part(1, 0, half), part(3, 0, half)]).astype(bf16)
    send_y = jnp.stack([part(2, half, rows), part(3, half, rows)]).astype(bf16)
    got_x = lax.ppermute(send_x, "mp", _pairs(n, 1))
    got_y = lax.ppermute(send_y, "mp", _pairs(n, 2))
    fwd_y = (got_x[1].astype(jnp.float32) + part(2, 0, half)).astype(bf16)
    fwd_x = (got_y[1].astype(jnp.float32) + part(1, half, rows)).astype(bf16)
    last_y = lax.ppermute(fwd_y, "mp", _pairs(n, 2))
    last_x = lax.ppermute(fwd_x, "mp", _pairs(n, 1))
    low = part(0, 0, half) + got_x[0].astype(jnp.float32) + last_y.astype(jnp.float32)
    high = part(0, half, rows) + got_y[0].astype(jnp.float32) + last_x.astype(jnp.float32)
    return jnp.concatenate([low, high], axis=axis)


def layer_norm(values, gain, shift):
    centre = values - jnp.mean(values, axis=-1, keepdims=True)
    spread = jnp.mean(centre * centre, axis=-1, keepdims=True)
    return centre * lax.rsqrt(spread + 1e-05) * gain + shift


def allowed_keys(lengths, seq_len):
    places = gathered_positions(seq_len)
    causal = places[None, :] <= places[:, None]
    inside = places[None, None, :] < lengths[:, None, None]
    return (causal[None] & inside)[:, None]


def head_scores(query_heads, key_heads, allowed):
    scores = jnp.einsum(
        "iqhd,ikhd->ihqk", query_heads, key_heads, preferred_element_type=jnp.float32
    ) * HEAD_DIM ** (-0.5)
    return jnp.where(allowed, scores, -1e30)


def halving_scatter(values, name, dim):
    n = lax.axis_size(name)
    if n & (n - 1):
        return lax.psum_scatter(values, name, scatter_dimension=dim, tiled=True)
    me = lax.axis_index(name)
    bit = n // 2
    while bit:
        half = values.shape[dim] // 2
        upper = (me & bit) != 0
        keep = lax.dynamic_slice_in_dim(values, jnp.where(upper, half, 0), half, axis=dim)
        give = lax.dynamic_slice_in_dim(values, jnp.where(upper, 0, half), half, axis=dim)
        values = keep + lax.ppermute(give, name, _pairs(n, bit))
        bit //= 2
    return values


def forward_item(rows_in, length, p):
    f32 = jnp.float32
    bf16 = jnp.bfloat16
    normed_one = layer_norm(rows_in, p["norm1_gain"], p["norm1_shift"]).astype(bf16)
    full_one = gather_rows(normed_one)
    items, seq_len = (full_one.shape[0], full_one.shape[1])
    heads_here = p["w_query"].shape[1] // HEAD_DIM
    split = (items, seq_len, heads_here, HEAD_DIM)

    def project(weight):
        return jnp.einsum("isd,de->ise", full_one, weight, preferred_element_type=f32)

    queries = (project(p["w_query"]) + p["b_query"].reshape(-1)).astype(bf16)
    keys_all = project(p["w_key"]).astype(bf16)
    values_all = (project(p["w_value"]) + p["b_value"].reshape(-1)).astype(bf16)
    query_heads = queries.reshape(split)
    key_heads = keys_all.reshape(split)
    value_heads = values_all.reshape(split)
    allowed = allowed_keys(length, seq_len)
    scores = head_scores(query_heads, key_heads, allowed)
    row_max = jnp.max(scores, axis=-1, keepdims=True)
    raw_weights = jnp.exp(scores - row_max)
    row_total = jnp.sum(raw_weights, axis=-1, keepdims=True)
    probs = (raw_weights / row_total).astype(bf16)
    mixed = (
        jnp.einsum("ihqk,ikhd->iqhd", probs, value_heads, preferred_element_type=f32)
        .reshape(items, seq_len, -1)
        .astype(bf16)
    )
    attn_terms = jnp.einsum("ise,ed->isd", mixed, p["w_out"], preferred_element_type=f32)
    attn_rows = scatter_rows(attn_terms)
    middle = rows_in + attn_rows + p["b_out"]
    normed_two = layer_norm(middle, p["norm2_gain"], p["norm2_shift"]).astype(bf16)
    full_two = gather_rows(normed_two)
    hidden_pre = jnp.einsum(
        "isd,df->isf", full_two, p["w_up"], preferred_element_type=f32
    ) + p["b_up"].reshape(-1)
    normal_cdf = (lax.erf(hidden_pre * (2.0 ** -0.5)) + 1.0) * 0.5
    hidden = (hidden_pre * normal_cdf).astype(bf16)
    ffn_terms = jnp.einsum("isf,fd->isd", hidden, p["w_down"], preferred_element_type=f32)
    ffn_rows = scatter_rows(ffn_terms)
    result = (middle + ffn_rows + p["b_down"]).astype(bf16)
    kept = dict(
        full_one=full_one, query_heads=query_heads, key_heads=key_heads,
        value_heads=value_heads, allowed=allowed, row_max=row_max, row_total=row_total,
        mixed=mixed, middle=middle, full_two=full_two, hidden_pre=hidden_pre, hidden=hidden,
        normal_cdf=normal_cdf,
    )
    return result, kept


def backward_ffn(grad_full, k, p):
    f32 = jnp.float32
    bf16 = jnp.bfloat16
    grad_hidden = jnp.einsum("isd,fd->isf", grad_full, p["w_down"], preferred_element_type=f32)
    u = k["hidden_pre"]
    density = jnp.exp(u * u * -0.5) * (2.0 * math.pi) ** -0.5
    grad_pre = (grad_hidden * (k["normal_cdf"] + u * density)).astype(bf16)
    back_terms = jnp.einsum("isf,df->isd", grad_pre, p["w_up"], preferred_element_type=f32)
    return grad_full, grad_pre, back_terms


def backward_mid(cotangent, back_rows, k, p):
    grad_out = cotangent.astype(jnp.float32)
    _, second_back = jax.vjp(layer_norm, k["middle"], p["norm2_gain"], p["norm2_shift"])
    grad_mid_norm, grad_gain_two, grad_shift_two = second_back(back_rows)
    grad_middle = grad_out + grad_mid_norm
    middle_full = gather_rows(grad_middle.astype(jnp.bfloat16))
    g = dict(
        grad_b_out=jnp.sum(grad_middle, axis=(0, 1)),
        grad_b_down=jnp.sum(grad_out, axis=(0, 1)),
        grad_gain_two=grad_gain_two, grad_shift_two=grad_shift_two,
    )
    return grad_middle, middle_full, g


def backward_attn(rows_in, grad_middle, middle_full, k, p):
    f32 = jnp.float32
    bf16 = jnp.bfloat16
    items, seq_len = k["full_one"].shape[:2]
    heads_here = p["w_query"].shape[1] // HEAD_DIM
    split = (items, seq_len, heads_here, HEAD_DIM)
    grad_mixed = (
        jnp.einsum("isd,ed->ise", middle_full, p["w_out"], preferred_element_type=f32)
        .astype(bf16)
        .reshape(split)
    )
    query_heads, key_heads, value_heads = k["query_heads"], k["key_heads"], k["value_heads"]
    again = head_scores(query_heads, key_heads, k["allowed"])
    probs_full = jnp.exp(again - k["row_max"]) / k["row_total"]
    probs_low = probs_full.astype(bf16)
    grad_value = (
        jnp.einsum("ihqk,iqhd->ikhd", probs_low, grad_mixed, preferred_element_type=f32)
        .astype(bf16)
        .reshape(items, seq_len, -1)
    )
    grad_probs = jnp.einsum("iqhd,ikhd->ihqk", grad_mixed, value_heads, preferred_element_type=f32)
    inner = jnp.sum(probs_full * grad_probs, axis=-1, keepdims=True)
    grad_scores = (probs_full * (grad_probs - inner)).astype(bf16)
    grad_query = (
        (
            jnp.einsum("ihqk,ikhd->iqhd", grad_scores, key_heads, preferred_element_type=f32)
            * HEAD_DIM ** (-0.5)
        )
        .astype(bf16)
        .reshape(items, seq_len, -1)
    )
    grad_key = (
        (
            jnp.einsum("ihqk,iqhd->ikhd", grad_scores, query_heads, preferred_element_type=f32)
            * HEAD_DIM ** (-0.5)
        )
        .astype(bf16)
        .reshape(items, seq_len, -1)
    )
    back_one = (
        jnp.einsum("ise,de->isd", grad_query, p["w_query"], preferred_element_type=f32)
        + jnp.einsum("ise,de->isd", grad_key, p["w_key"], preferred_element_type=f32)
        + jnp.einsum("ise,de->isd", grad_value, p["w_value"], preferred_element_type=f32)
    )
    rows_one = scatter_rows(back_one)
    _, first_back = jax.vjp(layer_norm, rows_in, p["norm1_gain"], p["norm1_shift"])
    grad_in_norm, grad_gain_one, grad_shift_one = first_back(rows_one)
    grad_inputs = (grad_middle + grad_in_norm).astype(bf16)
    g = dict(
        grad_query=grad_query, grad_key=grad_key, grad_value=grad_value,
        grad_gain_one=grad_gain_one, grad_shift_one=grad_shift_one,
    )
    return grad_inputs, g


def body(
    tokens,
    lengths,
    w_query,
    w_key,
    w_value,
    b_query,
    b_value,
    w_out,
    b_out,
    w_up,
    b_up,
    w_down,
    b_down,
    norm1_gain,
    norm1_shift,
    norm2_gain,
    norm2_shift,
    cotangent,
):
    f32 = jnp.float32
    bf16 = jnp.bfloat16
    p = dict(
        w_query=w_query, w_key=w_key, w_value=w_value, b_query=b_query, b_value=b_value,
        w_out=w_out, b_out=b_out, w_up=w_up, b_up=b_up, w_down=w_down, b_down=b_down,
        norm1_gain=norm1_gain, norm1_shift=norm1_shift,
        norm2_gain=norm2_gain, norm2_shift=norm2_shift,
    )
    count = tokens.shape[0]
    results, kept = [], []
    for i in range(count):
        rows_in = tokens[i : i + 1].astype(f32)
        result, k = forward_item(rows_in, lengths[i : i + 1], p)
        results.append(result)
        kept.append((rows_in, k))
    ks = [k for _, k in kept]
    cots = [
        lax.optimization_barrier((ks[i]["full_two"], cotangent[i : i + 1]))[1] for i in range(count)
    ]

    def cat(parts):
        return jnp.concatenate(parts, axis=0)

    def dp_sum(grad, dim):
        return lax.psum_scatter(
            grad.astype(bf16), "dp", scatter_dimension=dim, tiled=True
        ).astype(f32)

    grad_fulls = [gather_rows(cots[i]) for i in range(count)]
    grad_full = cat(grad_fulls)
    grad_w_down = jnp.einsum(
        "isf,isd->fd", cat([k["hidden"] for k in ks]), grad_full, preferred_element_type=f32
    )
    ffn = [backward_ffn(grad_fulls[i], ks[i], p) for i in range(count)]
    back_terms = [f[2] for f in ffn]
    grad_w_down, back_terms[-1] = lax.optimization_barrier((grad_w_down, back_terms[-1]))
    sum_w_down = dp_sum(grad_w_down, 1)
    grad_pre = cat([f[1] for f in ffn])
    grad_w_up = jnp.einsum(
        "isd,isf->df", cat([k["full_two"] for k in ks]), grad_pre, preferred_element_type=f32
    )
    back_rows = [scatter_rows(t) for t in back_terms]
    grad_w_up, back_rows = lax.optimization_barrier((grad_w_up, back_rows))
    sum_w_up = dp_sum(grad_w_up, 0)

    mids = [backward_mid(cots[i], back_rows[i], ks[i], p) for i in range(count)]
    middle_fulls = [m[1] for m in mids]
    attn = [
        backward_attn(kept[i][0], mids[i][0], middle_fulls[i], ks[i], p) for i in range(count)
    ]
    grad_ins = [a[0] for a in attn]
    grads = [dict(mids[i][2], **attn[i][1]) for i in range(count)]
    grad_query = cat([g["grad_query"] for g in grads])
    grad_key = cat([g["grad_key"] for g in grads])
    grad_value = cat([g["grad_value"] for g in grads])
    grad_qkv = jnp.einsum(
        "isd,ise->de",
        cat([k["full_one"] for k in ks]),
        jnp.concatenate([grad_query, grad_key, grad_value], axis=-1),
        preferred_element_type=f32,
    )
    grad_out_t = jnp.einsum(
        "isd,ise->de",
        cat(middle_fulls),
        cat([k["mixed"] for k in ks]),
        preferred_element_type=f32,
    )
    summed = dp_sum(jnp.concatenate([grad_qkv, grad_out_t], axis=1), 0)
    width = w_query.shape[1]
    sum_w_query = summed[:, :width]
    sum_w_key = summed[:, width : 2 * width]
    sum_w_value = summed[:, 2 * width : 3 * width]
    sum_w_out = summed[:, 3 * width :].T

    grad_b_up = jnp.sum(grad_pre, axis=(0, 1), dtype=f32).reshape(b_up.shape)
    grad_b_query = jnp.sum(grad_query, axis=(0, 1), dtype=f32).reshape(b_query.shape)
    grad_b_value = jnp.sum(grad_value, axis=(0, 1), dtype=f32).reshape(b_value.shape)
    biases = halving_scatter(jnp.concatenate([grad_b_up, grad_b_query, grad_b_value]), "dp", 1)
    n_up, n_q = b_up.shape[0], b_query.shape[0]
    sum_b_up = biases[:n_up]
    sum_b_query = biases[n_up : n_up + n_q]
    sum_b_value = biases[n_up + n_q :]

    names = ["grad_b_out", "grad_b_down", "grad_gain_one", "grad_shift_one", "grad_gain_two", "grad_shift_two"]
    vectors = jnp.stack([sum(g[key] for g in grads) for key in names])
    vectors = halving_scatter(halving_scatter(vectors, "dp", 1), "mp", 1)
    sum_b_out, sum_b_down, sum_gain_one, sum_shift_one, sum_gain_two, sum_shift_two = (
        vectors[j] for j in range(len(names))
    )
    return (
        jnp.concatenate(results, axis=0),
        jnp.concatenate(grad_ins, axis=0),
        sum_w_query,
        sum_w_key,
        sum_w_value,
        sum_b_query,
        sum_b_value,
        sum_w_out,
        sum_b_out,
        sum_w_up,
        sum_b_up,
        sum_w_down,
        sum_b_down,
        sum_gain_one,
        sum_shift_one,
        sum_gain_two,
        sum_shift_two,
    )


def solution(mesh):
    return jax.shard_map(
        body,
        mesh=mesh,
        in_specs=(
            P("dp", "mp", None),
            P("dp"),
            P(None, "mp"),
            P(None, "mp"),
            P(None, "mp"),
            P("mp", None),
            P("mp", None),
            P("mp", None),
            P(),
            P(None, "mp"),
            P("mp", None),
            P("mp", None),
            P(),
            P(),
            P(),
            P(),
            P(),
            P("dp", "mp", None),
        ),
        out_specs=(
            P("dp", "mp", None),
            P("dp", "mp", None),
            P("dp", "mp"),
            P("dp", "mp"),
            P("dp", "mp"),
            P("mp", "dp"),
            P("mp", "dp"),
            P("mp", "dp"),
            P(("dp", "mp")),
            P("dp", "mp"),
            P("mp", "dp"),
            P("mp", "dp"),
            P(("dp", "mp")),
            P(("dp", "mp")),
            P(("dp", "mp")),
            P(("dp", "mp")),
            P(("dp", "mp")),
        ),
        check_vma=False,
    )
```

```python
import math
from functools import partial

import jax
import jax.numpy as jnp
from jax import lax
from jax.sharding import PartitionSpec as P

HEAD_DIM = 128


def _pairs(n, flip):
    return [(m, m ^ flip) for m in range(n)]


def gather_rows(x, axis=1):
    n = lax.axis_size("mp")
    if n != 4:
        return lax.all_gather(x, "mp", axis=axis, tiled=True)
    rows = x.shape[axis]
    half = rows // 2
    from_x = lax.ppermute(x, "mp", _pairs(n, 1))
    from_y = lax.ppermute(x, "mp", _pairs(n, 2))
    diag_a = lax.ppermute(lax.slice_in_dim(from_y, 0, half, axis=axis), "mp", _pairs(n, 1))
    diag_b = lax.ppermute(lax.slice_in_dim(from_x, half, rows, axis=axis), "mp", _pairs(n, 2))
    return jnp.concatenate([x, from_x, from_y, diag_a, diag_b], axis=axis)


def gathered_positions(total):
    n = lax.axis_size("mp")
    places = jnp.arange(total)
    if n != 4:
        return places
    rows = total // n
    return ((lax.axis_index("mp") ^ (places // rows)) * rows) + places % rows


def scatter_rows(y, axis=1):
    n = lax.axis_size("mp")
    if n != 4:
        return lax.psum_scatter(
            y.astype(jnp.bfloat16), "mp", scatter_dimension=axis, tiled=True
        ).astype(jnp.float32)
    rows = y.shape[axis] // n
    half = rows // 2

    def part(flip, lo, hi):
        return lax.slice_in_dim(y, flip * rows + lo, flip * rows + hi, axis=axis)

    bf16 = jnp.bfloat16
    send_x = jnp.stack([part(1, 0, half), part(3, 0, half)]).astype(bf16)
    send_y = jnp.stack([part(2, half, rows), part(3, half, rows)]).astype(bf16)
    got_x = lax.ppermute(send_x, "mp", _pairs(n, 1))
    got_y = lax.ppermute(send_y, "mp", _pairs(n, 2))
    fwd_y = (got_x[1].astype(jnp.float32) + part(2, 0, half)).astype(bf16)
    fwd_x = (got_y[1].astype(jnp.float32) + part(1, half, rows)).astype(bf16)
    last_y = lax.ppermute(fwd_y, "mp", _pairs(n, 2))
    last_x = lax.ppermute(fwd_x, "mp", _pairs(n, 1))
    low = part(0, 0, half) + got_x[0].astype(jnp.float32) + last_y.astype(jnp.float32)
    high = part(0, half, rows) + got_y[0].astype(jnp.float32) + last_x.astype(jnp.float32)
    return jnp.concatenate([low, high], axis=axis)


def layer_norm(values, gain, shift):
    centre = values - jnp.mean(values, axis=-1, keepdims=True)
    spread = jnp.mean(centre * centre, axis=-1, keepdims=True)
    return centre * lax.rsqrt(spread + 1e-05) * gain + shift


def allowed_keys(lengths, seq_len):
    places = gathered_positions(seq_len)
    causal = places[None, :] <= places[:, None]
    inside = places[None, None, :] < lengths[:, None, None]
    return (causal[None] & inside)[:, None]


def head_scores(query_heads, key_heads, allowed):
    scores = jnp.einsum(
        "iqhd,ikhd->ihqk", query_heads, key_heads, preferred_element_type=jnp.float32
    ) * HEAD_DIM ** (-0.5)
    return jnp.where(allowed, scores, -1e30)


def halving_scatter(values, name, dim):
    n = lax.axis_size(name)
    if n & (n - 1):
        return lax.psum_scatter(values, name, scatter_dimension=dim, tiled=True)
    me = lax.axis_index(name)
    bit = n // 2
    while bit:
        half = values.shape[dim] // 2
        upper = (me & bit) != 0
        keep = lax.dynamic_slice_in_dim(values, jnp.where(upper, half, 0), half, axis=dim)
        give = lax.dynamic_slice_in_dim(values, jnp.where(upper, 0, half), half, axis=dim)
        values = keep + lax.ppermute(give, name, _pairs(n, bit))
        bit //= 2
    return values


def forward_item(rows_in, length, p):
    f32 = jnp.float32
    bf16 = jnp.bfloat16
    normed_one = layer_norm(rows_in, p["norm1_gain"], p["norm1_shift"]).astype(bf16)
    full_one = gather_rows(normed_one)
    items, seq_len = (full_one.shape[0], full_one.shape[1])
    heads_here = p["w_query"].shape[1] // HEAD_DIM
    split = (items, seq_len, heads_here, HEAD_DIM)

    def project(weight):
        return jnp.einsum("isd,de->ise", full_one, weight, preferred_element_type=f32)

    queries = (project(p["w_query"]) + p["b_query"].reshape(-1)).astype(bf16)
    keys_all = project(p["w_key"]).astype(bf16)
    values_all = (project(p["w_value"]) + p["b_value"].reshape(-1)).astype(bf16)
    query_heads = queries.reshape(split)
    key_heads = keys_all.reshape(split)
    value_heads = values_all.reshape(split)
    allowed = allowed_keys(length, seq_len)
    scores = head_scores(query_heads, key_heads, allowed)
    row_max = jnp.max(scores, axis=-1, keepdims=True)
    raw_weights = jnp.exp(scores - row_max)
    row_total = jnp.sum(raw_weights, axis=-1, keepdims=True)
    probs = (raw_weights / row_total).astype(bf16)
    mixed = (
        jnp.einsum("ihqk,ikhd->iqhd", probs, value_heads, preferred_element_type=f32)
        .reshape(items, seq_len, -1)
        .astype(bf16)
    )
    attn_terms = jnp.einsum("ise,ed->isd", mixed, p["w_out"], preferred_element_type=f32)
    attn_rows = scatter_rows(attn_terms)
    middle = rows_in + attn_rows + p["b_out"]
    normed_two = layer_norm(middle, p["norm2_gain"], p["norm2_shift"]).astype(bf16)
    full_two = gather_rows(normed_two)
    hidden_pre = jnp.einsum(
        "isd,df->isf", full_two, p["w_up"], preferred_element_type=f32
    ) + p["b_up"].reshape(-1)
    normal_cdf = (lax.erf(hidden_pre * (2.0 ** -0.5)) + 1.0) * 0.5
    hidden = (hidden_pre * normal_cdf).astype(bf16)
    ffn_terms = jnp.einsum("isf,fd->isd", hidden, p["w_down"], preferred_element_type=f32)
    ffn_rows = scatter_rows(ffn_terms)
    result = (middle + ffn_rows + p["b_down"]).astype(bf16)
    kept = dict(
        full_one=full_one, query_heads=query_heads, key_heads=key_heads,
        value_heads=value_heads, allowed=allowed, row_max=row_max, row_total=row_total,
        mixed=mixed, middle=middle, full_two=full_two, hidden_pre=hidden_pre, hidden=hidden,
        normal_cdf=normal_cdf,
    )
    return result, kept


def backward_ffn(grad_full, k, p):
    f32 = jnp.float32
    bf16 = jnp.bfloat16
    grad_hidden = jnp.einsum("isd,fd->isf", grad_full, p["w_down"], preferred_element_type=f32)
    u = k["hidden_pre"]
    density = jnp.exp(u * u * -0.5) * (2.0 * math.pi) ** -0.5
    grad_pre = (grad_hidden * (k["normal_cdf"] + u * density)).astype(bf16)
    back_terms = jnp.einsum("isf,df->isd", grad_pre, p["w_up"], preferred_element_type=f32)
    return grad_full, grad_pre, back_terms


def backward_mid(cotangent, back_rows, k, p):
    grad_out = cotangent.astype(jnp.float32)
    _, second_back = jax.vjp(layer_norm, k["middle"], p["norm2_gain"], p["norm2_shift"])
    grad_mid_norm, grad_gain_two, grad_shift_two = second_back(back_rows)
    grad_middle = grad_out + grad_mid_norm
    middle_full = gather_rows(grad_middle.astype(jnp.bfloat16))
    g = dict(
        grad_b_out=jnp.sum(grad_middle, axis=(0, 1)),
        grad_b_down=jnp.sum(grad_out, axis=(0, 1)),
        grad_gain_two=grad_gain_two, grad_shift_two=grad_shift_two,
    )
    return grad_middle, middle_full, g


def backward_attn(rows_in, grad_middle, middle_full, k, p):
    f32 = jnp.float32
    bf16 = jnp.bfloat16
    items, seq_len = k["full_one"].shape[:2]
    heads_here = p["w_query"].shape[1] // HEAD_DIM
    split = (items, seq_len, heads_here, HEAD_DIM)
    grad_mixed = (
        jnp.einsum("isd,ed->ise", middle_full, p["w_out"], preferred_element_type=f32)
        .astype(bf16)
        .reshape(split)
    )
    query_heads, key_heads, value_heads = k["query_heads"], k["key_heads"], k["value_heads"]
    again = head_scores(query_heads, key_heads, k["allowed"])
    probs_full = jnp.exp(again - k["row_max"]) / k["row_total"]
    probs_low = probs_full.astype(bf16)
    grad_value = (
        jnp.einsum("ihqk,iqhd->ikhd", probs_low, grad_mixed, preferred_element_type=f32)
        .astype(bf16)
        .reshape(items, seq_len, -1)
    )
    grad_probs = jnp.einsum("iqhd,ikhd->ihqk", grad_mixed, value_heads, preferred_element_type=f32)
    inner = jnp.sum(probs_full * grad_probs, axis=-1, keepdims=True)
    grad_scores = (probs_full * (grad_probs - inner)).astype(bf16)
    grad_query = (
        (
            jnp.einsum("ihqk,ikhd->iqhd", grad_scores, key_heads, preferred_element_type=f32)
            * HEAD_DIM ** (-0.5)
        )
        .astype(bf16)
        .reshape(items, seq_len, -1)
    )
    grad_key = (
        (
            jnp.einsum("ihqk,iqhd->ikhd", grad_scores, query_heads, preferred_element_type=f32)
            * HEAD_DIM ** (-0.5)
        )
        .astype(bf16)
        .reshape(items, seq_len, -1)
    )
    back_one = (
        jnp.einsum("ise,de->isd", grad_query, p["w_query"], preferred_element_type=f32)
        + jnp.einsum("ise,de->isd", grad_key, p["w_key"], preferred_element_type=f32)
        + jnp.einsum("ise,de->isd", grad_value, p["w_value"], preferred_element_type=f32)
    )
    rows_one = scatter_rows(back_one)
    _, first_back = jax.vjp(layer_norm, rows_in, p["norm1_gain"], p["norm1_shift"])
    grad_in_norm, grad_gain_one, grad_shift_one = first_back(rows_one)
    grad_inputs = (grad_middle + grad_in_norm).astype(bf16)
    g = dict(
        grad_query=grad_query, grad_key=grad_key, grad_value=grad_value,
        grad_gain_one=grad_gain_one, grad_shift_one=grad_shift_one,
    )
    return grad_inputs, g


def body(
    tokens,
    lengths,
    w_query,
    w_key,
    w_value,
    b_query,
    b_value,
    w_out,
    b_out,
    w_up,
    b_up,
    w_down,
    b_down,
    norm1_gain,
    norm1_shift,
    norm2_gain,
    norm2_shift,
    cotangent,
):
    f32 = jnp.float32
    bf16 = jnp.bfloat16
    p = dict(
        w_query=w_query, w_key=w_key, w_value=w_value, b_query=b_query, b_value=b_value,
        w_out=w_out, b_out=b_out, w_up=w_up, b_up=b_up, w_down=w_down, b_down=b_down,
        norm1_gain=norm1_gain, norm1_shift=norm1_shift,
        norm2_gain=norm2_gain, norm2_shift=norm2_shift,
    )
    count = tokens.shape[0]
    results, kept = [], []
    for i in range(count):
        rows_in = tokens[i : i + 1].astype(f32)
        result, k = forward_item(rows_in, lengths[i : i + 1], p)
        results.append(result)
        kept.append((rows_in, k))
    ks = [k for _, k in kept]
    cots = [
        lax.optimization_barrier((ks[i]["full_two"], cotangent[i : i + 1]))[1] for i in range(count)
    ]

    def cat(parts):
        return jnp.concatenate(parts, axis=0)

    def dp_sum(grad, dim):
        return lax.psum_scatter(
            grad.astype(bf16), "dp", scatter_dimension=dim, tiled=True
        ).astype(f32)

    grad_fulls = [gather_rows(cots[i]) for i in range(count)]
    grad_full = cat(grad_fulls)
    grad_w_down = jnp.einsum(
        "isf,isd->fd", cat([k["hidden"] for k in ks]), grad_full, preferred_element_type=f32
    )
    ffn = [backward_ffn(grad_fulls[i], ks[i], p) for i in range(count)]
    back_terms = [f[2] for f in ffn]
    grad_w_down, back_terms[-1] = lax.optimization_barrier((grad_w_down, back_terms[-1]))
    sum_w_down = dp_sum(grad_w_down, 1)
    grad_pre = cat([f[1] for f in ffn])
    grad_w_up = jnp.einsum(
        "isd,isf->df", cat([k["full_two"] for k in ks]), grad_pre, preferred_element_type=f32
    )
    back_rows = [scatter_rows(t) for t in back_terms]
    grad_w_up, back_rows[-1] = lax.optimization_barrier((grad_w_up, back_rows[-1]))
    sum_w_up = dp_sum(grad_w_up, 0)

    mids = [backward_mid(cots[i], back_rows[i], ks[i], p) for i in range(count)]
    middle_fulls = [m[1] for m in mids]
    attn = [
        backward_attn(kept[i][0], mids[i][0], middle_fulls[i], ks[i], p) for i in range(count)
    ]
    grad_ins = [a[0] for a in attn]
    grads = [dict(mids[i][2], **attn[i][1]) for i in range(count)]
    grad_query = cat([g["grad_query"] for g in grads])
    grad_key = cat([g["grad_key"] for g in grads])
    grad_value = cat([g["grad_value"] for g in grads])
    grad_qkv = jnp.einsum(
        "isd,ise->de",
        cat([k["full_one"] for k in ks]),
        jnp.concatenate([grad_query, grad_key, grad_value], axis=-1),
        preferred_element_type=f32,
    )
    grad_out_t = jnp.einsum(
        "isd,ise->de",
        cat(middle_fulls),
        cat([k["mixed"] for k in ks]),
        preferred_element_type=f32,
    )
    summed = dp_sum(jnp.concatenate([grad_qkv, grad_out_t], axis=1), 0)
    width = w_query.shape[1]
    sum_w_query = summed[:, :width]
    sum_w_key = summed[:, width : 2 * width]
    sum_w_value = summed[:, 2 * width : 3 * width]
    sum_w_out = summed[:, 3 * width :].T

    grad_b_up = jnp.sum(grad_pre, axis=(0, 1), dtype=f32).reshape(b_up.shape)
    grad_b_query = jnp.sum(grad_query, axis=(0, 1), dtype=f32).reshape(b_query.shape)
    grad_b_value = jnp.sum(grad_value, axis=(0, 1), dtype=f32).reshape(b_value.shape)
    biases = halving_scatter(jnp.concatenate([grad_b_up, grad_b_query, grad_b_value]), "dp", 1)
    n_up, n_q = b_up.shape[0], b_query.shape[0]
    sum_b_up = biases[:n_up]
    sum_b_query = biases[n_up : n_up + n_q]
    sum_b_value = biases[n_up + n_q :]

    names = ["grad_b_out", "grad_b_down", "grad_gain_one", "grad_shift_one", "grad_gain_two", "grad_shift_two"]
    vectors = jnp.stack([sum(g[key] for g in grads) for key in names])
    vectors = halving_scatter(halving_scatter(vectors, "dp", 1), "mp", 1)
    sum_b_out, sum_b_down, sum_gain_one, sum_shift_one, sum_gain_two, sum_shift_two = (
        vectors[j] for j in range(len(names))
    )
    return (
        jnp.concatenate(results, axis=0),
        jnp.concatenate(grad_ins, axis=0),
        sum_w_query,
        sum_w_key,
        sum_w_value,
        sum_b_query,
        sum_b_value,
        sum_w_out,
        sum_b_out,
        sum_w_up,
        sum_b_up,
        sum_w_down,
        sum_b_down,
        sum_gain_one,
        sum_shift_one,
        sum_gain_two,
        sum_shift_two,
    )


def solution(mesh):
    return jax.shard_map(
        body,
        mesh=mesh,
        in_specs=(
            P("dp", "mp", None),
            P("dp"),
            P(None, "mp"),
            P(None, "mp"),
            P(None, "mp"),
            P("mp", None),
            P("mp", None),
            P("mp", None),
            P(),
            P(None, "mp"),
            P("mp", None),
            P("mp", None),
            P(),
            P(),
            P(),
            P(),
            P(),
            P("dp", "mp", None),
        ),
        out_specs=(
            P("dp", "mp", None),
            P("dp", "mp", None),
            P("dp", "mp"),
            P("dp", "mp"),
            P("dp", "mp"),
            P("mp", "dp"),
            P("mp", "dp"),
            P("mp", "dp"),
            P(("dp", "mp")),
            P("dp", "mp"),
            P("mp", "dp"),
            P("mp", "dp"),
            P(("dp", "mp")),
            P(("dp", "mp")),
            P(("dp", "mp")),
            P(("dp", "mp")),
            P(("dp", "mp")),
        ),
        check_vma=False,
    )
```

```python
import math
from functools import partial

import jax
import jax.numpy as jnp
from jax import lax
from jax.sharding import PartitionSpec as P

HEAD_DIM = 128


def _pairs(n, flip):
    return [(m, m ^ flip) for m in range(n)]


def gather_rows(x, axis=1):
    n = lax.axis_size("mp")
    if n != 4:
        return lax.all_gather(x, "mp", axis=axis, tiled=True)
    rows = x.shape[axis]
    half = rows // 2
    from_x = lax.ppermute(x, "mp", _pairs(n, 1))
    from_y = lax.ppermute(x, "mp", _pairs(n, 2))
    diag_a = lax.ppermute(lax.slice_in_dim(from_y, 0, half, axis=axis), "mp", _pairs(n, 1))
    diag_b = lax.ppermute(lax.slice_in_dim(from_x, half, rows, axis=axis), "mp", _pairs(n, 2))
    return jnp.concatenate([x, from_x, from_y, diag_a, diag_b], axis=axis)


def gathered_positions(total):
    n = lax.axis_size("mp")
    places = jnp.arange(total)
    if n != 4:
        return places
    rows = total // n
    return ((lax.axis_index("mp") ^ (places // rows)) * rows) + places % rows


def scatter_rows(y, axis=1):
    n = lax.axis_size("mp")
    if n != 4:
        return lax.psum_scatter(
            y.astype(jnp.bfloat16), "mp", scatter_dimension=axis, tiled=True
        ).astype(jnp.float32)
    rows = y.shape[axis] // n
    half = rows // 2

    def part(flip, lo, hi):
        return lax.slice_in_dim(y, flip * rows + lo, flip * rows + hi, axis=axis)

    bf16 = jnp.bfloat16
    send_x = jnp.stack([part(1, 0, half), part(3, 0, half)]).astype(bf16)
    send_y = jnp.stack([part(2, half, rows), part(3, half, rows)]).astype(bf16)
    got_x = lax.ppermute(send_x, "mp", _pairs(n, 1))
    got_y = lax.ppermute(send_y, "mp", _pairs(n, 2))
    fwd_y = (got_x[1].astype(jnp.float32) + part(2, 0, half)).astype(bf16)
    fwd_x = (got_y[1].astype(jnp.float32) + part(1, half, rows)).astype(bf16)
    last_y = lax.ppermute(fwd_y, "mp", _pairs(n, 2))
    last_x = lax.ppermute(fwd_x, "mp", _pairs(n, 1))
    low = part(0, 0, half) + got_x[0].astype(jnp.float32) + last_y.astype(jnp.float32)
    high = part(0, half, rows) + got_y[0].astype(jnp.float32) + last_x.astype(jnp.float32)
    return jnp.concatenate([low, high], axis=axis)


def layer_norm(values, gain, shift):
    centre = values - jnp.mean(values, axis=-1, keepdims=True)
    spread = jnp.mean(centre * centre, axis=-1, keepdims=True)
    return centre * lax.rsqrt(spread + 1e-05) * gain + shift


def allowed_keys(lengths, seq_len):
    places = gathered_positions(seq_len)
    causal = places[None, :] <= places[:, None]
    inside = places[None, None, :] < lengths[:, None, None]
    return (causal[None] & inside)[:, None]


def head_scores(query_heads, key_heads, allowed):
    scores = jnp.einsum(
        "iqhd,ikhd->ihqk", query_heads, key_heads, preferred_element_type=jnp.float32
    ) * HEAD_DIM ** (-0.5)
    return jnp.where(allowed, scores, -1e30)


def halving_scatter(values, name, dim):
    n = lax.axis_size(name)
    if n & (n - 1):
        return lax.psum_scatter(values, name, scatter_dimension=dim, tiled=True)
    me = lax.axis_index(name)
    bit = n // 2
    while bit:
        half = values.shape[dim] // 2
        upper = (me & bit) != 0
        keep = lax.dynamic_slice_in_dim(values, jnp.where(upper, half, 0), half, axis=dim)
        give = lax.dynamic_slice_in_dim(values, jnp.where(upper, 0, half), half, axis=dim)
        values = keep + lax.ppermute(give, name, _pairs(n, bit))
        bit //= 2
    return values


def forward_item(rows_in, length, p):
    f32 = jnp.float32
    bf16 = jnp.bfloat16
    normed_one = layer_norm(rows_in, p["norm1_gain"], p["norm1_shift"]).astype(bf16)
    full_one = gather_rows(normed_one)
    items, seq_len = (full_one.shape[0], full_one.shape[1])
    heads_here = p["w_query"].shape[1] // HEAD_DIM
    split = (items, seq_len, heads_here, HEAD_DIM)

    def project(weight):
        return jnp.einsum("isd,de->ise", full_one, weight, preferred_element_type=f32)

    queries = (project(p["w_query"]) + p["b_query"].reshape(-1)).astype(bf16)
    keys_all = project(p["w_key"]).astype(bf16)
    values_all = (project(p["w_value"]) + p["b_value"].reshape(-1)).astype(bf16)
    query_heads = queries.reshape(split)
    key_heads = keys_all.reshape(split)
    value_heads = values_all.reshape(split)
    allowed = allowed_keys(length, seq_len)
    scores = head_scores(query_heads, key_heads, allowed)
    row_max = jnp.max(scores, axis=-1, keepdims=True)
    raw_weights = jnp.exp(scores - row_max)
    row_total = jnp.sum(raw_weights, axis=-1, keepdims=True)
    probs = (raw_weights / row_total).astype(bf16)
    mixed = (
        jnp.einsum("ihqk,ikhd->iqhd", probs, value_heads, preferred_element_type=f32)
        .reshape(items, seq_len, -1)
        .astype(bf16)
    )
    attn_terms = jnp.einsum("ise,ed->isd", mixed, p["w_out"], preferred_element_type=f32)
    attn_rows = scatter_rows(attn_terms)
    middle = rows_in + attn_rows + p["b_out"]
    normed_two = layer_norm(middle, p["norm2_gain"], p["norm2_shift"]).astype(bf16)
    full_two = gather_rows(normed_two)
    hidden_pre = jnp.einsum(
        "isd,df->isf", full_two, p["w_up"], preferred_element_type=f32
    ) + p["b_up"].reshape(-1)
    normal_cdf = (lax.erf(hidden_pre * (2.0 ** -0.5)) + 1.0) * 0.5
    hidden = (hidden_pre * normal_cdf).astype(bf16)
    ffn_terms = jnp.einsum("isf,fd->isd", hidden, p["w_down"], preferred_element_type=f32)
    ffn_rows = scatter_rows(ffn_terms)
    result = (middle + ffn_rows + p["b_down"]).astype(bf16)
    kept = dict(
        full_one=full_one, query_heads=query_heads, key_heads=key_heads,
        value_heads=value_heads, allowed=allowed, row_max=row_max, row_total=row_total,
        mixed=mixed, middle=middle, full_two=full_two, hidden_pre=hidden_pre, hidden=hidden,
        normal_cdf=normal_cdf,
    )
    return result, kept


def backward_ffn(grad_full, k, p):
    f32 = jnp.float32
    bf16 = jnp.bfloat16
    grad_hidden = jnp.einsum("isd,fd->isf", grad_full, p["w_down"], preferred_element_type=f32)
    u = k["hidden_pre"]
    density = jnp.exp(u * u * -0.5) * (2.0 * math.pi) ** -0.5
    grad_pre = (grad_hidden * (k["normal_cdf"] + u * density)).astype(bf16)
    back_terms = jnp.einsum("isf,df->isd", grad_pre, p["w_up"], preferred_element_type=f32)
    return grad_full, grad_pre, back_terms


def backward_mid(cotangent, back_rows, k, p):
    grad_out = cotangent.astype(jnp.float32)
    _, second_back = jax.vjp(layer_norm, k["middle"], p["norm2_gain"], p["norm2_shift"])
    grad_mid_norm, grad_gain_two, grad_shift_two = second_back(back_rows)
    grad_middle = grad_out + grad_mid_norm
    middle_full = gather_rows(grad_middle.astype(jnp.bfloat16))
    g = dict(
        grad_b_out=jnp.sum(grad_middle, axis=(0, 1)),
        grad_b_down=jnp.sum(grad_out, axis=(0, 1)),
        grad_gain_two=grad_gain_two, grad_shift_two=grad_shift_two,
    )
    return grad_middle, middle_full, g


def backward_attn(rows_in, grad_middle, middle_full, k, p):
    f32 = jnp.float32
    bf16 = jnp.bfloat16
    items, seq_len = k["full_one"].shape[:2]
    heads_here = p["w_query"].shape[1] // HEAD_DIM
    split = (items, seq_len, heads_here, HEAD_DIM)
    grad_mixed = (
        jnp.einsum("isd,ed->ise", middle_full, p["w_out"], preferred_element_type=f32)
        .astype(bf16)
        .reshape(split)
    )
    query_heads, key_heads, value_heads = k["query_heads"], k["key_heads"], k["value_heads"]
    again = head_scores(query_heads, key_heads, k["allowed"])
    probs_full = jnp.exp(again - k["row_max"]) / k["row_total"]
    probs_low = probs_full.astype(bf16)
    grad_value = (
        jnp.einsum("ihqk,iqhd->ikhd", probs_low, grad_mixed, preferred_element_type=f32)
        .astype(bf16)
        .reshape(items, seq_len, -1)
    )
    grad_probs = jnp.einsum("iqhd,ikhd->ihqk", grad_mixed, value_heads, preferred_element_type=f32)
    inner = jnp.sum(probs_full * grad_probs, axis=-1, keepdims=True)
    grad_scores = (probs_full * (grad_probs - inner)).astype(bf16)
    grad_query = (
        (
            jnp.einsum("ihqk,ikhd->iqhd", grad_scores, key_heads, preferred_element_type=f32)
            * HEAD_DIM ** (-0.5)
        )
        .astype(bf16)
        .reshape(items, seq_len, -1)
    )
    grad_key = (
        (
            jnp.einsum("ihqk,iqhd->ikhd", grad_scores, query_heads, preferred_element_type=f32)
            * HEAD_DIM ** (-0.5)
        )
        .astype(bf16)
        .reshape(items, seq_len, -1)
    )
    back_one = (
        jnp.einsum("ise,de->isd", grad_query, p["w_query"], preferred_element_type=f32)
        + jnp.einsum("ise,de->isd", grad_key, p["w_key"], preferred_element_type=f32)
        + jnp.einsum("ise,de->isd", grad_value, p["w_value"], preferred_element_type=f32)
    )
    rows_one = scatter_rows(back_one)
    _, first_back = jax.vjp(layer_norm, rows_in, p["norm1_gain"], p["norm1_shift"])
    grad_in_norm, grad_gain_one, grad_shift_one = first_back(rows_one)
    grad_inputs = (grad_middle + grad_in_norm).astype(bf16)
    g = dict(
        grad_query=grad_query, grad_key=grad_key, grad_value=grad_value,
        grad_gain_one=grad_gain_one, grad_shift_one=grad_shift_one,
    )
    return grad_inputs, g


def body(
    tokens,
    lengths,
    w_query,
    w_key,
    w_value,
    b_query,
    b_value,
    w_out,
    b_out,
    w_up,
    b_up,
    w_down,
    b_down,
    norm1_gain,
    norm1_shift,
    norm2_gain,
    norm2_shift,
    cotangent,
):
    f32 = jnp.float32
    bf16 = jnp.bfloat16
    p = dict(
        w_query=w_query, w_key=w_key, w_value=w_value, b_query=b_query, b_value=b_value,
        w_out=w_out, b_out=b_out, w_up=w_up, b_up=b_up, w_down=w_down, b_down=b_down,
        norm1_gain=norm1_gain, norm1_shift=norm1_shift,
        norm2_gain=norm2_gain, norm2_shift=norm2_shift,
    )
    count = tokens.shape[0]
    results, kept = [], []
    for i in range(count):
        rows_in = tokens[i : i + 1].astype(f32)
        result, k = forward_item(rows_in, lengths[i : i + 1], p)
        results.append(result)
        kept.append((rows_in, k))
    ks = [k for _, k in kept]
    cots = [
        lax.optimization_barrier((ks[i]["full_two"], cotangent[i : i + 1]))[1] for i in range(count)
    ]

    def cat(parts):
        return jnp.concatenate(parts, axis=0)

    def dp_sum(grad, dim):
        return lax.psum_scatter(
            grad.astype(bf16), "dp", scatter_dimension=dim, tiled=True
        ).astype(f32)

    grad_fulls = [gather_rows(cots[i]) for i in range(count)]
    grad_full = cat(grad_fulls)
    grad_w_down = jnp.einsum(
        "isf,isd->fd", cat([k["hidden"] for k in ks]), grad_full, preferred_element_type=f32
    )
    ffn = [backward_ffn(grad_fulls[i], ks[i], p) for i in range(count)]
    back_terms = [f[2] for f in ffn]
    grad_w_down, back_terms[-1] = lax.optimization_barrier((grad_w_down, back_terms[-1]))
    sum_w_down = dp_sum(grad_w_down, 1)
    grad_pre = cat([f[1] for f in ffn])
    grad_w_up = jnp.einsum(
        "isd,isf->df", cat([k["full_two"] for k in ks]), grad_pre, preferred_element_type=f32
    )
    back_rows = [scatter_rows(t) for t in back_terms]
    grad_w_up, back_rows = lax.optimization_barrier((grad_w_up, back_rows))
    sum_w_up = dp_sum(grad_w_up, 0)

    mids = [backward_mid(cots[i], back_rows[i], ks[i], p) for i in range(count)]
    middle_fulls = [m[1] for m in mids]
    attn = [
        backward_attn(kept[i][0], mids[i][0], middle_fulls[i], ks[i], p) for i in range(count)
    ]
    grad_ins = [a[0] for a in attn]
    grads = [dict(mids[i][2], **attn[i][1]) for i in range(count)]
    grad_query = cat([g["grad_query"] for g in grads])
    grad_key = cat([g["grad_key"] for g in grads])
    grad_value = cat([g["grad_value"] for g in grads])
    grad_qkv = jnp.einsum(
        "isd,ise->de",
        cat([k["full_one"] for k in ks]),
        jnp.concatenate([grad_query, grad_key, grad_value], axis=-1),
        preferred_element_type=f32,
    )
    grad_out_t = jnp.einsum(
        "isd,ise->de",
        cat(middle_fulls),
        cat([k["mixed"] for k in ks]),
        preferred_element_type=f32,
    )
    grad_out_t, sum_w_down, sum_w_up = lax.optimization_barrier((grad_out_t, sum_w_down, sum_w_up))
    sum_w_out = dp_sum(grad_out_t, 0)
    grad_qkv, sum_w_out = lax.optimization_barrier((grad_qkv, sum_w_out))
    sum_w_out = sum_w_out.T
    summed = dp_sum(grad_qkv, 0)
    width = w_query.shape[1]
    sum_w_query = summed[:, :width]
    sum_w_key = summed[:, width : 2 * width]
    sum_w_value = summed[:, 2 * width :]

    grad_b_up = jnp.sum(grad_pre, axis=(0, 1), dtype=f32).reshape(b_up.shape)
    grad_b_query = jnp.sum(grad_query, axis=(0, 1), dtype=f32).reshape(b_query.shape)
    grad_b_value = jnp.sum(grad_value, axis=(0, 1), dtype=f32).reshape(b_value.shape)
    biases = halving_scatter(jnp.concatenate([grad_b_up, grad_b_query, grad_b_value]), "dp", 1)
    n_up, n_q = b_up.shape[0], b_query.shape[0]
    sum_b_up = biases[:n_up]
    sum_b_query = biases[n_up : n_up + n_q]
    sum_b_value = biases[n_up + n_q :]

    names = ["grad_b_out", "grad_b_down", "grad_gain_one", "grad_shift_one", "grad_gain_two", "grad_shift_two"]
    vectors = jnp.stack([sum(g[key] for g in grads) for key in names])
    vectors = halving_scatter(halving_scatter(vectors, "dp", 1), "mp", 1)
    sum_b_out, sum_b_down, sum_gain_one, sum_shift_one, sum_gain_two, sum_shift_two = (
        vectors[j] for j in range(len(names))
    )
    return (
        jnp.concatenate(results, axis=0),
        jnp.concatenate(grad_ins, axis=0),
        sum_w_query,
        sum_w_key,
        sum_w_value,
        sum_b_query,
        sum_b_value,
        sum_w_out,
        sum_b_out,
        sum_w_up,
        sum_b_up,
        sum_w_down,
        sum_b_down,
        sum_gain_one,
        sum_shift_one,
        sum_gain_two,
        sum_shift_two,
    )


def solution(mesh):
    return jax.shard_map(
        body,
        mesh=mesh,
        in_specs=(
            P("dp", "mp", None),
            P("dp"),
            P(None, "mp"),
            P(None, "mp"),
            P(None, "mp"),
            P("mp", None),
            P("mp", None),
            P("mp", None),
            P(),
            P(None, "mp"),
            P("mp", None),
            P("mp", None),
            P(),
            P(),
            P(),
            P(),
            P(),
            P("dp", "mp", None),
        ),
        out_specs=(
            P("dp", "mp", None),
            P("dp", "mp", None),
            P("dp", "mp"),
            P("dp", "mp"),
            P("dp", "mp"),
            P("mp", "dp"),
            P("mp", "dp"),
            P("mp", "dp"),
            P(("dp", "mp")),
            P("dp", "mp"),
            P("mp", "dp"),
            P("mp", "dp"),
            P(("dp", "mp")),
            P(("dp", "mp")),
            P(("dp", "mp")),
            P(("dp", "mp")),
            P(("dp", "mp")),
        ),
        check_vma=False,
    )
```

```python
import math
from functools import partial

import jax
import jax.numpy as jnp
from jax import lax
from jax.experimental.layout import Layout, with_layout_constraint
from jax.sharding import PartitionSpec as P

HEAD_DIM = 128


def _pairs(n, flip):
    return [(m, m ^ flip) for m in range(n)]


def gather_rows(x, axis=1):
    n = lax.axis_size("mp")
    if n != 4:
        return lax.all_gather(x, "mp", axis=axis, tiled=True)
    rows = x.shape[axis]
    half = rows // 2
    from_x = lax.ppermute(x, "mp", _pairs(n, 1))
    from_y = lax.ppermute(x, "mp", _pairs(n, 2))
    diag_a = lax.ppermute(lax.slice_in_dim(from_y, 0, half, axis=axis), "mp", _pairs(n, 1))
    diag_b = lax.ppermute(lax.slice_in_dim(from_x, half, rows, axis=axis), "mp", _pairs(n, 2))
    return jnp.concatenate([x, from_x, from_y, diag_a, diag_b], axis=axis)


def gathered_positions(total):
    n = lax.axis_size("mp")
    places = jnp.arange(total)
    if n != 4:
        return places
    rows = total // n
    return ((lax.axis_index("mp") ^ (places // rows)) * rows) + places % rows


def scatter_rows(y, axis=1):
    n = lax.axis_size("mp")
    if n != 4:
        return lax.psum_scatter(
            y.astype(jnp.bfloat16), "mp", scatter_dimension=axis, tiled=True
        ).astype(jnp.float32)
    rows = y.shape[axis] // n
    half = rows // 2

    def part(flip, lo, hi):
        return lax.slice_in_dim(y, flip * rows + lo, flip * rows + hi, axis=axis)

    bf16 = jnp.bfloat16
    send_x = jnp.stack([part(1, 0, half), part(3, 0, half)]).astype(bf16)
    send_y = jnp.stack([part(2, half, rows), part(3, half, rows)]).astype(bf16)
    got_x = lax.ppermute(send_x, "mp", _pairs(n, 1))
    got_y = lax.ppermute(send_y, "mp", _pairs(n, 2))
    fwd_y = (got_x[1].astype(jnp.float32) + part(2, 0, half)).astype(bf16)
    fwd_x = (got_y[1].astype(jnp.float32) + part(1, half, rows)).astype(bf16)
    last_y = lax.ppermute(fwd_y, "mp", _pairs(n, 2))
    last_x = lax.ppermute(fwd_x, "mp", _pairs(n, 1))
    low = part(0, 0, half) + got_x[0].astype(jnp.float32) + last_y.astype(jnp.float32)
    high = part(0, half, rows) + got_y[0].astype(jnp.float32) + last_x.astype(jnp.float32)
    return jnp.concatenate([low, high], axis=axis)


def layer_norm(values, gain, shift):
    centre = values - jnp.mean(values, axis=-1, keepdims=True)
    spread = jnp.mean(centre * centre, axis=-1, keepdims=True)
    return centre * lax.rsqrt(spread + 1e-05) * gain + shift


def allowed_keys(lengths, seq_len):
    places = gathered_positions(seq_len)
    causal = places[None, :] <= places[:, None]
    inside = places[None, None, :] < lengths[:, None, None]
    return (causal[None] & inside)[:, None]


def head_scores(query_heads, key_heads, allowed):
    scores = jnp.einsum(
        "iqhd,ikhd->ihqk", query_heads, key_heads, preferred_element_type=jnp.float32
    ) * HEAD_DIM ** (-0.5)
    return jnp.where(allowed, scores, -1e30)


def halving_scatter(values, name, dim):
    n = lax.axis_size(name)
    if n & (n - 1):
        return lax.psum_scatter(values, name, scatter_dimension=dim, tiled=True)
    me = lax.axis_index(name)
    bit = n // 2
    while bit:
        half = values.shape[dim] // 2
        upper = (me & bit) != 0
        keep = lax.dynamic_slice_in_dim(values, jnp.where(upper, half, 0), half, axis=dim)
        give = lax.dynamic_slice_in_dim(values, jnp.where(upper, 0, half), half, axis=dim)
        values = keep + lax.ppermute(give, name, _pairs(n, bit))
        bit //= 2
    return values


def forward_item(rows_in, length, p):
    f32 = jnp.float32
    bf16 = jnp.bfloat16
    normed_one = layer_norm(rows_in, p["norm1_gain"], p["norm1_shift"]).astype(bf16)
    full_one = gather_rows(normed_one)
    items, seq_len = (full_one.shape[0], full_one.shape[1])
    heads_here = p["w_query"].shape[1] // HEAD_DIM
    split = (items, seq_len, heads_here, HEAD_DIM)

    def project(weight):
        return jnp.einsum("isd,de->ise", full_one, weight, preferred_element_type=f32)

    queries = (project(p["w_query"]) + p["b_query"].reshape(-1)).astype(bf16)
    keys_all = project(p["w_key"]).astype(bf16)
    values_all = (project(p["w_value"]) + p["b_value"].reshape(-1)).astype(bf16)
    query_heads = queries.reshape(split)
    key_heads = keys_all.reshape(split)
    value_heads = values_all.reshape(split)
    allowed = allowed_keys(length, seq_len)
    scores = head_scores(query_heads, key_heads, allowed)
    row_max = jnp.max(scores, axis=-1, keepdims=True)
    raw_weights = jnp.exp(scores - row_max)
    row_total = jnp.sum(raw_weights, axis=-1, keepdims=True)
    probs = (raw_weights / row_total).astype(bf16)
    mixed = (
        jnp.einsum("ihqk,ikhd->iqhd", probs, value_heads, preferred_element_type=f32)
        .reshape(items, seq_len, -1)
        .astype(bf16)
    )
    attn_terms = jnp.einsum("ise,ed->isd", mixed, p["w_out"], preferred_element_type=f32)
    attn_rows = scatter_rows(attn_terms)
    middle = rows_in + attn_rows + p["b_out"]
    normed_two = layer_norm(middle, p["norm2_gain"], p["norm2_shift"]).astype(bf16)
    full_two = gather_rows(normed_two)
    hidden_pre = jnp.einsum(
        "isd,df->isf", full_two, p["w_up"], preferred_element_type=f32
    ) + p["b_up"].reshape(-1)
    normal_cdf = (lax.erf(hidden_pre * (2.0 ** -0.5)) + 1.0) * 0.5
    hidden = (hidden_pre * normal_cdf).astype(bf16)
    ffn_terms = jnp.einsum("isf,fd->isd", hidden, p["w_down"], preferred_element_type=f32)
    ffn_rows = scatter_rows(ffn_terms)
    result = (middle + ffn_rows + p["b_down"]).astype(bf16)
    kept = dict(
        full_one=full_one, query_heads=query_heads, key_heads=key_heads,
        value_heads=value_heads, allowed=allowed, row_max=row_max, row_total=row_total,
        mixed=mixed, middle=middle, full_two=full_two, hidden_pre=hidden_pre, hidden=hidden,
        normal_cdf=normal_cdf,
    )
    return result, kept


def backward_ffn(grad_full, k, p):
    f32 = jnp.float32
    bf16 = jnp.bfloat16
    grad_hidden = jnp.einsum("isd,fd->isf", grad_full, p["w_down"], preferred_element_type=f32)
    u = k["hidden_pre"]
    density = jnp.exp(u * u * -0.5) * (2.0 * math.pi) ** -0.5
    grad_pre = (grad_hidden * (k["normal_cdf"] + u * density)).astype(bf16)
    back_terms = jnp.einsum("isf,df->isd", grad_pre, p["w_up"], preferred_element_type=f32)
    return grad_full, grad_pre, back_terms


def backward_mid(cotangent, back_rows, k, p):
    grad_out = cotangent.astype(jnp.float32)
    _, second_back = jax.vjp(layer_norm, k["middle"], p["norm2_gain"], p["norm2_shift"])
    grad_mid_norm, grad_gain_two, grad_shift_two = second_back(back_rows)
    grad_middle = grad_out + grad_mid_norm
    middle_full = gather_rows(grad_middle.astype(jnp.bfloat16))
    g = dict(
        grad_b_out=jnp.sum(grad_middle, axis=(0, 1)),
        grad_b_down=jnp.sum(grad_out, axis=(0, 1)),
        grad_gain_two=grad_gain_two, grad_shift_two=grad_shift_two,
    )
    return grad_middle, middle_full, g


def backward_attn(rows_in, grad_middle, middle_full, k, p):
    f32 = jnp.float32
    bf16 = jnp.bfloat16
    items, seq_len = k["full_one"].shape[:2]
    heads_here = p["w_query"].shape[1] // HEAD_DIM
    split = (items, seq_len, heads_here, HEAD_DIM)
    grad_mixed = (
        jnp.einsum("isd,ed->ise", middle_full, p["w_out"], preferred_element_type=f32)
        .astype(bf16)
        .reshape(split)
    )
    query_heads, key_heads, value_heads = k["query_heads"], k["key_heads"], k["value_heads"]
    again = head_scores(query_heads, key_heads, k["allowed"])
    probs_full = jnp.exp(again - k["row_max"]) / k["row_total"]
    probs_low = probs_full.astype(bf16)
    grad_value = (
        jnp.einsum("ihqk,iqhd->ikhd", probs_low, grad_mixed, preferred_element_type=f32)
        .astype(bf16)
        .reshape(items, seq_len, -1)
    )
    grad_probs = jnp.einsum("iqhd,ikhd->ihqk", grad_mixed, value_heads, preferred_element_type=f32)
    inner = jnp.sum(probs_full * grad_probs, axis=-1, keepdims=True)
    grad_scores = (probs_full * (grad_probs - inner)).astype(bf16)
    grad_query = (
        (
            jnp.einsum("ihqk,ikhd->iqhd", grad_scores, key_heads, preferred_element_type=f32)
            * HEAD_DIM ** (-0.5)
        )
        .astype(bf16)
        .reshape(items, seq_len, -1)
    )
    grad_key = (
        (
            jnp.einsum("ihqk,iqhd->ikhd", grad_scores, query_heads, preferred_element_type=f32)
            * HEAD_DIM ** (-0.5)
        )
        .astype(bf16)
        .reshape(items, seq_len, -1)
    )
    back_one = (
        jnp.einsum("ise,de->isd", grad_query, p["w_query"], preferred_element_type=f32)
        + jnp.einsum("ise,de->isd", grad_key, p["w_key"], preferred_element_type=f32)
        + jnp.einsum("ise,de->isd", grad_value, p["w_value"], preferred_element_type=f32)
    )
    rows_one = scatter_rows(back_one)
    _, first_back = jax.vjp(layer_norm, rows_in, p["norm1_gain"], p["norm1_shift"])
    grad_in_norm, grad_gain_one, grad_shift_one = first_back(rows_one)
    grad_inputs = (grad_middle + grad_in_norm).astype(bf16)
    g = dict(
        grad_query=grad_query, grad_key=grad_key, grad_value=grad_value,
        grad_gain_one=grad_gain_one, grad_shift_one=grad_shift_one,
    )
    return grad_inputs, g


def body(
    tokens,
    lengths,
    w_query,
    w_key,
    w_value,
    b_query,
    b_value,
    w_out,
    b_out,
    w_up,
    b_up,
    w_down,
    b_down,
    norm1_gain,
    norm1_shift,
    norm2_gain,
    norm2_shift,
    cotangent,
):
    f32 = jnp.float32
    bf16 = jnp.bfloat16
    p = dict(
        w_query=w_query, w_key=w_key, w_value=w_value, b_query=b_query, b_value=b_value,
        w_out=w_out, b_out=b_out, w_up=w_up, b_up=b_up, w_down=w_down, b_down=b_down,
        norm1_gain=norm1_gain, norm1_shift=norm1_shift,
        norm2_gain=norm2_gain, norm2_shift=norm2_shift,
    )
    count = tokens.shape[0]
    results, kept = [], []
    for i in range(count):
        rows_in = tokens[i : i + 1].astype(f32)
        result, k = forward_item(rows_in, lengths[i : i + 1], p)
        results.append(result)
        kept.append((rows_in, k))
    ks = [k for _, k in kept]
    cots = [
        lax.optimization_barrier((ks[i]["full_two"], cotangent[i : i + 1]))[1] for i in range(count)
    ]

    def cat(parts):
        return jnp.concatenate(parts, axis=0)

    def dp_sum(grad, dim):
        return lax.psum_scatter(
            grad.astype(bf16), "dp", scatter_dimension=dim, tiled=True
        ).astype(f32)

    grad_fulls = [gather_rows(cots[i]) for i in range(count)]
    grad_full = cat(grad_fulls)
    grad_w_down = jnp.einsum(
        "isf,isd->fd", cat([k["hidden"] for k in ks]), grad_full, preferred_element_type=f32
    )
    ffn = [backward_ffn(grad_fulls[i], ks[i], p) for i in range(count)]
    back_terms = [f[2] for f in ffn]
    grad_w_down, back_terms[-1] = lax.optimization_barrier((grad_w_down, back_terms[-1]))
    sum_w_down = dp_sum(grad_w_down, 1)
    grad_pre = cat([f[1] for f in ffn])
    grad_w_up = jnp.einsum(
        "isd,isf->df", cat([k["full_two"] for k in ks]), grad_pre, preferred_element_type=f32
    )
    back_rows = [scatter_rows(t) for t in back_terms]
    grad_w_up, back_rows = lax.optimization_barrier((grad_w_up, back_rows))
    sum_w_up = dp_sum(grad_w_up, 0)

    mids = [backward_mid(cots[i], back_rows[i], ks[i], p) for i in range(count)]
    middle_fulls = [m[1] for m in mids]
    attn = [
        backward_attn(kept[i][0], mids[i][0], middle_fulls[i], ks[i], p) for i in range(count)
    ]
    grad_ins = [a[0] for a in attn]
    grads = [dict(mids[i][2], **attn[i][1]) for i in range(count)]
    grad_query = cat([g["grad_query"] for g in grads])
    grad_key = cat([g["grad_key"] for g in grads])
    grad_value = cat([g["grad_value"] for g in grads])
    grad_qkv = jnp.einsum(
        "isd,ise->de",
        cat([k["full_one"] for k in ks]),
        jnp.concatenate([grad_query, grad_key, grad_value], axis=-1),
        preferred_element_type=f32,
    )
    grad_out_t = jnp.einsum(
        "isd,ise->de",
        cat(middle_fulls),
        cat([k["mixed"] for k in ks]),
        preferred_element_type=f32,
    )
    joined = jnp.concatenate([grad_qkv, grad_out_t], axis=1).astype(bf16)
    joined = with_layout_constraint(joined, Layout(major_to_minor=(0, 1)))
    summed = lax.psum_scatter(joined, "dp", scatter_dimension=0, tiled=True).astype(f32)
    width = w_query.shape[1]
    sum_w_query = summed[:, :width]
    sum_w_key = summed[:, width : 2 * width]
    sum_w_value = summed[:, 2 * width : 3 * width]
    sum_w_out = summed[:, 3 * width :].T

    grad_b_up = jnp.sum(grad_pre, axis=(0, 1), dtype=f32).reshape(b_up.shape)
    grad_b_query = jnp.sum(grad_query, axis=(0, 1), dtype=f32).reshape(b_query.shape)
    grad_b_value = jnp.sum(grad_value, axis=(0, 1), dtype=f32).reshape(b_value.shape)
    biases = halving_scatter(jnp.concatenate([grad_b_up, grad_b_query, grad_b_value]), "dp", 1)
    n_up, n_q = b_up.shape[0], b_query.shape[0]
    sum_b_up = biases[:n_up]
    sum_b_query = biases[n_up : n_up + n_q]
    sum_b_value = biases[n_up + n_q :]

    names = ["grad_b_out", "grad_b_down", "grad_gain_one", "grad_shift_one", "grad_gain_two", "grad_shift_two"]
    vectors = jnp.stack([sum(g[key] for g in grads) for key in names])
    vectors = halving_scatter(halving_scatter(vectors, "dp", 1), "mp", 1)
    sum_b_out, sum_b_down, sum_gain_one, sum_shift_one, sum_gain_two, sum_shift_two = (
        vectors[j] for j in range(len(names))
    )
    return (
        jnp.concatenate(results, axis=0),
        jnp.concatenate(grad_ins, axis=0),
        sum_w_query,
        sum_w_key,
        sum_w_value,
        sum_b_query,
        sum_b_value,
        sum_w_out,
        sum_b_out,
        sum_w_up,
        sum_b_up,
        sum_w_down,
        sum_b_down,
        sum_gain_one,
        sum_shift_one,
        sum_gain_two,
        sum_shift_two,
    )


def solution(mesh):
    return jax.shard_map(
        body,
        mesh=mesh,
        in_specs=(
            P("dp", "mp", None),
            P("dp"),
            P(None, "mp"),
            P(None, "mp"),
            P(None, "mp"),
            P("mp", None),
            P("mp", None),
            P("mp", None),
            P(),
            P(None, "mp"),
            P("mp", None),
            P("mp", None),
            P(),
            P(),
            P(),
            P(),
            P(),
            P("dp", "mp", None),
        ),
        out_specs=(
            P("dp", "mp", None),
            P("dp", "mp", None),
            P("dp", "mp"),
            P("dp", "mp"),
            P("dp", "mp"),
            P("mp", "dp"),
            P("mp", "dp"),
            P("mp", "dp"),
            P(("dp", "mp")),
            P("dp", "mp"),
            P("mp", "dp"),
            P("mp", "dp"),
            P(("dp", "mp")),
            P(("dp", "mp")),
            P(("dp", "mp")),
            P(("dp", "mp")),
            P(("dp", "mp")),
        ),
        check_vma=False,
    )
```

```python
import math
from functools import partial

import jax
import jax.numpy as jnp
from jax import lax
from jax.experimental.layout import Layout, with_layout_constraint
from jax.sharding import PartitionSpec as P

HEAD_DIM = 128


def _pairs(n, flip):
    return [(m, m ^ flip) for m in range(n)]


def gather_rows(x, axis=1):
    n = lax.axis_size("mp")
    if n != 4:
        return lax.all_gather(x, "mp", axis=axis, tiled=True)
    rows = x.shape[axis]
    half = rows // 2
    from_x = lax.ppermute(x, "mp", _pairs(n, 1))
    from_y = lax.ppermute(x, "mp", _pairs(n, 2))
    diag_a = lax.ppermute(lax.slice_in_dim(from_y, 0, half, axis=axis), "mp", _pairs(n, 1))
    diag_b = lax.ppermute(lax.slice_in_dim(from_x, half, rows, axis=axis), "mp", _pairs(n, 2))
    return jnp.concatenate([x, from_x, from_y, diag_a, diag_b], axis=axis)


def gathered_positions(total):
    n = lax.axis_size("mp")
    places = jnp.arange(total)
    if n != 4:
        return places
    rows = total // n
    return ((lax.axis_index("mp") ^ (places // rows)) * rows) + places % rows


def scatter_rows(y, axis=1):
    n = lax.axis_size("mp")
    if n != 4:
        return lax.psum_scatter(
            y.astype(jnp.bfloat16), "mp", scatter_dimension=axis, tiled=True
        ).astype(jnp.float32)
    rows = y.shape[axis] // n
    half = rows // 2

    def part(flip, lo, hi):
        return lax.slice_in_dim(y, flip * rows + lo, flip * rows + hi, axis=axis)

    bf16 = jnp.bfloat16
    send_x = jnp.stack([part(1, 0, half), part(3, 0, half)]).astype(bf16)
    send_y = jnp.stack([part(2, half, rows), part(3, half, rows)]).astype(bf16)
    got_x = lax.ppermute(send_x, "mp", _pairs(n, 1))
    got_y = lax.ppermute(send_y, "mp", _pairs(n, 2))
    fwd_y = (got_x[1].astype(jnp.float32) + part(2, 0, half)).astype(bf16)
    fwd_x = (got_y[1].astype(jnp.float32) + part(1, half, rows)).astype(bf16)
    last_y = lax.ppermute(fwd_y, "mp", _pairs(n, 2))
    last_x = lax.ppermute(fwd_x, "mp", _pairs(n, 1))
    low = part(0, 0, half) + got_x[0].astype(jnp.float32) + last_y.astype(jnp.float32)
    high = part(0, half, rows) + got_y[0].astype(jnp.float32) + last_x.astype(jnp.float32)
    return jnp.concatenate([low, high], axis=axis)


def layer_norm(values, gain, shift):
    centre = values - jnp.mean(values, axis=-1, keepdims=True)
    spread = jnp.mean(centre * centre, axis=-1, keepdims=True)
    return centre * lax.rsqrt(spread + 1e-05) * gain + shift


def allowed_keys(lengths, seq_len):
    places = gathered_positions(seq_len)
    causal = places[None, :] <= places[:, None]
    inside = places[None, None, :] < lengths[:, None, None]
    return (causal[None] & inside)[:, None]


def head_scores(query_heads, key_heads, allowed):
    scores = jnp.einsum(
        "iqhd,ikhd->ihqk", query_heads, key_heads, preferred_element_type=jnp.float32
    ) * HEAD_DIM ** (-0.5)
    return jnp.where(allowed, scores, -1e30)


def halving_scatter(values, name, dim):
    n = lax.axis_size(name)
    if n & (n - 1):
        return lax.psum_scatter(values, name, scatter_dimension=dim, tiled=True)
    me = lax.axis_index(name)
    bit = n // 2
    while bit:
        half = values.shape[dim] // 2
        upper = (me & bit) != 0
        keep = lax.dynamic_slice_in_dim(values, jnp.where(upper, half, 0), half, axis=dim)
        give = lax.dynamic_slice_in_dim(values, jnp.where(upper, 0, half), half, axis=dim)
        values = keep + lax.ppermute(give, name, _pairs(n, bit))
        bit //= 2
    return values


def forward_item(rows_in, length, p):
    f32 = jnp.float32
    bf16 = jnp.bfloat16
    normed_one = layer_norm(rows_in, p["norm1_gain"], p["norm1_shift"]).astype(bf16)
    full_one = gather_rows(normed_one)
    items, seq_len = (full_one.shape[0], full_one.shape[1])
    heads_here = p["w_query"].shape[1] // HEAD_DIM
    split = (items, seq_len, heads_here, HEAD_DIM)

    def project(weight):
        return jnp.einsum("isd,de->ise", full_one, weight, preferred_element_type=f32)

    queries = (project(p["w_query"]) + p["b_query"].reshape(-1)).astype(bf16)
    keys_all = project(p["w_key"]).astype(bf16)
    values_all = (project(p["w_value"]) + p["b_value"].reshape(-1)).astype(bf16)
    query_heads = queries.reshape(split)
    key_heads = keys_all.reshape(split)
    value_heads = values_all.reshape(split)
    allowed = allowed_keys(length, seq_len)
    scores = head_scores(query_heads, key_heads, allowed)
    row_max = jnp.max(scores, axis=-1, keepdims=True)
    raw_weights = jnp.exp(scores - row_max)
    row_total = jnp.sum(raw_weights, axis=-1, keepdims=True)
    probs = (raw_weights / row_total).astype(bf16)
    mixed = (
        jnp.einsum("ihqk,ikhd->iqhd", probs, value_heads, preferred_element_type=f32)
        .reshape(items, seq_len, -1)
        .astype(bf16)
    )
    attn_terms = jnp.einsum("ise,ed->isd", mixed, p["w_out"], preferred_element_type=f32)
    attn_rows = scatter_rows(attn_terms)
    middle = rows_in + attn_rows + p["b_out"]
    normed_two = layer_norm(middle, p["norm2_gain"], p["norm2_shift"]).astype(bf16)
    full_two = gather_rows(normed_two)
    hidden_pre = jnp.einsum(
        "isd,df->isf", full_two, p["w_up"], preferred_element_type=f32
    ) + p["b_up"].reshape(-1)
    normal_cdf = (lax.erf(hidden_pre * (2.0 ** -0.5)) + 1.0) * 0.5
    hidden = (hidden_pre * normal_cdf).astype(bf16)
    ffn_terms = jnp.einsum("isf,fd->isd", hidden, p["w_down"], preferred_element_type=f32)
    ffn_rows = scatter_rows(ffn_terms)
    result = (middle + ffn_rows + p["b_down"]).astype(bf16)
    kept = dict(
        full_one=full_one, query_heads=query_heads, key_heads=key_heads,
        value_heads=value_heads, allowed=allowed, row_max=row_max, row_total=row_total,
        mixed=mixed, middle=middle, full_two=full_two, hidden_pre=hidden_pre, hidden=hidden,
        normal_cdf=normal_cdf,
    )
    return result, kept


def backward_ffn(grad_full, k, p):
    f32 = jnp.float32
    bf16 = jnp.bfloat16
    grad_hidden = jnp.einsum("isd,fd->isf", grad_full, p["w_down"], preferred_element_type=f32)
    u = k["hidden_pre"]
    density = jnp.exp(u * u * -0.5) * (2.0 * math.pi) ** -0.5
    grad_pre = (grad_hidden * (k["normal_cdf"] + u * density)).astype(bf16)
    back_terms = jnp.einsum("isf,df->isd", grad_pre, p["w_up"], preferred_element_type=f32)
    return grad_full, grad_pre, back_terms


def backward_mid(cotangent, back_rows, k, p):
    grad_out = cotangent.astype(jnp.float32)
    _, second_back = jax.vjp(layer_norm, k["middle"], p["norm2_gain"], p["norm2_shift"])
    grad_mid_norm, grad_gain_two, grad_shift_two = second_back(back_rows)
    grad_middle = grad_out + grad_mid_norm
    middle_full = gather_rows(grad_middle.astype(jnp.bfloat16))
    g = dict(
        grad_b_out=jnp.sum(grad_middle, axis=(0, 1)),
        grad_b_down=jnp.sum(grad_out, axis=(0, 1)),
        grad_gain_two=grad_gain_two, grad_shift_two=grad_shift_two,
    )
    return grad_middle, middle_full, g


def backward_attn(rows_in, grad_middle, middle_full, k, p):
    f32 = jnp.float32
    bf16 = jnp.bfloat16
    items, seq_len = k["full_one"].shape[:2]
    heads_here = p["w_query"].shape[1] // HEAD_DIM
    split = (items, seq_len, heads_here, HEAD_DIM)
    grad_mixed = (
        jnp.einsum("isd,ed->ise", middle_full, p["w_out"], preferred_element_type=f32)
        .astype(bf16)
        .reshape(split)
    )
    query_heads, key_heads, value_heads = k["query_heads"], k["key_heads"], k["value_heads"]
    again = head_scores(query_heads, key_heads, k["allowed"])
    probs_full = jnp.exp(again - k["row_max"]) / k["row_total"]
    probs_low = probs_full.astype(bf16)
    grad_value = (
        jnp.einsum("ihqk,iqhd->ikhd", probs_low, grad_mixed, preferred_element_type=f32)
        .astype(bf16)
        .reshape(items, seq_len, -1)
    )
    grad_probs = jnp.einsum("iqhd,ikhd->ihqk", grad_mixed, value_heads, preferred_element_type=f32)
    inner = jnp.sum(probs_full * grad_probs, axis=-1, keepdims=True)
    grad_scores = (probs_full * (grad_probs - inner)).astype(bf16)
    grad_query = (
        (
            jnp.einsum("ihqk,ikhd->iqhd", grad_scores, key_heads, preferred_element_type=f32)
            * HEAD_DIM ** (-0.5)
        )
        .astype(bf16)
        .reshape(items, seq_len, -1)
    )
    grad_key = (
        (
            jnp.einsum("ihqk,iqhd->ikhd", grad_scores, query_heads, preferred_element_type=f32)
            * HEAD_DIM ** (-0.5)
        )
        .astype(bf16)
        .reshape(items, seq_len, -1)
    )
    back_one = (
        jnp.einsum("ise,de->isd", grad_query, p["w_query"], preferred_element_type=f32)
        + jnp.einsum("ise,de->isd", grad_key, p["w_key"], preferred_element_type=f32)
        + jnp.einsum("ise,de->isd", grad_value, p["w_value"], preferred_element_type=f32)
    )
    rows_one = scatter_rows(back_one)
    _, first_back = jax.vjp(layer_norm, rows_in, p["norm1_gain"], p["norm1_shift"])
    grad_in_norm, grad_gain_one, grad_shift_one = first_back(rows_one)
    grad_inputs = (grad_middle + grad_in_norm).astype(bf16)
    g = dict(
        grad_query=grad_query, grad_key=grad_key, grad_value=grad_value,
        grad_gain_one=grad_gain_one, grad_shift_one=grad_shift_one,
    )
    return grad_inputs, g


def body(
    tokens,
    lengths,
    w_query,
    w_key,
    w_value,
    b_query,
    b_value,
    w_out,
    b_out,
    w_up,
    b_up,
    w_down,
    b_down,
    norm1_gain,
    norm1_shift,
    norm2_gain,
    norm2_shift,
    cotangent,
):
    f32 = jnp.float32
    bf16 = jnp.bfloat16
    p = dict(
        w_query=w_query, w_key=w_key, w_value=w_value, b_query=b_query, b_value=b_value,
        w_out=w_out, b_out=b_out, w_up=w_up, b_up=b_up, w_down=w_down, b_down=b_down,
        norm1_gain=norm1_gain, norm1_shift=norm1_shift,
        norm2_gain=norm2_gain, norm2_shift=norm2_shift,
    )
    count = tokens.shape[0]
    results, kept = [], []
    for i in range(count):
        rows_in = tokens[i : i + 1].astype(f32)
        result, k = forward_item(rows_in, lengths[i : i + 1], p)
        results.append(result)
        kept.append((rows_in, k))
    ks = [k for _, k in kept]
    cots = [
        lax.optimization_barrier((ks[i]["full_two"], cotangent[i : i + 1]))[1] for i in range(count)
    ]

    def cat(parts):
        return jnp.concatenate(parts, axis=0)

    def dp_sum(grad, dim):
        return lax.psum_scatter(
            grad.astype(bf16), "dp", scatter_dimension=dim, tiled=True
        ).astype(f32)

    grad_fulls = [gather_rows(cots[i]) for i in range(count)]
    grad_full = cat(grad_fulls)
    grad_w_down = jnp.einsum(
        "isf,isd->fd", cat([k["hidden"] for k in ks]), grad_full, preferred_element_type=f32
    )
    ffn = [backward_ffn(grad_fulls[i], ks[i], p) for i in range(count)]
    back_terms = [f[2] for f in ffn]
    grad_pre = cat([f[1] for f in ffn])
    grad_w_up = jnp.einsum(
        "isd,isf->df", cat([k["full_two"] for k in ks]), grad_pre, preferred_element_type=f32
    )
    back_rows = [scatter_rows(t) for t in back_terms]
    grad_w_down, back_rows[0] = lax.optimization_barrier((grad_w_down, back_rows[0]))
    sum_w_down = dp_sum(grad_w_down, 1)
    grad_w_up, back_rows = lax.optimization_barrier((grad_w_up, back_rows))
    sum_w_up = dp_sum(grad_w_up, 0)

    mids = [backward_mid(cots[i], back_rows[i], ks[i], p) for i in range(count)]
    middle_fulls = [m[1] for m in mids]
    attn = [
        backward_attn(kept[i][0], mids[i][0], middle_fulls[i], ks[i], p) for i in range(count)
    ]
    grad_ins = [a[0] for a in attn]
    grads = [dict(mids[i][2], **attn[i][1]) for i in range(count)]
    grad_query = cat([g["grad_query"] for g in grads])
    grad_key = cat([g["grad_key"] for g in grads])
    grad_value = cat([g["grad_value"] for g in grads])
    grad_qkv = jnp.einsum(
        "isd,ise->de",
        cat([k["full_one"] for k in ks]),
        jnp.concatenate([grad_query, grad_key, grad_value], axis=-1),
        preferred_element_type=f32,
    )
    grad_out_t = jnp.einsum(
        "isd,ise->de",
        cat(middle_fulls),
        cat([k["mixed"] for k in ks]),
        preferred_element_type=f32,
    )
    joined = jnp.concatenate([grad_qkv, grad_out_t], axis=1).astype(bf16)
    joined = with_layout_constraint(joined, Layout(major_to_minor=(0, 1)))
    summed = lax.psum_scatter(joined, "dp", scatter_dimension=0, tiled=True).astype(f32)
    width = w_query.shape[1]
    sum_w_query = summed[:, :width]
    sum_w_key = summed[:, width : 2 * width]
    sum_w_value = summed[:, 2 * width : 3 * width]
    sum_w_out = summed[:, 3 * width :].T

    grad_b_up = jnp.sum(grad_pre, axis=(0, 1), dtype=f32).reshape(b_up.shape)
    grad_b_query = jnp.sum(grad_query, axis=(0, 1), dtype=f32).reshape(b_query.shape)
    grad_b_value = jnp.sum(grad_value, axis=(0, 1), dtype=f32).reshape(b_value.shape)
    biases = halving_scatter(jnp.concatenate([grad_b_up, grad_b_query, grad_b_value]), "dp", 1)
    n_up, n_q = b_up.shape[0], b_query.shape[0]
    sum_b_up = biases[:n_up]
    sum_b_query = biases[n_up : n_up + n_q]
    sum_b_value = biases[n_up + n_q :]

    names = ["grad_b_out", "grad_b_down", "grad_gain_one", "grad_shift_one", "grad_gain_two", "grad_shift_two"]
    vectors = jnp.stack([sum(g[key] for g in grads) for key in names])
    vectors = halving_scatter(halving_scatter(vectors, "dp", 1), "mp", 1)
    sum_b_out, sum_b_down, sum_gain_one, sum_shift_one, sum_gain_two, sum_shift_two = (
        vectors[j] for j in range(len(names))
    )
    return (
        jnp.concatenate(results, axis=0),
        jnp.concatenate(grad_ins, axis=0),
        sum_w_query,
        sum_w_key,
        sum_w_value,
        sum_b_query,
        sum_b_value,
        sum_w_out,
        sum_b_out,
        sum_w_up,
        sum_b_up,
        sum_w_down,
        sum_b_down,
        sum_gain_one,
        sum_shift_one,
        sum_gain_two,
        sum_shift_two,
    )


def solution(mesh):
    return jax.shard_map(
        body,
        mesh=mesh,
        in_specs=(
            P("dp", "mp", None),
            P("dp"),
            P(None, "mp"),
            P(None, "mp"),
            P(None, "mp"),
            P("mp", None),
            P("mp", None),
            P("mp", None),
            P(),
            P(None, "mp"),
            P("mp", None),
            P("mp", None),
            P(),
            P(),
            P(),
            P(),
            P(),
            P("dp", "mp", None),
        ),
        out_specs=(
            P("dp", "mp", None),
            P("dp", "mp", None),
            P("dp", "mp"),
            P("dp", "mp"),
            P("dp", "mp"),
            P("mp", "dp"),
            P("mp", "dp"),
            P("mp", "dp"),
            P(("dp", "mp")),
            P("dp", "mp"),
            P("mp", "dp"),
            P("mp", "dp"),
            P(("dp", "mp")),
            P(("dp", "mp")),
            P(("dp", "mp")),
            P(("dp", "mp")),
            P(("dp", "mp")),
        ),
        check_vma=False,
    )
```

```python
import math
from functools import partial

import jax
import jax.numpy as jnp
from jax import lax
from jax.experimental.layout import Layout, with_layout_constraint
from jax.sharding import PartitionSpec as P

HEAD_DIM = 128


def _pairs(n, flip):
    return [(m, m ^ flip) for m in range(n)]


def gather_rows(x, axis=1):
    n = lax.axis_size("mp")
    if n != 4:
        return lax.all_gather(x, "mp", axis=axis, tiled=True)
    rows = x.shape[axis]
    half = rows // 2
    from_x = lax.ppermute(x, "mp", _pairs(n, 1))
    from_y = lax.ppermute(x, "mp", _pairs(n, 2))
    diag_a = lax.ppermute(lax.slice_in_dim(from_y, 0, half, axis=axis), "mp", _pairs(n, 1))
    diag_b = lax.ppermute(lax.slice_in_dim(from_x, half, rows, axis=axis), "mp", _pairs(n, 2))
    return jnp.concatenate([x, from_x, from_y, diag_a, diag_b], axis=axis)


def gathered_positions(total):
    n = lax.axis_size("mp")
    places = jnp.arange(total)
    if n != 4:
        return places
    rows = total // n
    return ((lax.axis_index("mp") ^ (places // rows)) * rows) + places % rows


def scatter_rows(y, axis=1):
    n = lax.axis_size("mp")
    if n != 4:
        return lax.psum_scatter(
            y.astype(jnp.bfloat16), "mp", scatter_dimension=axis, tiled=True
        ).astype(jnp.float32)
    rows = y.shape[axis] // n
    half = rows // 2

    def part(flip, lo, hi):
        return lax.slice_in_dim(y, flip * rows + lo, flip * rows + hi, axis=axis)

    bf16 = jnp.bfloat16
    send_x = jnp.stack([part(1, 0, half), part(3, 0, half)]).astype(bf16)
    send_y = jnp.stack([part(2, half, rows), part(3, half, rows)]).astype(bf16)
    got_x = lax.ppermute(send_x, "mp", _pairs(n, 1))
    got_y = lax.ppermute(send_y, "mp", _pairs(n, 2))
    fwd_y = (got_x[1].astype(jnp.float32) + part(2, 0, half)).astype(bf16)
    fwd_x = (got_y[1].astype(jnp.float32) + part(1, half, rows)).astype(bf16)
    last_y = lax.ppermute(fwd_y, "mp", _pairs(n, 2))
    last_x = lax.ppermute(fwd_x, "mp", _pairs(n, 1))
    low = part(0, 0, half) + got_x[0].astype(jnp.float32) + last_y.astype(jnp.float32)
    high = part(0, half, rows) + got_y[0].astype(jnp.float32) + last_x.astype(jnp.float32)
    return jnp.concatenate([low, high], axis=axis)


def layer_norm(values, gain, shift):
    centre = values - jnp.mean(values, axis=-1, keepdims=True)
    spread = jnp.mean(centre * centre, axis=-1, keepdims=True)
    return centre * lax.rsqrt(spread + 1e-05) * gain + shift


def allowed_keys(lengths, seq_len):
    places = gathered_positions(seq_len)
    causal = places[None, :] <= places[:, None]
    inside = places[None, None, :] < lengths[:, None, None]
    return (causal[None] & inside)[:, None]


def head_scores(query_heads, key_heads, allowed):
    scores = jnp.einsum(
        "iqhd,ikhd->ihqk", query_heads, key_heads, preferred_element_type=jnp.float32
    ) * HEAD_DIM ** (-0.5)
    return jnp.where(allowed, scores, -1e30)


def halving_scatter(values, name, dim):
    n = lax.axis_size(name)
    if n & (n - 1):
        return lax.psum_scatter(values, name, scatter_dimension=dim, tiled=True)
    me = lax.axis_index(name)
    bit = n // 2
    while bit:
        half = values.shape[dim] // 2
        upper = (me & bit) != 0
        keep = lax.dynamic_slice_in_dim(values, jnp.where(upper, half, 0), half, axis=dim)
        give = lax.dynamic_slice_in_dim(values, jnp.where(upper, 0, half), half, axis=dim)
        values = keep + lax.ppermute(give, name, _pairs(n, bit))
        bit //= 2
    return values


def forward_item(rows_in, length, p):
    f32 = jnp.float32
    bf16 = jnp.bfloat16
    normed_one = layer_norm(rows_in, p["norm1_gain"], p["norm1_shift"]).astype(bf16)
    full_one = gather_rows(normed_one)
    items, seq_len = (full_one.shape[0], full_one.shape[1])
    heads_here = p["w_query"].shape[1] // HEAD_DIM
    split = (items, seq_len, heads_here, HEAD_DIM)

    def project(weight):
        return jnp.einsum("isd,de->ise", full_one, weight, preferred_element_type=f32)

    queries = (project(p["w_query"]) + p["b_query"].reshape(-1)).astype(bf16)
    keys_all = project(p["w_key"]).astype(bf16)
    values_all = (project(p["w_value"]) + p["b_value"].reshape(-1)).astype(bf16)
    query_heads = queries.reshape(split)
    key_heads = keys_all.reshape(split)
    value_heads = values_all.reshape(split)
    allowed = allowed_keys(length, seq_len)
    scores = head_scores(query_heads, key_heads, allowed)
    row_max = jnp.max(scores, axis=-1, keepdims=True)
    raw_weights = jnp.exp(scores - row_max)
    row_total = jnp.sum(raw_weights, axis=-1, keepdims=True)
    probs = (raw_weights / row_total).astype(bf16)
    mixed = (
        jnp.einsum("ihqk,ikhd->iqhd", probs, value_heads, preferred_element_type=f32)
        .reshape(items, seq_len, -1)
        .astype(bf16)
    )
    attn_terms = jnp.einsum("ise,ed->isd", mixed, p["w_out"], preferred_element_type=f32)
    attn_rows = scatter_rows(attn_terms)
    middle = rows_in + attn_rows + p["b_out"]
    normed_two = layer_norm(middle, p["norm2_gain"], p["norm2_shift"]).astype(bf16)
    full_two = gather_rows(normed_two)
    hidden_pre = jnp.einsum(
        "isd,df->isf", full_two, p["w_up"], preferred_element_type=f32
    ) + p["b_up"].reshape(-1)
    normal_cdf = (lax.erf(hidden_pre * (2.0 ** -0.5)) + 1.0) * 0.5
    hidden = (hidden_pre * normal_cdf).astype(bf16)
    ffn_terms = jnp.einsum("isf,fd->isd", hidden, p["w_down"], preferred_element_type=f32)
    ffn_rows = scatter_rows(ffn_terms)
    result = (middle + ffn_rows + p["b_down"]).astype(bf16)
    kept = dict(
        full_one=full_one, query_heads=query_heads, key_heads=key_heads,
        value_heads=value_heads, allowed=allowed, row_max=row_max, row_total=row_total,
        mixed=mixed, middle=middle, full_two=full_two, hidden_pre=hidden_pre, hidden=hidden,
        normal_cdf=normal_cdf,
    )
    return result, kept


def backward_ffn(grad_full, k, p):
    f32 = jnp.float32
    bf16 = jnp.bfloat16
    grad_hidden = jnp.einsum("isd,fd->isf", grad_full, p["w_down"], preferred_element_type=f32)
    u = k["hidden_pre"]
    density = jnp.exp(u * u * -0.5) * (2.0 * math.pi) ** -0.5
    grad_pre = (grad_hidden * (k["normal_cdf"] + u * density)).astype(bf16)
    back_terms = jnp.einsum("isf,df->isd", grad_pre, p["w_up"], preferred_element_type=f32)
    return grad_full, grad_pre, back_terms


def backward_mid(cotangent, back_rows, k, p):
    grad_out = cotangent.astype(jnp.float32)
    _, second_back = jax.vjp(layer_norm, k["middle"], p["norm2_gain"], p["norm2_shift"])
    grad_mid_norm, grad_gain_two, grad_shift_two = second_back(back_rows)
    grad_middle = grad_out + grad_mid_norm
    middle_full = gather_rows(grad_middle.astype(jnp.bfloat16))
    g = dict(
        grad_b_out=jnp.sum(grad_middle, axis=(0, 1)),
        grad_b_down=jnp.sum(grad_out, axis=(0, 1)),
        grad_gain_two=grad_gain_two, grad_shift_two=grad_shift_two,
    )
    return grad_middle, middle_full, g


def backward_attn(rows_in, grad_middle, middle_full, k, p):
    f32 = jnp.float32
    bf16 = jnp.bfloat16
    items, seq_len = k["full_one"].shape[:2]
    heads_here = p["w_query"].shape[1] // HEAD_DIM
    split = (items, seq_len, heads_here, HEAD_DIM)
    grad_mixed = (
        jnp.einsum("isd,ed->ise", middle_full, p["w_out"], preferred_element_type=f32)
        .astype(bf16)
        .reshape(split)
    )
    query_heads, key_heads, value_heads = k["query_heads"], k["key_heads"], k["value_heads"]
    again = head_scores(query_heads, key_heads, k["allowed"])
    probs_full = jnp.exp(again - k["row_max"]) / k["row_total"]
    probs_low = probs_full.astype(bf16)
    grad_value = (
        jnp.einsum("ihqk,iqhd->ikhd", probs_low, grad_mixed, preferred_element_type=f32)
        .astype(bf16)
        .reshape(items, seq_len, -1)
    )
    grad_probs = jnp.einsum("iqhd,ikhd->ihqk", grad_mixed, value_heads, preferred_element_type=f32)
    inner = jnp.sum(probs_full * grad_probs, axis=-1, keepdims=True)
    grad_scores = (probs_full * (grad_probs - inner)).astype(bf16)
    grad_query = (
        (
            jnp.einsum("ihqk,ikhd->iqhd", grad_scores, key_heads, preferred_element_type=f32)
            * HEAD_DIM ** (-0.5)
        )
        .astype(bf16)
        .reshape(items, seq_len, -1)
    )
    grad_key = (
        (
            jnp.einsum("ihqk,iqhd->ikhd", grad_scores, query_heads, preferred_element_type=f32)
            * HEAD_DIM ** (-0.5)
        )
        .astype(bf16)
        .reshape(items, seq_len, -1)
    )
    back_one = (
        jnp.einsum("ise,de->isd", grad_query, p["w_query"], preferred_element_type=f32)
        + jnp.einsum("ise,de->isd", grad_key, p["w_key"], preferred_element_type=f32)
        + jnp.einsum("ise,de->isd", grad_value, p["w_value"], preferred_element_type=f32)
    )
    rows_one = scatter_rows(back_one)
    _, first_back = jax.vjp(layer_norm, rows_in, p["norm1_gain"], p["norm1_shift"])
    grad_in_norm, grad_gain_one, grad_shift_one = first_back(rows_one)
    grad_inputs = (grad_middle + grad_in_norm).astype(bf16)
    g = dict(
        grad_query=grad_query, grad_key=grad_key, grad_value=grad_value,
        grad_gain_one=grad_gain_one, grad_shift_one=grad_shift_one,
    )
    return grad_inputs, g


def body(
    tokens,
    lengths,
    w_query,
    w_key,
    w_value,
    b_query,
    b_value,
    w_out,
    b_out,
    w_up,
    b_up,
    w_down,
    b_down,
    norm1_gain,
    norm1_shift,
    norm2_gain,
    norm2_shift,
    cotangent,
):
    f32 = jnp.float32
    bf16 = jnp.bfloat16
    p = dict(
        w_query=w_query, w_key=w_key, w_value=w_value, b_query=b_query, b_value=b_value,
        w_out=w_out, b_out=b_out, w_up=w_up, b_up=b_up, w_down=w_down, b_down=b_down,
        norm1_gain=norm1_gain, norm1_shift=norm1_shift,
        norm2_gain=norm2_gain, norm2_shift=norm2_shift,
    )
    count = tokens.shape[0]
    results, kept = [], []
    for i in range(count):
        rows_in = tokens[i : i + 1].astype(f32)
        result, k = forward_item(rows_in, lengths[i : i + 1], p)
        results.append(result)
        kept.append((rows_in, k))
    ks = [k for _, k in kept]
    cots = [
        lax.optimization_barrier((ks[i]["full_two"], cotangent[i : i + 1]))[1] for i in range(count)
    ]

    def cat(parts):
        return jnp.concatenate(parts, axis=0)

    def dp_sum(grad, dim):
        return lax.psum_scatter(
            grad.astype(bf16), "dp", scatter_dimension=dim, tiled=True
        ).astype(f32)

    grad_fulls = [gather_rows(cots[i]) for i in range(count)]
    grad_full = cat(grad_fulls)
    grad_w_down = jnp.einsum(
        "isf,isd->fd", cat([k["hidden"] for k in ks]), grad_full, preferred_element_type=f32
    )
    ffn = [backward_ffn(grad_fulls[i], ks[i], p) for i in range(count)]
    back_terms = [f[2] for f in ffn]
    grad_w_down, back_terms[-1] = lax.optimization_barrier((grad_w_down, back_terms[-1]))
    sum_w_down = dp_sum(grad_w_down, 1)
    grad_pre = cat([f[1] for f in ffn])
    grad_w_up = jnp.einsum(
        "isd,isf->df", cat([k["full_two"] for k in ks]), grad_pre, preferred_element_type=f32
    )
    back_rows = [scatter_rows(t) for t in back_terms]
    grad_w_up, back_rows = lax.optimization_barrier((grad_w_up, back_rows))
    sum_w_up = dp_sum(grad_w_up, 0)

    mids = [backward_mid(cots[i], back_rows[i], ks[i], p) for i in range(count)]
    middle_fulls = [m[1] for m in mids]
    attn = [
        backward_attn(kept[i][0], mids[i][0], middle_fulls[i], ks[i], p) for i in range(count)
    ]
    grad_ins = [a[0] for a in attn]
    grads = [dict(mids[i][2], **attn[i][1]) for i in range(count)]
    grad_query = cat([g["grad_query"] for g in grads])
    grad_key = cat([g["grad_key"] for g in grads])
    grad_value = cat([g["grad_value"] for g in grads])
    grad_qkv = jnp.einsum(
        "isd,ise->de",
        cat([k["full_one"] for k in ks]),
        jnp.concatenate([grad_query, grad_key, grad_value], axis=-1),
        preferred_element_type=f32,
    )
    grad_out_t = jnp.einsum(
        "isd,ise->de",
        cat(middle_fulls),
        cat([k["mixed"] for k in ks]),
        preferred_element_type=f32,
    )
    joined = jnp.concatenate([grad_qkv, grad_out_t], axis=1).astype(bf16)
    joined = with_layout_constraint(joined, Layout(major_to_minor=(0, 1)))
    summed = lax.psum_scatter(joined, "dp", scatter_dimension=0, tiled=True)
    width = w_query.shape[1]
    sum_w_query = summed[:, :width].astype(f32)
    sum_w_key = summed[:, width : 2 * width].astype(f32)
    sum_w_value = summed[:, 2 * width : 3 * width].astype(f32)
    sum_w_out = summed[:, 3 * width :].T.astype(f32)

    grad_b_up = jnp.sum(grad_pre, axis=(0, 1), dtype=f32).reshape(b_up.shape)
    grad_b_query = jnp.sum(grad_query, axis=(0, 1), dtype=f32).reshape(b_query.shape)
    grad_b_value = jnp.sum(grad_value, axis=(0, 1), dtype=f32).reshape(b_value.shape)
    biases = halving_scatter(jnp.concatenate([grad_b_up, grad_b_query, grad_b_value]), "dp", 1)
    n_up, n_q = b_up.shape[0], b_query.shape[0]
    sum_b_up = biases[:n_up]
    sum_b_query = biases[n_up : n_up + n_q]
    sum_b_value = biases[n_up + n_q :]

    names = ["grad_b_out", "grad_b_down", "grad_gain_one", "grad_shift_one", "grad_gain_two", "grad_shift_two"]
    vectors = jnp.stack([sum(g[key] for g in grads) for key in names])
    vectors = halving_scatter(halving_scatter(vectors, "dp", 1), "mp", 1)
    sum_b_out, sum_b_down, sum_gain_one, sum_shift_one, sum_gain_two, sum_shift_two = (
        vectors[j] for j in range(len(names))
    )
    return (
        jnp.concatenate(results, axis=0),
        jnp.concatenate(grad_ins, axis=0),
        sum_w_query,
        sum_w_key,
        sum_w_value,
        sum_b_query,
        sum_b_value,
        sum_w_out,
        sum_b_out,
        sum_w_up,
        sum_b_up,
        sum_w_down,
        sum_b_down,
        sum_gain_one,
        sum_shift_one,
        sum_gain_two,
        sum_shift_two,
    )


def solution(mesh):
    return jax.shard_map(
        body,
        mesh=mesh,
        in_specs=(
            P("dp", "mp", None),
            P("dp"),
            P(None, "mp"),
            P(None, "mp"),
            P(None, "mp"),
            P("mp", None),
            P("mp", None),
            P("mp", None),
            P(),
            P(None, "mp"),
            P("mp", None),
            P("mp", None),
            P(),
            P(),
            P(),
            P(),
            P(),
            P("dp", "mp", None),
        ),
        out_specs=(
            P("dp", "mp", None),
            P("dp", "mp", None),
            P("dp", "mp"),
            P("dp", "mp"),
            P("dp", "mp"),
            P("mp", "dp"),
            P("mp", "dp"),
            P("mp", "dp"),
            P(("dp", "mp")),
            P("dp", "mp"),
            P("mp", "dp"),
            P("mp", "dp"),
            P(("dp", "mp")),
            P(("dp", "mp")),
            P(("dp", "mp")),
            P(("dp", "mp")),
            P(("dp", "mp")),
        ),
        check_vma=False,
    )
```

```python
import math
from functools import partial

import jax
import jax.numpy as jnp
from jax import lax
from jax.experimental.layout import Layout, with_layout_constraint
from jax.sharding import PartitionSpec as P

HEAD_DIM = 128


def _pairs(n, flip):
    return [(m, m ^ flip) for m in range(n)]


def gather_rows(x, axis=1):
    n = lax.axis_size("mp")
    if n != 4:
        return lax.all_gather(x, "mp", axis=axis, tiled=True)
    rows = x.shape[axis]
    half = rows // 2
    from_x = lax.ppermute(x, "mp", _pairs(n, 1))
    from_y = lax.ppermute(x, "mp", _pairs(n, 2))
    diag_a = lax.ppermute(lax.slice_in_dim(from_y, 0, half, axis=axis), "mp", _pairs(n, 1))
    diag_b = lax.ppermute(lax.slice_in_dim(from_x, half, rows, axis=axis), "mp", _pairs(n, 2))
    return jnp.concatenate([x, from_x, from_y, diag_a, diag_b], axis=axis)


def gathered_positions(total):
    n = lax.axis_size("mp")
    places = jnp.arange(total)
    if n != 4:
        return places
    rows = total // n
    return ((lax.axis_index("mp") ^ (places // rows)) * rows) + places % rows


def scatter_rows(y, axis=1):
    n = lax.axis_size("mp")
    if n != 4:
        return lax.psum_scatter(
            y.astype(jnp.bfloat16), "mp", scatter_dimension=axis, tiled=True
        ).astype(jnp.float32)
    rows = y.shape[axis] // n
    half = rows // 2

    def part(flip, lo, hi):
        return lax.slice_in_dim(y, flip * rows + lo, flip * rows + hi, axis=axis)

    bf16 = jnp.bfloat16
    send_x = jnp.stack([part(1, 0, half), part(3, 0, half)]).astype(bf16)
    send_y = jnp.stack([part(2, half, rows), part(3, half, rows)]).astype(bf16)
    got_x = lax.ppermute(send_x, "mp", _pairs(n, 1))
    got_y = lax.ppermute(send_y, "mp", _pairs(n, 2))
    fwd_y = (got_x[1].astype(jnp.float32) + part(2, 0, half)).astype(bf16)
    fwd_x = (got_y[1].astype(jnp.float32) + part(1, half, rows)).astype(bf16)
    last_y = lax.ppermute(fwd_y, "mp", _pairs(n, 2))
    last_x = lax.ppermute(fwd_x, "mp", _pairs(n, 1))
    low = part(0, 0, half) + got_x[0].astype(jnp.float32) + last_y.astype(jnp.float32)
    high = part(0, half, rows) + got_y[0].astype(jnp.float32) + last_x.astype(jnp.float32)
    return jnp.concatenate([low, high], axis=axis)


def layer_norm(values, gain, shift):
    centre = values - jnp.mean(values, axis=-1, keepdims=True)
    spread = jnp.mean(centre * centre, axis=-1, keepdims=True)
    return centre * lax.rsqrt(spread + 1e-05) * gain + shift


def allowed_keys(lengths, seq_len):
    places = gathered_positions(seq_len)
    causal = places[None, :] <= places[:, None]
    inside = places[None, None, :] < lengths[:, None, None]
    return (causal[None] & inside)[:, None]


def head_scores(query_heads, key_heads, allowed):
    scores = jnp.einsum(
        "iqhd,ikhd->ihqk", query_heads, key_heads, preferred_element_type=jnp.float32
    ) * HEAD_DIM ** (-0.5)
    return jnp.where(allowed, scores, -1e30)


def halving_scatter(values, name, dim):
    n = lax.axis_size(name)
    if n & (n - 1):
        return lax.psum_scatter(values, name, scatter_dimension=dim, tiled=True)
    me = lax.axis_index(name)
    bit = n // 2
    while bit:
        half = values.shape[dim] // 2
        upper = (me & bit) != 0
        keep = lax.dynamic_slice_in_dim(values, jnp.where(upper, half, 0), half, axis=dim)
        give = lax.dynamic_slice_in_dim(values, jnp.where(upper, 0, half), half, axis=dim)
        values = keep + lax.ppermute(give, name, _pairs(n, bit))
        bit //= 2
    return values


def forward_item(rows_in, length, p):
    f32 = jnp.float32
    bf16 = jnp.bfloat16
    normed_one = layer_norm(rows_in, p["norm1_gain"], p["norm1_shift"]).astype(bf16)
    full_one = gather_rows(normed_one)
    items, seq_len = (full_one.shape[0], full_one.shape[1])
    heads_here = p["w_query"].shape[1] // HEAD_DIM
    split = (items, seq_len, heads_here, HEAD_DIM)

    def project(weight):
        return jnp.einsum("isd,de->ise", full_one, weight, preferred_element_type=f32)

    queries = (project(p["w_query"]) + p["b_query"].reshape(-1)).astype(bf16)
    keys_all = project(p["w_key"]).astype(bf16)
    values_all = (project(p["w_value"]) + p["b_value"].reshape(-1)).astype(bf16)
    query_heads = queries.reshape(split)
    key_heads = keys_all.reshape(split)
    value_heads = values_all.reshape(split)
    allowed = allowed_keys(length, seq_len)
    scores = head_scores(query_heads, key_heads, allowed)
    row_max = jnp.max(scores, axis=-1, keepdims=True)
    raw_weights = jnp.exp(scores - row_max)
    row_total = jnp.sum(raw_weights, axis=-1, keepdims=True)
    probs = (raw_weights / row_total).astype(bf16)
    mixed = (
        jnp.einsum("ihqk,ikhd->iqhd", probs, value_heads, preferred_element_type=f32)
        .reshape(items, seq_len, -1)
        .astype(bf16)
    )
    attn_terms = jnp.einsum("ise,ed->isd", mixed, p["w_out"], preferred_element_type=f32)
    attn_rows = scatter_rows(attn_terms)
    middle = rows_in + attn_rows + p["b_out"]
    normed_two = layer_norm(middle, p["norm2_gain"], p["norm2_shift"]).astype(bf16)
    full_two = gather_rows(normed_two)
    hidden_pre = jnp.einsum(
        "isd,df->isf", full_two, p["w_up"], preferred_element_type=f32
    ) + p["b_up"].reshape(-1)
    normal_cdf = (lax.erf(hidden_pre * (2.0 ** -0.5)) + 1.0) * 0.5
    hidden = (hidden_pre * normal_cdf).astype(bf16)
    ffn_terms = jnp.einsum("isf,fd->isd", hidden, p["w_down"], preferred_element_type=f32)
    ffn_rows = scatter_rows(ffn_terms)
    result = (middle + ffn_rows + p["b_down"]).astype(bf16)
    kept = dict(
        full_one=full_one, query_heads=query_heads, key_heads=key_heads,
        value_heads=value_heads, allowed=allowed, row_max=row_max, row_total=row_total,
        mixed=mixed, middle=middle, full_two=full_two, hidden_pre=hidden_pre, hidden=hidden,
        normal_cdf=normal_cdf,
    )
    return result, kept


def backward_ffn(grad_full, k, p):
    f32 = jnp.float32
    bf16 = jnp.bfloat16
    grad_hidden = jnp.einsum("isd,fd->isf", grad_full, p["w_down"], preferred_element_type=f32)
    u = k["hidden_pre"]
    density = jnp.exp(u * u * -0.5) * (2.0 * math.pi) ** -0.5
    grad_pre = (grad_hidden * (k["normal_cdf"] + u * density)).astype(bf16)
    back_terms = jnp.einsum("isf,df->isd", grad_pre, p["w_up"], preferred_element_type=f32)
    return grad_full, grad_pre, back_terms


def backward_mid(cotangent, back_rows, k, p):
    grad_out = cotangent.astype(jnp.float32)
    _, second_back = jax.vjp(layer_norm, k["middle"], p["norm2_gain"], p["norm2_shift"])
    grad_mid_norm, grad_gain_two, grad_shift_two = second_back(back_rows)
    grad_middle = grad_out + grad_mid_norm
    middle_full = gather_rows(grad_middle.astype(jnp.bfloat16))
    g = dict(
        grad_b_out=jnp.sum(grad_middle, axis=(0, 1)),
        grad_b_down=jnp.sum(grad_out, axis=(0, 1)),
        grad_gain_two=grad_gain_two, grad_shift_two=grad_shift_two,
    )
    return grad_middle, middle_full, g


def backward_attn(rows_in, grad_middle, middle_full, k, p):
    f32 = jnp.float32
    bf16 = jnp.bfloat16
    items, seq_len = k["full_one"].shape[:2]
    heads_here = p["w_query"].shape[1] // HEAD_DIM
    split = (items, seq_len, heads_here, HEAD_DIM)
    grad_mixed = (
        jnp.einsum("isd,ed->ise", middle_full, p["w_out"], preferred_element_type=f32)
        .astype(bf16)
        .reshape(split)
    )
    query_heads, key_heads, value_heads = k["query_heads"], k["key_heads"], k["value_heads"]
    again = head_scores(query_heads, key_heads, k["allowed"])
    probs_full = jnp.exp(again - k["row_max"]) / k["row_total"]
    probs_low = probs_full.astype(bf16)
    grad_value = (
        jnp.einsum("ihqk,iqhd->ikhd", probs_low, grad_mixed, preferred_element_type=f32)
        .astype(bf16)
        .reshape(items, seq_len, -1)
    )
    grad_probs = jnp.einsum("iqhd,ikhd->ihqk", grad_mixed, value_heads, preferred_element_type=f32)
    inner = jnp.sum(probs_full * grad_probs, axis=-1, keepdims=True)
    grad_scores = (probs_full * (grad_probs - inner)).astype(bf16)
    grad_query = (
        (
            jnp.einsum("ihqk,ikhd->iqhd", grad_scores, key_heads, preferred_element_type=f32)
            * HEAD_DIM ** (-0.5)
        )
        .astype(bf16)
        .reshape(items, seq_len, -1)
    )
    grad_key = (
        (
            jnp.einsum("ihqk,iqhd->ikhd", grad_scores, query_heads, preferred_element_type=f32)
            * HEAD_DIM ** (-0.5)
        )
        .astype(bf16)
        .reshape(items, seq_len, -1)
    )
    back_one = (
        jnp.einsum("ise,de->isd", grad_query, p["w_query"], preferred_element_type=f32)
        + jnp.einsum("ise,de->isd", grad_key, p["w_key"], preferred_element_type=f32)
        + jnp.einsum("ise,de->isd", grad_value, p["w_value"], preferred_element_type=f32)
    )
    rows_one = scatter_rows(back_one)
    _, first_back = jax.vjp(layer_norm, rows_in, p["norm1_gain"], p["norm1_shift"])
    grad_in_norm, grad_gain_one, grad_shift_one = first_back(rows_one)
    grad_inputs = (grad_middle + grad_in_norm).astype(bf16)
    g = dict(
        grad_query=grad_query, grad_key=grad_key, grad_value=grad_value,
        grad_gain_one=grad_gain_one, grad_shift_one=grad_shift_one,
    )
    return grad_inputs, g


def body(
    tokens,
    lengths,
    w_query,
    w_key,
    w_value,
    b_query,
    b_value,
    w_out,
    b_out,
    w_up,
    b_up,
    w_down,
    b_down,
    norm1_gain,
    norm1_shift,
    norm2_gain,
    norm2_shift,
    cotangent,
):
    f32 = jnp.float32
    bf16 = jnp.bfloat16
    p = dict(
        w_query=w_query, w_key=w_key, w_value=w_value, b_query=b_query, b_value=b_value,
        w_out=w_out, b_out=b_out, w_up=w_up, b_up=b_up, w_down=w_down, b_down=b_down,
        norm1_gain=norm1_gain, norm1_shift=norm1_shift,
        norm2_gain=norm2_gain, norm2_shift=norm2_shift,
    )
    count = tokens.shape[0]
    results, kept = [], []
    for i in range(count):
        rows_in = tokens[i : i + 1].astype(f32)
        result, k = forward_item(rows_in, lengths[i : i + 1], p)
        results.append(result)
        kept.append((rows_in, k))
    ks = [k for _, k in kept]
    cots = [
        lax.optimization_barrier((ks[i]["full_two"], cotangent[i : i + 1]))[1] for i in range(count)
    ]

    def cat(parts):
        return jnp.concatenate(parts, axis=0)

    def dp_sum(grad, dim):
        return lax.psum_scatter(
            grad.astype(bf16), "dp", scatter_dimension=dim, tiled=True
        ).astype(f32)

    grad_fulls = [gather_rows(cots[i]) for i in range(count)]
    grad_full = cat(grad_fulls)
    grad_w_down = jnp.einsum(
        "isf,isd->fd", cat([k["hidden"] for k in ks]), grad_full, preferred_element_type=f32
    )
    ffn = [backward_ffn(grad_fulls[i], ks[i], p) for i in range(count)]
    back_terms = [f[2] for f in ffn]
    grad_w_down, back_terms[-1] = lax.optimization_barrier((grad_w_down, back_terms[-1]))
    sum_w_down = dp_sum(grad_w_down, 1)
    grad_pre = cat([f[1] for f in ffn])
    grad_w_up = jnp.einsum(
        "isd,isf->df", cat([k["full_two"] for k in ks]), grad_pre, preferred_element_type=f32
    )
    back_rows = [scatter_rows(t) for t in back_terms]
    grad_w_up, back_rows[0] = lax.optimization_barrier((grad_w_up, back_rows[0]))
    sum_w_up = dp_sum(grad_w_up, 0)

    mids = [backward_mid(cots[i], back_rows[i], ks[i], p) for i in range(count)]
    middle_fulls = [m[1] for m in mids]
    attn = [
        backward_attn(kept[i][0], mids[i][0], middle_fulls[i], ks[i], p) for i in range(count)
    ]
    grad_ins = [a[0] for a in attn]
    grads = [dict(mids[i][2], **attn[i][1]) for i in range(count)]
    grad_query = cat([g["grad_query"] for g in grads])
    grad_key = cat([g["grad_key"] for g in grads])
    grad_value = cat([g["grad_value"] for g in grads])
    grad_qkv = jnp.einsum(
        "isd,ise->de",
        cat([k["full_one"] for k in ks]),
        jnp.concatenate([grad_query, grad_key, grad_value], axis=-1),
        preferred_element_type=f32,
    )
    grad_out_t = jnp.einsum(
        "isd,ise->de",
        cat(middle_fulls),
        cat([k["mixed"] for k in ks]),
        preferred_element_type=f32,
    )
    joined = jnp.concatenate([grad_qkv, grad_out_t], axis=1).astype(bf16)
    joined = with_layout_constraint(joined, Layout(major_to_minor=(0, 1)))
    summed = lax.psum_scatter(joined, "dp", scatter_dimension=0, tiled=True).astype(f32)
    width = w_query.shape[1]
    sum_w_query = summed[:, :width]
    sum_w_key = summed[:, width : 2 * width]
    sum_w_value = summed[:, 2 * width : 3 * width]
    sum_w_out = summed[:, 3 * width :].T

    grad_b_up = jnp.sum(grad_pre, axis=(0, 1), dtype=f32).reshape(b_up.shape)
    grad_b_query = jnp.sum(grad_query, axis=(0, 1), dtype=f32).reshape(b_query.shape)
    grad_b_value = jnp.sum(grad_value, axis=(0, 1), dtype=f32).reshape(b_value.shape)
    biases = halving_scatter(jnp.concatenate([grad_b_up, grad_b_query, grad_b_value]), "dp", 1)
    n_up, n_q = b_up.shape[0], b_query.shape[0]
    sum_b_up = biases[:n_up]
    sum_b_query = biases[n_up : n_up + n_q]
    sum_b_value = biases[n_up + n_q :]

    names = ["grad_b_out", "grad_b_down", "grad_gain_one", "grad_shift_one", "grad_gain_two", "grad_shift_two"]
    vectors = jnp.stack([sum(g[key] for g in grads) for key in names])
    vectors = halving_scatter(halving_scatter(vectors, "dp", 1), "mp", 1)
    sum_b_out, sum_b_down, sum_gain_one, sum_shift_one, sum_gain_two, sum_shift_two = (
        vectors[j] for j in range(len(names))
    )
    return (
        jnp.concatenate(results, axis=0),
        jnp.concatenate(grad_ins, axis=0),
        sum_w_query,
        sum_w_key,
        sum_w_value,
        sum_b_query,
        sum_b_value,
        sum_w_out,
        sum_b_out,
        sum_w_up,
        sum_b_up,
        sum_w_down,
        sum_b_down,
        sum_gain_one,
        sum_shift_one,
        sum_gain_two,
        sum_shift_two,
    )


def solution(mesh):
    return jax.shard_map(
        body,
        mesh=mesh,
        in_specs=(
            P("dp", "mp", None),
            P("dp"),
            P(None, "mp"),
            P(None, "mp"),
            P(None, "mp"),
            P("mp", None),
            P("mp", None),
            P("mp", None),
            P(),
            P(None, "mp"),
            P("mp", None),
            P("mp", None),
            P(),
            P(),
            P(),
            P(),
            P(),
            P("dp", "mp", None),
        ),
        out_specs=(
            P("dp", "mp", None),
            P("dp", "mp", None),
            P("dp", "mp"),
            P("dp", "mp"),
            P("dp", "mp"),
            P("mp", "dp"),
            P("mp", "dp"),
            P("mp", "dp"),
            P(("dp", "mp")),
            P("dp", "mp"),
            P("mp", "dp"),
            P("mp", "dp"),
            P(("dp", "mp")),
            P(("dp", "mp")),
            P(("dp", "mp")),
            P(("dp", "mp")),
            P(("dp", "mp")),
        ),
        check_vma=False,
    )
```

```python
import math
from functools import partial

import jax
import jax.numpy as jnp
from jax import lax
from jax.experimental.layout import Layout, with_layout_constraint
from jax.sharding import PartitionSpec as P

HEAD_DIM = 128


def _pairs(n, flip):
    return [(m, m ^ flip) for m in range(n)]


def gather_rows(x, axis=1):
    n = lax.axis_size("mp")
    if n != 4:
        return lax.all_gather(x, "mp", axis=axis, tiled=True)
    rows = x.shape[axis]
    half = rows // 2
    from_x = lax.ppermute(x, "mp", _pairs(n, 1))
    from_y = lax.ppermute(x, "mp", _pairs(n, 2))
    diag_a = lax.ppermute(lax.slice_in_dim(from_y, 0, half, axis=axis), "mp", _pairs(n, 1))
    diag_b = lax.ppermute(lax.slice_in_dim(from_x, half, rows, axis=axis), "mp", _pairs(n, 2))
    return jnp.concatenate([x, from_x, from_y, diag_a, diag_b], axis=axis)


def gathered_positions(total):
    n = lax.axis_size("mp")
    places = jnp.arange(total)
    if n != 4:
        return places
    rows = total // n
    return ((lax.axis_index("mp") ^ (places // rows)) * rows) + places % rows


def scatter_rows(y, axis=1):
    n = lax.axis_size("mp")
    if n != 4:
        return lax.psum_scatter(
            y.astype(jnp.bfloat16), "mp", scatter_dimension=axis, tiled=True
        ).astype(jnp.float32)
    rows = y.shape[axis] // n
    half = rows // 2

    def part(flip, lo, hi):
        return lax.slice_in_dim(y, flip * rows + lo, flip * rows + hi, axis=axis)

    bf16 = jnp.bfloat16
    send_x = jnp.stack([part(1, 0, half), part(3, 0, half)]).astype(bf16)
    send_y = jnp.stack([part(2, half, rows), part(3, half, rows)]).astype(bf16)
    got_x = lax.ppermute(send_x, "mp", _pairs(n, 1))
    got_y = lax.ppermute(send_y, "mp", _pairs(n, 2))
    fwd_y = (got_x[1].astype(jnp.float32) + part(2, 0, half)).astype(bf16)
    fwd_x = (got_y[1].astype(jnp.float32) + part(1, half, rows)).astype(bf16)
    last_y = lax.ppermute(fwd_y, "mp", _pairs(n, 2))
    last_x = lax.ppermute(fwd_x, "mp", _pairs(n, 1))
    low = part(0, 0, half) + got_x[0].astype(jnp.float32) + last_y.astype(jnp.float32)
    high = part(0, half, rows) + got_y[0].astype(jnp.float32) + last_x.astype(jnp.float32)
    return jnp.concatenate([low, high], axis=axis)


def layer_norm(values, gain, shift):
    centre = values - jnp.mean(values, axis=-1, keepdims=True)
    spread = jnp.mean(centre * centre, axis=-1, keepdims=True)
    return centre * lax.rsqrt(spread + 1e-05) * gain + shift


def allowed_keys(lengths, seq_len):
    places = gathered_positions(seq_len)
    causal = places[None, :] <= places[:, None]
    inside = places[None, None, :] < lengths[:, None, None]
    return (causal[None] & inside)[:, None]


def head_scores(query_heads, key_heads, allowed):
    scores = jnp.einsum(
        "iqhd,ikhd->ihqk", query_heads, key_heads, preferred_element_type=jnp.float32
    ) * HEAD_DIM ** (-0.5)
    return jnp.where(allowed, scores, -1e30)


def halving_scatter(values, name, dim):
    n = lax.axis_size(name)
    if n & (n - 1):
        return lax.psum_scatter(values, name, scatter_dimension=dim, tiled=True)
    me = lax.axis_index(name)
    bit = n // 2
    while bit:
        half = values.shape[dim] // 2
        upper = (me & bit) != 0
        keep = lax.dynamic_slice_in_dim(values, jnp.where(upper, half, 0), half, axis=dim)
        give = lax.dynamic_slice_in_dim(values, jnp.where(upper, 0, half), half, axis=dim)
        values = keep + lax.ppermute(give, name, _pairs(n, bit))
        bit //= 2
    return values


def forward_item(rows_in, length, p):
    f32 = jnp.float32
    bf16 = jnp.bfloat16
    normed_one = layer_norm(rows_in, p["norm1_gain"], p["norm1_shift"]).astype(bf16)
    full_one = gather_rows(normed_one)
    items, seq_len = (full_one.shape[0], full_one.shape[1])
    heads_here = p["w_query"].shape[1] // HEAD_DIM
    split = (items, seq_len, heads_here, HEAD_DIM)

    def project(weight):
        return jnp.einsum("isd,de->ise", full_one, weight, preferred_element_type=f32)

    queries = (project(p["w_query"]) + p["b_query"].reshape(-1)).astype(bf16)
    keys_all = project(p["w_key"]).astype(bf16)
    values_all = (project(p["w_value"]) + p["b_value"].reshape(-1)).astype(bf16)
    query_heads = queries.reshape(split)
    key_heads = keys_all.reshape(split)
    value_heads = values_all.reshape(split)
    allowed = allowed_keys(length, seq_len)
    scores = head_scores(query_heads, key_heads, allowed)
    row_max = jnp.max(scores, axis=-1, keepdims=True)
    raw_weights = jnp.exp(scores - row_max)
    row_total = jnp.sum(raw_weights, axis=-1, keepdims=True)
    probs = (raw_weights / row_total).astype(bf16)
    mixed = (
        jnp.einsum("ihqk,ikhd->iqhd", probs, value_heads, preferred_element_type=f32)
        .reshape(items, seq_len, -1)
        .astype(bf16)
    )
    attn_terms = jnp.einsum("ise,ed->isd", mixed, p["w_out"], preferred_element_type=f32)
    attn_rows = scatter_rows(attn_terms)
    middle = rows_in + attn_rows + p["b_out"]
    normed_two = layer_norm(middle, p["norm2_gain"], p["norm2_shift"]).astype(bf16)
    full_two = gather_rows(normed_two)
    hidden_pre = jnp.einsum(
        "isd,df->isf", full_two, p["w_up"], preferred_element_type=f32
    ) + p["b_up"].reshape(-1)
    normal_cdf = (lax.erf(hidden_pre * (2.0 ** -0.5)) + 1.0) * 0.5
    hidden = (hidden_pre * normal_cdf).astype(bf16)
    ffn_terms = jnp.einsum("isf,fd->isd", hidden, p["w_down"], preferred_element_type=f32)
    ffn_rows = scatter_rows(ffn_terms)
    result = (middle + ffn_rows + p["b_down"]).astype(bf16)
    kept = dict(
        full_one=full_one, query_heads=query_heads, key_heads=key_heads,
        value_heads=value_heads, allowed=allowed, row_max=row_max, row_total=row_total,
        mixed=mixed, middle=middle, full_two=full_two, hidden_pre=hidden_pre, hidden=hidden,
        normal_cdf=normal_cdf,
    )
    return result, kept


def backward_ffn(grad_full, k, p):
    f32 = jnp.float32
    bf16 = jnp.bfloat16
    grad_hidden = jnp.einsum("isd,fd->isf", grad_full, p["w_down"], preferred_element_type=f32)
    u = k["hidden_pre"]
    density = jnp.exp(u * u * -0.5) * (2.0 * math.pi) ** -0.5
    grad_pre = (grad_hidden * (k["normal_cdf"] + u * density)).astype(bf16)
    back_terms = jnp.einsum("isf,df->isd", grad_pre, p["w_up"], preferred_element_type=f32)
    return grad_full, grad_pre, back_terms


def backward_mid(cotangent, back_rows, k, p):
    grad_out = cotangent.astype(jnp.float32)
    _, second_back = jax.vjp(layer_norm, k["middle"], p["norm2_gain"], p["norm2_shift"])
    grad_mid_norm, grad_gain_two, grad_shift_two = second_back(back_rows)
    grad_middle = grad_out + grad_mid_norm
    middle_full = gather_rows(grad_middle.astype(jnp.bfloat16))
    g = dict(
        grad_b_out=jnp.sum(grad_middle, axis=(0, 1)),
        grad_b_down=jnp.sum(grad_out, axis=(0, 1)),
        grad_gain_two=grad_gain_two, grad_shift_two=grad_shift_two,
    )
    return grad_middle, middle_full, g


def backward_attn(rows_in, grad_middle, middle_full, k, p):
    f32 = jnp.float32
    bf16 = jnp.bfloat16
    items, seq_len = k["full_one"].shape[:2]
    heads_here = p["w_query"].shape[1] // HEAD_DIM
    split = (items, seq_len, heads_here, HEAD_DIM)
    grad_mixed = (
        jnp.einsum("isd,ed->ise", middle_full, p["w_out"], preferred_element_type=f32)
        .astype(bf16)
        .reshape(split)
    )
    query_heads, key_heads, value_heads = k["query_heads"], k["key_heads"], k["value_heads"]
    again = head_scores(query_heads, key_heads, k["allowed"])
    probs_full = jnp.exp(again - k["row_max"]) / k["row_total"]
    probs_low = probs_full.astype(bf16)
    grad_value = (
        jnp.einsum("ihqk,iqhd->ikhd", probs_low, grad_mixed, preferred_element_type=f32)
        .astype(bf16)
        .reshape(items, seq_len, -1)
    )
    grad_probs = jnp.einsum("iqhd,ikhd->ihqk", grad_mixed, value_heads, preferred_element_type=f32)
    inner = jnp.sum(probs_full * grad_probs, axis=-1, keepdims=True)
    grad_scores = (probs_full * (grad_probs - inner)).astype(bf16)
    grad_query = (
        (
            jnp.einsum("ihqk,ikhd->iqhd", grad_scores, key_heads, preferred_element_type=f32)
            * HEAD_DIM ** (-0.5)
        )
        .astype(bf16)
        .reshape(items, seq_len, -1)
    )
    grad_key = (
        (
            jnp.einsum("ihqk,iqhd->ikhd", grad_scores, query_heads, preferred_element_type=f32)
            * HEAD_DIM ** (-0.5)
        )
        .astype(bf16)
        .reshape(items, seq_len, -1)
    )
    back_one = (
        jnp.einsum("ise,de->isd", grad_query, p["w_query"], preferred_element_type=f32)
        + jnp.einsum("ise,de->isd", grad_key, p["w_key"], preferred_element_type=f32)
        + jnp.einsum("ise,de->isd", grad_value, p["w_value"], preferred_element_type=f32)
    )
    rows_one = scatter_rows(back_one)
    _, first_back = jax.vjp(layer_norm, rows_in, p["norm1_gain"], p["norm1_shift"])
    grad_in_norm, grad_gain_one, grad_shift_one = first_back(rows_one)
    grad_inputs = (grad_middle + grad_in_norm).astype(bf16)
    g = dict(
        grad_query=grad_query, grad_key=grad_key, grad_value=grad_value,
        grad_gain_one=grad_gain_one, grad_shift_one=grad_shift_one,
    )
    return grad_inputs, g


def body(
    tokens,
    lengths,
    w_query,
    w_key,
    w_value,
    b_query,
    b_value,
    w_out,
    b_out,
    w_up,
    b_up,
    w_down,
    b_down,
    norm1_gain,
    norm1_shift,
    norm2_gain,
    norm2_shift,
    cotangent,
):
    f32 = jnp.float32
    bf16 = jnp.bfloat16
    p = dict(
        w_query=w_query, w_key=w_key, w_value=w_value, b_query=b_query, b_value=b_value,
        w_out=w_out, b_out=b_out, w_up=w_up, b_up=b_up, w_down=w_down, b_down=b_down,
        norm1_gain=norm1_gain, norm1_shift=norm1_shift,
        norm2_gain=norm2_gain, norm2_shift=norm2_shift,
    )
    count = tokens.shape[0]
    results, kept = [], []
    for i in range(count):
        rows_in = tokens[i : i + 1].astype(f32)
        result, k = forward_item(rows_in, lengths[i : i + 1], p)
        results.append(result)
        kept.append((rows_in, k))
    ks = [k for _, k in kept]
    cots = [
        lax.optimization_barrier((ks[i]["full_two"], cotangent[i : i + 1]))[1] for i in range(count)
    ]

    def cat(parts):
        return jnp.concatenate(parts, axis=0)

    def dp_sum(grad, dim):
        return lax.psum_scatter(
            grad.astype(bf16), "dp", scatter_dimension=dim, tiled=True
        ).astype(f32)

    grad_fulls = [gather_rows(cots[i]) for i in range(count)]
    grad_full = cat(grad_fulls)
    grad_w_down = jnp.einsum(
        "isf,isd->fd", cat([k["hidden"] for k in ks]), grad_full, preferred_element_type=f32
    )
    ffn = [backward_ffn(grad_fulls[i], ks[i], p) for i in range(count)]
    back_terms = [f[2] for f in ffn]
    grad_w_down, back_terms[0] = lax.optimization_barrier((grad_w_down, back_terms[0]))
    sum_w_down = dp_sum(grad_w_down, 1)
    grad_pre = cat([f[1] for f in ffn])
    grad_w_up = jnp.einsum(
        "isd,isf->df", cat([k["full_two"] for k in ks]), grad_pre, preferred_element_type=f32
    )
    back_rows = [scatter_rows(t) for t in back_terms]
    grad_w_up, back_rows = lax.optimization_barrier((grad_w_up, back_rows))
    sum_w_up = dp_sum(grad_w_up, 0)

    mids = [backward_mid(cots[i], back_rows[i], ks[i], p) for i in range(count)]
    middle_fulls = [m[1] for m in mids]
    attn = [
        backward_attn(kept[i][0], mids[i][0], middle_fulls[i], ks[i], p) for i in range(count)
    ]
    grad_ins = [a[0] for a in attn]
    grads = [dict(mids[i][2], **attn[i][1]) for i in range(count)]
    grad_query = cat([g["grad_query"] for g in grads])
    grad_key = cat([g["grad_key"] for g in grads])
    grad_value = cat([g["grad_value"] for g in grads])
    grad_qkv = jnp.einsum(
        "isd,ise->de",
        cat([k["full_one"] for k in ks]),
        jnp.concatenate([grad_query, grad_key, grad_value], axis=-1),
        preferred_element_type=f32,
    )
    grad_out_t = jnp.einsum(
        "isd,ise->de",
        cat(middle_fulls),
        cat([k["mixed"] for k in ks]),
        preferred_element_type=f32,
    )
    joined = jnp.concatenate([grad_qkv, grad_out_t], axis=1).astype(bf16)
    joined = with_layout_constraint(joined, Layout(major_to_minor=(0, 1)))
    summed = lax.psum_scatter(joined, "dp", scatter_dimension=0, tiled=True).astype(f32)
    width = w_query.shape[1]
    sum_w_query = summed[:, :width]
    sum_w_key = summed[:, width : 2 * width]
    sum_w_value = summed[:, 2 * width : 3 * width]
    sum_w_out = summed[:, 3 * width :].T

    grad_b_up = jnp.sum(grad_pre, axis=(0, 1), dtype=f32).reshape(b_up.shape)
    grad_b_query = jnp.sum(grad_query, axis=(0, 1), dtype=f32).reshape(b_query.shape)
    grad_b_value = jnp.sum(grad_value, axis=(0, 1), dtype=f32).reshape(b_value.shape)
    biases = halving_scatter(jnp.concatenate([grad_b_up, grad_b_query, grad_b_value]), "dp", 1)
    n_up, n_q = b_up.shape[0], b_query.shape[0]
    sum_b_up = biases[:n_up]
    sum_b_query = biases[n_up : n_up + n_q]
    sum_b_value = biases[n_up + n_q :]

    names = ["grad_b_out", "grad_b_down", "grad_gain_one", "grad_shift_one", "grad_gain_two", "grad_shift_two"]
    vectors = jnp.stack([sum(g[key] for g in grads) for key in names])
    vectors = halving_scatter(halving_scatter(vectors, "dp", 1), "mp", 1)
    sum_b_out, sum_b_down, sum_gain_one, sum_shift_one, sum_gain_two, sum_shift_two = (
        vectors[j] for j in range(len(names))
    )
    return (
        jnp.concatenate(results, axis=0),
        jnp.concatenate(grad_ins, axis=0),
        sum_w_query,
        sum_w_key,
        sum_w_value,
        sum_b_query,
        sum_b_value,
        sum_w_out,
        sum_b_out,
        sum_w_up,
        sum_b_up,
        sum_w_down,
        sum_b_down,
        sum_gain_one,
        sum_shift_one,
        sum_gain_two,
        sum_shift_two,
    )


def solution(mesh):
    return jax.shard_map(
        body,
        mesh=mesh,
        in_specs=(
            P("dp", "mp", None),
            P("dp"),
            P(None, "mp"),
            P(None, "mp"),
            P(None, "mp"),
            P("mp", None),
            P("mp", None),
            P("mp", None),
            P(),
            P(None, "mp"),
            P("mp", None),
            P("mp", None),
            P(),
            P(),
            P(),
            P(),
            P(),
            P("dp", "mp", None),
        ),
        out_specs=(
            P("dp", "mp", None),
            P("dp", "mp", None),
            P("dp", "mp"),
            P("dp", "mp"),
            P("dp", "mp"),
            P("mp", "dp"),
            P("mp", "dp"),
            P("mp", "dp"),
            P(("dp", "mp")),
            P("dp", "mp"),
            P("mp", "dp"),
            P("mp", "dp"),
            P(("dp", "mp")),
            P(("dp", "mp")),
            P(("dp", "mp")),
            P(("dp", "mp")),
            P(("dp", "mp")),
        ),
        check_vma=False,
    )
```
